512 devices in a mesh: wide: 64 (over y, x, core), narrow: 8 (over z).
Axes of the slice: x: 4, y: 8, z: 8, core: 2. Of those that a mesh axis runs over, the one named last changes fastest.
Arguments:
- point_owner: int32 [524288, 1], P(('wide', 'narrow')), may hold values from 0 to 63; in each aligned block of 1024 rows (0 to 1023, 1024 to 2047, ...) at most 32 rows name the same one
- point_cell: int32 [524288], P(('wide', 'narrow')), may hold values from 0 to 8191
- normals: float32 [3, 524288], P(None, ('wide', 'narrow')), may hold values from -6 to 6
- strip_count: int32 [512], P(('wide', 'narrow')), may hold values from 1 to 1024, 458752 in all
- neighbours: int32 [64, 8, 2, 27], P('wide', 'narrow'), may hold values from 0 to 18, as said below
Outputs:
- solution: float32 [64, 8, 2, 4096], P('wide', 'narrow')
- residual: float32 [64, 8, 2, 4096], P('wide', 'narrow')
The draws below stay inside these ranges and needn't reach their ends.
Inputs may be any that keep to these rules, and one draw needn't show every extreme that they name: `point_owner`: the points of one device name each wide index at most 32 times, and some wide index exactly 32 times. `strip_count`: some device has exactly 1024 live points. `neighbours`: entries follow the encoding of the steps; dw and dn are -1, 0 or 1; the relation is mutual (b sees c in a direction exactly when c sees b in the opposite one); entry 13 names the brick itself.
All inputs are finite; a program needn't handle non-finite values.
Results may differ from the reference program's by a relative error of at most 0.0003.
Values sent between devices are 32-bit elements; how exact they have to be, the bound alone decides.
No kernel may reach another device: no remote copies, remote signals or barrier semaphores. Data moves between devices by JAX's collectives and lax.ppermute only.
A program may use at most 64 MiB of HBM per device.

```python
import math
import jax
import jax.numpy as jnp
import numpy as np
from jax import lax

P_DEV = 1024
BR_DEV = 2
ITERS = 3
CAP = 32
POINTS = 524288
N_WIDE = 64
N_NARROW = 8


def draw_neighbours(key, part):
    device_count = N_WIDE * N_NARROW
    device = jnp.arange(device_count, dtype=jnp.int32)
    places = jax.vmap(lambda d: jax.random.permutation(jax.random.fold_in(key, d), 8))(device)[:, :BR_DEV].astype(jnp.int32)
    wide_at = (device // N_NARROW)[:, None]
    narrow_at = (device % N_NARROW)[:, None]
    coord_x = 2 * wide_at + places // 4
    coord_y = places // 2 % 2
    coord_z = 2 * narrow_at + places % 2
    slots = jnp.broadcast_to(jnp.arange(BR_DEV, dtype=jnp.int32)[None, :], places.shape)
    occupancy = jnp.full((2 * N_WIDE, 2, 2 * N_NARROW), -1, jnp.int32).at[coord_x, coord_y, coord_z].set(slots)
    steps_table = np.array([[a, b, c] for a in (-1, 0, 1) for b in (-1, 0, 1) for c in (-1, 0, 1)], np.int32)
    near_x = coord_x[:, :, None] + jnp.asarray(steps_table[:, 0])
    near_y = coord_y[:, :, None] + jnp.asarray(steps_table[:, 1])
    near_z = coord_z[:, :, None] + jnp.asarray(steps_table[:, 2])
    inside = (near_x >= 0) & (near_x < 2 * N_WIDE) & (near_y >= 0) & (near_y < 2) & (near_z >= 0) & (near_z < 2 * N_NARROW)
    found = occupancy[jnp.clip(near_x, 0, 2 * N_WIDE - 1), jnp.clip(near_y, 0, 1), jnp.clip(near_z, 0, 2 * N_NARROW - 1)]
    shift_w = jnp.clip(near_x, 0, 2 * N_WIDE - 1) // 2 - wide_at[:, :, None]
    shift_n = jnp.clip(near_z, 0, 2 * N_NARROW - 1) // 2 - narrow_at[:, :, None]
    encoded = ((shift_w + 1) * 3 + shift_n + 1) * BR_DEV + found
    encoded = jnp.where(inside & (found >= 0), encoded, 9 * BR_DEV)
    return encoded.reshape(N_WIDE, N_NARROW, BR_DEV, 27).astype(jnp.int32)


def touch_ends(drawn, key, low, largest):
    shape = drawn.shape
    index_at = [jax.random.randint(jax.random.fold_in(key, axis), (), 0, shape[axis]) for axis in range(len(shape))]
    drawn = drawn.at[tuple(index_at)].set(low)
    longest = shape.index(max(shape))
    index_at[longest] = (index_at[longest] + 1) % shape[longest]
    return drawn.at[tuple(index_at)].set(largest)


def levels(own_key, extent, pieces, smallest, top_value):
    def one(dim, blocks):
        steps = jax.random.uniform(jax.random.fold_in(jax.random.fold_in(own_key, 6), dim), (blocks,), jnp.float32, smallest / len(pieces), top_value / len(pieces))
        return jnp.repeat(jnp.exp(steps), extent[dim] // blocks).reshape((-1,) + (1,) * (len(extent) - dim - 1))

    gain = one(*pieces[0])
    for cut in pieces[1:]:
        gain = gain * one(*cut)
    return gain


def profile(amount, total, limit, lean):
    portions = [(1 << 20) // math.isqrt(grade ** lean) + 1 for grade in range(2, amount + 1)]
    rest, given = total - limit - (amount - 1), [1] * (amount - 1)
    while rest > 0:
        movable = [i for i in range(amount - 1) if given[i] < limit]
        mass, remaining = sum([portions[i] for i in movable]), rest
        for i in movable:
            extra = min(limit - given[i], max(1, remaining * portions[i] // mass), rest)
            given[i] = given[i] + extra
            rest = rest - extra
    return np.array([limit] + given)


def uneven(rng, number_of, total, most, slope):
    if number_of == 2:
        one = jax.random.randint(rng, (), max(1, total - most), min(most, total - 1) + 1)
        return jnp.stack([one, total - one])
    sizes = jnp.asarray(profile(number_of, total, most, slope), jnp.int32)
    twos = (number_of - 1) // 2
    source_of, receiver = sizes[1:1 + 2 * twos:2], sizes[2:2 + 2 * twos:2]
    margin = jnp.minimum(source_of - 1, most - receiver)
    moved = jax.random.randint(jax.random.fold_in(rng, 1), (twos,), 0, 1 << 20) % (margin + 1)
    sizes = sizes.at[1:1 + 2 * twos:2].set(source_of - moved).at[2:2 + 2 * twos:2].set(receiver + moved)
    return sizes[jax.random.permutation(jax.random.fold_in(rng, 2), number_of)]


def routed_block(key, own, number, rows, amount, top, most, lean):
    order = jax.random.permutation(key, amount)
    crowded, common = load_shares(amount, rows * top, most, lean, True), load_shares(amount, rows * top, most, lean, False)
    places = jnp.arange(amount)

    def named(sizes, turn):
        used = int((sizes > 0).sum())
        fixed = max(1, used // 4)
        shifted = fixed + (places - fixed + turn * (used - fixed)) % max(1, amount - fixed)
        return jnp.zeros((amount,), jnp.int32).at[order[jnp.where(places < fixed, places, shifted)]].set(jnp.asarray(sizes, jnp.int32))

    sizes = jnp.where(number % 4 == 0, named(crowded, number // 4), named(common, number - number // 4 - 1))
    mixed = jax.random.permutation(jax.random.fold_in(own, 3), amount)
    donor, sink = mixed[0:amount // 2 * 2:2], mixed[1:amount // 2 * 2:2]
    room = jnp.minimum(sizes[donor] - 1, most - sizes[sink]) // 2
    room = jnp.where((donor == order[0]) | (sink == order[0]) | (sizes[sink] == 0), 0, jnp.maximum(room, 0))
    shifted = jax.random.randint(jax.random.fold_in(own, 4), (amount // 2,), 0, 1 << 20) % (room + 1)
    sizes = sizes.at[donor].add(-shifted).at[sink].add(shifted)
    members = jnp.searchsorted(jnp.cumsum(sizes), jnp.arange(rows * top), side="right").astype(jnp.int32)
    grid = members.reshape(top, rows).T
    grid = grid[jax.random.permutation(jax.random.fold_in(own, 1), rows)]
    turn = jax.random.randint(jax.random.fold_in(own, 2), (rows, 1), 0, top)
    return jnp.take_along_axis(grid, (jnp.arange(top)[None, :] + turn) % top, axis=1)


def load_shares(number_of, total, most, lean, full):
    portions = [(1 << 20) // math.isqrt(standing ** lean) + 1 for standing in range(1, number_of + 1)]
    largest = most if full else min(most, max(-(-total // number_of), total * portions[0] // sum(portions)))
    least = 1 if total - largest >= number_of - 1 else 0
    counts, surplus = [largest] + [least] * (number_of - 1), total - largest - least * (number_of - 1)
    while surplus > 0:
        movable = [i for i in range(1, number_of) if counts[i] < largest] or [i for i in range(1, number_of) if counts[i] < most]
        pool, budget = sum([portions[i] for i in movable]), surplus
        for i in movable:
            addition = min(most - counts[i], max(1, budget * portions[i] // pool), surplus)
            counts[i] = counts[i] + addition
            surplus = surplus - addition
    return np.array(counts)


def noise(own_key, extent, scale, bound, cuts=(), kind=jnp.bfloat16):
    result = jax.random.normal(own_key, extent, jnp.float32) * scale
    if len(cuts) > 0:
        result = levels(own_key, extent, cuts, -0.22, 0.18) * result
    return jnp.clip(result, min=-bound, max=bound).astype(kind)


def setup_inputs(seed: int = 0) -> dict:
    streams_of = jax.random.split(jax.random.key(seed), 6)
    point_owner_keys = jax.random.split(jax.random.fold_in(streams_of[0], 1), POINTS // P_DEV)
    point_owner_turns = jax.random.permutation(jax.random.fold_in(streams_of[0], 3), POINTS // P_DEV)
    point_owner = jax.vmap(lambda own, number: routed_block(jax.random.fold_in(streams_of[0], 2), own, number, P_DEV, N_WIDE, 1, CAP, 2))(point_owner_keys, point_owner_turns).reshape((POINTS, 1))
    point_cell = touch_ends(jax.random.randint(streams_of[1], (POINTS,), 0, BR_DEV * 4096), jax.random.fold_in(streams_of[1], 1), 0, (BR_DEV * 4096) - 1).astype(jnp.int32)
    normals = noise(streams_of[2], (3, POINTS), 1.0, 6.0, ((1, 512),), jnp.float32)
    strip_count = uneven(streams_of[3], N_WIDE * N_NARROW, N_WIDE * N_NARROW * P_DEV * 7 // 8, P_DEV, 2).astype(jnp.int32)
    neighbours = draw_neighbours(jax.random.fold_in(streams_of[5], 71), 0)
    return {"point_owner": point_owner, "point_cell": point_cell, "normals": normals, "strip_count": strip_count, "neighbours": neighbours}


WEIGHTS = (0.0, 1.0, 0.5, 0.25)
DIRECTIONS = tuple((a, b, c) for a in (-1, 0, 1) for b in (-1, 0, 1) for c in (-1, 0, 1))


def cell_span(shift_by):
    if shift_by == -1:
        return 15, 16
    if shift_by == 1:
        return 0, 1
    return 0, 16


def fetch_piece(source, brick_table, step_x, step_y, step_z):
    column = (step_x + 1) * 9 + (step_y + 1) * 3 + (step_z + 1)
    low_x, high_x = cell_span(step_x)
    low_y, high_y = cell_span(step_y)
    low_z, high_z = cell_span(step_z)
    piece = source[:, low_x:high_x, low_y:high_y, low_z:high_z]
    return jnp.take(piece, brick_table[:, column], axis=0)


def make_source(rim_data):
    flat_rows = rim_data.reshape(-1, 4096)
    flat_rows = jnp.concatenate([flat_rows, jnp.zeros((1, 4096), flat_rows.dtype)], 0)
    return flat_rows.reshape(-1, 16, 16, 16)


def stencil(source, brick_table, values, diagonal):
    brick_count = values.shape[0]
    own_cube = values.reshape(brick_count, 16, 16, 16)
    planes = []
    for step_x in (-1, 0, 1):
        row_parts = []
        for step_y in (-1, 0, 1):
            col_parts = []
            for step_z in (-1, 0, 1):
                if step_x == 0 and step_y == 0 and step_z == 0:
                    col_parts.append(own_cube)
                else:
                    col_parts.append(fetch_piece(source, brick_table, step_x, step_y, step_z))
            row_parts.append(jnp.concatenate(col_parts, 3))
        planes.append(jnp.concatenate(row_parts, 2))
    padded = jnp.concatenate(planes, 1)
    summed = jnp.zeros_like(own_cube)
    for step_x, step_y, step_z in DIRECTIONS:
        reach = abs(step_x) + abs(step_y) + abs(step_z)
        if reach > 0:
            summed = summed + WEIGHTS[reach] * padded[:, 1 + step_x:17 + step_x, 1 + step_y:17 + step_y, 1 + step_z:17 + step_z]
    return diagonal * values - summed.reshape(brick_count, 4096)


def divergence(sources, brick_table, vector_field):
    brick_count = vector_field.shape[1]
    summed = jnp.zeros((brick_count, 16, 16, 16), vector_field.dtype)
    for direction in range(3):
        upper_step = [0, 0, 0]
        upper_step[direction] = 1
        lower_step = [0, 0, 0]
        lower_step[direction] = -1
        lower_piece = fetch_piece(sources[direction], brick_table, *lower_step)
        upper_piece = fetch_piece(sources[direction], brick_table, *upper_step)
        own_cube = vector_field[direction].reshape(brick_count, 16, 16, 16)
        extended = jnp.concatenate([lower_piece, own_cube, upper_piece], direction + 1)
        change = lax.slice_in_dim(extended, 2, 18, axis=direction + 1) - lax.slice_in_dim(extended, 0, 16, axis=direction + 1)
        summed = summed + change
    return -4.0 * summed.reshape(brick_count, 4096)


def reference(point_owner, point_cell, normals, strip_count, neighbours):
    device_count = N_WIDE * N_NARROW
    brick_cells = BR_DEV * 4096
    point_index = jnp.arange(POINTS, dtype=jnp.int32)
    device_of = point_index // P_DEV
    is_live = (point_index % P_DEV) < jnp.take(strip_count, device_of)
    owner_device = point_owner[:, 0] * N_NARROW + device_of % N_NARROW
    flat_cell = owner_device * brick_cells + point_cell
    weight_live = is_live.astype(jnp.float32)
    segments = device_count * brick_cells
    vector_field = jnp.stack([jax.ops.segment_sum(normals[c] * weight_live, flat_cell, num_segments=segments) for c in range(3)])
    vector_field = vector_field.reshape(3, N_WIDE, N_NARROW, BR_DEV, 4096)
    density = jax.ops.segment_sum(weight_live, flat_cell, num_segments=segments).reshape(N_WIDE, N_NARROW, BR_DEV, 4096)
    diagonal = 14.5 + 2.0 * density
    devices = jnp.arange(device_count, dtype=jnp.int32)

    padded_vectors = jnp.pad(vector_field, ((0, 0), (1, 1), (1, 1), (0, 0), (0, 0)))

    def source_at(device):
        wide_at = (device // N_NARROW).astype(jnp.int32)
        narrow_at = (device % N_NARROW).astype(jnp.int32)
        zero = jnp.zeros((), jnp.int32)
        sources = [make_source(lax.dynamic_slice(padded_vectors[c], (wide_at, narrow_at, zero, zero), (3, 3, BR_DEV, 4096))) for c in range(3)]
        return divergence(sources, neighbours[wide_at, narrow_at], vector_field[:, wide_at, narrow_at])

    right_side = lax.map(source_at, devices).reshape(N_WIDE, N_NARROW, BR_DEV, 4096)

    def apply_operator(values):
        padded = jnp.pad(values, ((1, 1), (1, 1), (0, 0), (0, 0)))

        def apply_at(device):
            wide_at = (device // N_NARROW).astype(jnp.int32)
            narrow_at = (device % N_NARROW).astype(jnp.int32)
            zero = jnp.zeros((), jnp.int32)
            source = make_source(lax.dynamic_slice(padded, (wide_at, narrow_at, zero, zero), (3, 3, BR_DEV, 4096)))
            return stencil(source, neighbours[wide_at, narrow_at], values[wide_at, narrow_at], diagonal[wide_at, narrow_at])

        return lax.map(apply_at, devices).reshape(N_WIDE, N_NARROW, BR_DEV, 4096)

    solution = jnp.zeros_like(right_side)
    residual = right_side
    direction = right_side
    norm_now = jnp.sum(residual * residual)
    for iteration in range(ITERS):
        image_field = apply_operator(direction)
        step_size = norm_now / jnp.sum(direction * image_field)
        solution = solution + step_size * direction
        residual = residual - step_size * image_field
        norm_next = jnp.sum(residual * residual)
        direction = residual + (norm_next / norm_now) * direction
        norm_now = norm_next
    return solution, residual
```

```python
import math

import jax
import jax.numpy as jnp
from jax import lax
from jax.sharding import PartitionSpec as P

ITERS = 3


WEIGHTS = (0.0, 1.0, 0.5, 0.25)
DIRECTIONS = tuple(((a, b, c) for a in (-1, 0, 1) for b in (-1, 0, 1) for c in (-1, 0, 1)))
HIGHEST = lax.Precision.HIGHEST


def padded_2(array, sides, width):
    for axis, dim in sides:
        peers, length = (lax.axis_size(axis), array.shape[dim])
        up = [(i, (i + 1) % peers) for i in range(peers - 1)]
        down = [(j, i) for i, j in up]
        last = lax.slice_in_dim(array, length - width, length, axis=dim)
        leading = lax.slice_in_dim(array, 0, width, axis=dim)
        before = lax.ppermute(last, axis, up)
        after = lax.ppermute(leading, axis, down)
        array = jnp.concatenate([before, array, after], axis=dim)
    return array


def cell_span(shift_by):
    if shift_by == -1:
        return (15, 16)
    if shift_by == 1:
        return (0, 1)
    return (0, 16)


def fetch_piece(source, layout, brick_table, step_x, step_y, step_z):
    column = (step_x + 1) * 9 + (step_y + 1) * 3 + (step_z + 1)
    low_x, high_x = cell_span(step_x)
    low_y, high_y = cell_span(step_y)
    low_z, high_z = cell_span(step_z)
    piece = source[:, low_x:high_x, low_y:high_y, low_z:high_z]
    return jnp.take(piece, brick_table[:, column], axis=0)


def make_source(rim_data):
    row_width = rim_data.shape[-1]
    flat_rows = rim_data.reshape(-1, row_width)
    flat_rows = jnp.concatenate([flat_rows, jnp.zeros((1, row_width), flat_rows.dtype)], 0)
    return flat_rows.reshape(-1, 16, 16, 16)


def stencil(source, layout, brick_table, values, diagonal):
    brick_count = values.shape[0]
    own_cube = values.reshape(brick_count, 16, 16, 16)
    planes = []
    for step_x in (-1, 0, 1):
        row_parts = []
        for step_y in (-1, 0, 1):
            col_parts = []
            for step_z in (-1, 0, 1):
                if step_x == 0 and step_y == 0 and (step_z == 0):
                    col_parts.append(own_cube)
                else:
                    col_parts.append(
                        fetch_piece(source, layout, brick_table, step_x, step_y, step_z)
                    )
            row_parts.append(jnp.concatenate(col_parts, 3))
        planes.append(jnp.concatenate(row_parts, 2))
    padded = jnp.concatenate(planes, 1)
    summed = jnp.zeros_like(own_cube)
    for step_x, step_y, step_z in DIRECTIONS:
        reach = abs(step_x) + abs(step_y) + abs(step_z)
        if reach > 0:
            summed = (
                summed
                + WEIGHTS[reach]
                * padded[
                    :, 1 + step_x : 17 + step_x, 1 + step_y : 17 + step_y, 1 + step_z : 17 + step_z
                ]
            )
    return diagonal * values - summed.reshape(brick_count, 4096)


def divergence(sources, layout, brick_table, vector_field):
    brick_count = vector_field.shape[1]
    summed = jnp.zeros((brick_count, 16, 16, 16), vector_field.dtype)
    for direction in range(3):
        upper_step = [0, 0, 0]
        upper_step[direction] = 1
        lower_step = [0, 0, 0]
        lower_step[direction] = -1
        lower_piece = fetch_piece(sources[direction], layout, brick_table, *lower_step)
        upper_piece = fetch_piece(sources[direction], layout, brick_table, *upper_step)
        own_cube = vector_field[direction].reshape(brick_count, 16, 16, 16)
        extended = jnp.concatenate([lower_piece, own_cube, upper_piece], direction + 1)
        change = lax.slice_in_dim(extended, 2, 18, axis=direction + 1) - lax.slice_in_dim(
            extended, 0, 16, axis=direction + 1
        )
        summed = summed + change
    return -4.0 * summed.reshape(brick_count, 4096)


def shards(point_owner, point_cell, normals, strip_count, neighbours):
    owners = lax.axis_size("wide")
    devices = owners * lax.axis_size("narrow")
    point_total = point_cell.shape[0]
    brick_table = neighbours[0, 0]
    brick_count = brick_table.shape[0]
    brick_cells = brick_count * 4096
    capacity = 2 * point_total // owners
    target_owner = point_owner[:, 0]
    is_live = jnp.arange(point_total, dtype=jnp.int32) < strip_count[0]
    target = jnp.where(is_live, point_cell, brick_cells)
    sort_order = jnp.argsort(target_owner, stable=True)
    sorted_owner = target_owner[sort_order]
    owner_ids = jnp.arange(owners, dtype=jnp.int32)
    per_owner = jnp.sum((target_owner[:, None] == owner_ids[None, :]).astype(jnp.int32), axis=0)
    first_slot = jnp.cumsum(per_owner) - per_owner
    sorted_marks = (sorted_owner[:, None] == owner_ids[None, :]).astype(jnp.int32)
    slot_rank = jnp.arange(point_total, dtype=jnp.int32) - jnp.sum(
        sorted_marks * first_slot[None, :], axis=1
    )
    send_index = (
        jnp.full((owners, capacity), brick_cells, jnp.int32)
        .at[sorted_owner, slot_rank]
        .set(target[sort_order])
    )
    send_vectors = (
        jnp.zeros((owners, 3, capacity), jnp.float32)
        .at[sorted_owner, :, slot_rank]
        .set(normals[:, sort_order].T)
    )
    got_index, got_vectors = (
        lax.all_to_all(send_index, "wide", split_axis=0, concat_axis=0, tiled=True),
        lax.all_to_all(send_vectors, "wide", split_axis=0, concat_axis=0, tiled=True),
    )
    slot_total = owners * capacity
    block_rows = math.gcd(slot_total, 2048)
    flat_index = got_index.reshape(slot_total // block_rows, block_rows)
    flat_vectors = got_vectors.transpose(0, 2, 1).reshape(slot_total // block_rows, block_rows, 3)
    columns_high = jnp.arange(brick_count * 64, dtype=jnp.int32)
    columns_low = jnp.arange(64, dtype=jnp.int32)

    def splat_step(summed, pieces):
        indices, vectors = pieces
        brick_hot = (indices[:, None] // 64 == columns_high[None, :]).astype(jnp.float32)
        cell_hot = (indices[:, None] % 64 == columns_low[None, :]).astype(jnp.float32)
        weighted = jnp.concatenate(
            [
                cell_hot * vectors[:, 0:1],
                cell_hot * vectors[:, 1:2],
                cell_hot * vectors[:, 2:3],
                cell_hot,
            ],
            1,
        )
        return (
            summed
            + jnp.einsum(
                "pa,pb->ab",
                brick_hot,
                weighted,
                precision=HIGHEST,
                preferred_element_type=jnp.float32,
            ),
            None,
        )

    splatted, leftover = lax.scan(
        splat_step, jnp.zeros((brick_count * 64, 256), jnp.float32), (flat_index, flat_vectors)
    )
    vector_field = jnp.stack(
        [splatted[:, c * 64 : (c + 1) * 64].reshape(brick_count, 4096) for c in range(3)]
    )
    density = splatted[:, 192:256].reshape(brick_count, 4096)
    diagonal = 14.5 + 2.0 * density
    vector_rim = padded_2(vector_field[None, None], (("wide", 0), ("narrow", 1)), 1)
    layout = "whole"
    sources = [make_source(vector_rim[:, :, c]) for c in range(3)]
    right_side = divergence(sources, layout, brick_table, vector_field)

    def global_sum(parts):
        stacked = jnp.stack(parts)[None, :]
        spread = jnp.broadcast_to(stacked, (devices, stacked.shape[1]))
        gathered = lax.all_to_all(spread, ("wide", "narrow"), 0, 0, tiled=True)
        return jnp.sum(gathered, axis=0)

    def global_squares(values):
        return global_sum([jnp.sum(values * values)])[0]

    solution = jnp.zeros_like(right_side)
    residual = right_side
    direction = right_side
    norm_now = global_squares(residual)
    for iteration in range(ITERS):
        field_rim = padded_2(direction[None, None], (("wide", 0), ("narrow", 1)), 1)
        image_field = stencil(make_source(field_rim), layout, brick_table, direction, diagonal)
        step_size = norm_now / global_sum([jnp.sum(direction * image_field)])[0]
        solution = solution + step_size * direction
        residual = residual - step_size * image_field
        norm_next = global_squares(residual)
        direction = residual + norm_next / norm_now * direction
        norm_now = norm_next
    return (solution.reshape(1, 1, brick_count, 4096), residual.reshape(1, 1, brick_count, 4096))


def solution(mesh):
    return jax.shard_map(
        shards,
        mesh=mesh,
        in_specs=(
            P(("wide", "narrow"), None),
            P(("wide", "narrow")),
            P(None, ("wide", "narrow")),
            P(("wide", "narrow")),
            P("wide", "narrow", None, None),
        ),
        out_specs=(P("wide", "narrow", None, None), P("wide", "narrow", None, None)),
        check_vma=False,
    )
```

```python
import math

import jax
import jax.numpy as jnp
from jax import lax
from jax.experimental import pallas as pl
from jax.experimental.pallas import tpu as pltpu
from jax.sharding import PartitionSpec as P

ITERS = 3
CAP = 32
HIGHEST = lax.Precision.HIGHEST
ROWS, LANES = 16, 256


def _masks():
    shape = (ROWS, LANES)
    lane = lax.broadcasted_iota(jnp.int32, shape, 1)
    row = lax.broadcasted_iota(jnp.int32, shape, 0)
    return row, lane >> 4, lane & 15


def _neighbour_x(c, m, p, row):
    lo = jnp.where(row == 0, pltpu.roll(m, 1, 0), pltpu.roll(c, 1, 0))
    hi = jnp.where(row == ROWS - 1, pltpu.roll(p, ROWS - 1, 0), pltpu.roll(c, ROWS - 1, 0))
    return lo, hi


def _neighbour_y(c, m, p, y):
    lo = jnp.where(y == 0, pltpu.roll(m, 16, 1), pltpu.roll(c, 16, 1))
    hi = jnp.where(y == 15, pltpu.roll(p, LANES - 16, 1), pltpu.roll(c, LANES - 16, 1))
    return lo, hi


def _neighbour_z(c, m, p, z):
    lo = jnp.where(z == 0, pltpu.roll(m, LANES - 15, 1), pltpu.roll(c, 1, 1))
    hi = jnp.where(z == 15, pltpu.roll(p, 15, 1), pltpu.roll(c, LANES - 1, 1))
    return lo, hi


def _column(ex, ey, ez):
    return (ex + 1) * 9 + (ey + 1) * 3 + (ez + 1)


def _stencil_kernel(tab_ref, src_ref, diag_ref, out_ref):
    row, y, z = _masks()
    bricks = out_ref.shape[0]
    for b in range(bricks):
        own = src_ref[4 * bricks + b]

        def brick(ex, ey, ez):
            if ex == 0 and ey == 0 and ez == 0:
                return own
            return src_ref[tab_ref[b * 27 + _column(ex, ey, ez)]]

        planes = {}
        for ex in (-1, 0, 1):
            lines = {}
            for ey in (-1, 0, 1):
                c = brick(ex, ey, 0)
                lo, hi = _neighbour_z(c, brick(ex, ey, -1), brick(ex, ey, 1), z)
                lines[ey] = c + 0.5 * (lo + hi)
            lo, hi = _neighbour_y(lines[0], lines[-1], lines[1], y)
            planes[ex] = lines[0] + 0.5 * (lo + hi)
        lo, hi = _neighbour_x(planes[0], planes[-1], planes[1], row)
        smoothed = planes[0] + 0.5 * (lo + hi)
        out_ref[b] = (diag_ref[b] + 2.0) * own - 2.0 * smoothed


def _divergence_kernel(tab_ref, src_ref, out_ref):
    row, y, z = _masks()
    bricks = out_ref.shape[0]
    for b in range(bricks):

        def brick(k, ex, ey, ez):
            if ex == 0 and ey == 0 and ez == 0:
                return src_ref[k, 4 * bricks + b]
            return src_ref[k, tab_ref[b * 27 + _column(ex, ey, ez)]]

        lo, hi = _neighbour_x(brick(0, 0, 0, 0), brick(0, -1, 0, 0), brick(0, 1, 0, 0), row)
        change_x = hi - lo
        lo, hi = _neighbour_y(brick(1, 0, 0, 0), brick(1, 0, -1, 0), brick(1, 0, 1, 0), y)
        change_y = hi - lo
        lo, hi = _neighbour_z(brick(2, 0, 0, 0), brick(2, 0, 0, -1), brick(2, 0, 0, 1), z)
        change_z = hi - lo
        out_ref[b] = -4.0 * ((change_x + change_y) + change_z)


def _local_call(kernel, out_shape, operands, flops):
    spaces = [pltpu.SMEM] + [pltpu.VMEM] * (len(operands) - 1)
    moved = sum(int(a.size) * 4 for a in operands) + math.prod(out_shape) * 4
    return pl.pallas_call(
        kernel,
        out_shape=jax.ShapeDtypeStruct(out_shape, jnp.float32),
        in_specs=[pl.BlockSpec(memory_space=s) for s in spaces],
        out_specs=pl.BlockSpec(memory_space=pltpu.VMEM),
        cost_estimate=pl.CostEstimate(flops=flops, bytes_accessed=moved, transcendentals=0),
    )(*operands)


def halo(field):
    n_wide, n_narrow = lax.axis_size("wide"), lax.axis_size("narrow")
    pieces = []
    for dw in (-1, 0, 1):
        for dn in (-1, 0, 1):
            if dw == 0 and dn == 0:
                pieces.append(field)
                continue
            pairs = [
                ((w + dw) * n_narrow + n + dn, w * n_narrow + n)
                for w in range(n_wide)
                for n in range(n_narrow)
                if 0 <= w + dw < n_wide and 0 <= n + dn < n_narrow
            ]
            pieces.append(lax.ppermute(field, ("wide", "narrow"), pairs))
    zero_shape = field.shape[:-3] + (1,) + field.shape[-2:]
    pieces.append(jnp.zeros(zero_shape, field.dtype))
    return jnp.concatenate(pieces, axis=-3)


def shards(point_owner, point_cell, normals, strip_count, neighbours):
    owners = lax.axis_size("wide")
    devices = owners * lax.axis_size("narrow")
    point_total = point_cell.shape[0]
    bricks = neighbours.shape[2]
    table = neighbours.reshape(bricks * 27)

    owner = point_owner[:, 0]
    slots = jnp.arange(point_total, dtype=jnp.int32)
    is_live = slots < strip_count[0]
    code = jnp.where(is_live, point_cell + 1, 0).astype(jnp.float32)
    owner_hot = (owner[:, None] == jnp.arange(owners, dtype=jnp.int32)[None, :]).astype(jnp.bfloat16)
    earlier = (slots[None, :] < slots[:, None]).astype(jnp.bfloat16)
    before = jnp.dot(earlier, owner_hot, preferred_element_type=jnp.float32)
    rank = jnp.sum(before * owner_hot.astype(jnp.float32), axis=1).astype(jnp.int32)
    dest = owner * CAP + rank
    payload = jnp.concatenate([code[:, None], normals.T], axis=1)
    place_hot = (jnp.arange(owners * CAP, dtype=jnp.int32)[:, None] == dest[None, :]).astype(jnp.float32)
    send = jnp.dot(place_hot, payload, precision=HIGHEST, preferred_element_type=jnp.float32)
    got = lax.all_to_all(send.reshape(owners, CAP, 4), "wide", 0, 0, tiled=True).reshape(owners * CAP, 4)

    cell = got[:, 0].astype(jnp.int32) - 1
    brick_x = cell >> 8
    cell_yz = cell & (LANES - 1)
    bx_hot = (brick_x[:, None] == jnp.arange(bricks * ROWS, dtype=jnp.int32)[None, :]).astype(jnp.float32)
    yz_hot = (cell_yz[:, None] == jnp.arange(LANES, dtype=jnp.int32)[None, :]).astype(jnp.float32)
    weighted = jnp.concatenate([bx_hot * got[:, 1:2], bx_hot * got[:, 2:3], bx_hot * got[:, 3:4], bx_hot], axis=1)
    splatted = jnp.einsum("pa,pb->ab", weighted, yz_hot, precision=HIGHEST, preferred_element_type=jnp.float32)
    splatted = splatted.reshape(4, bricks, ROWS, LANES)
    vector_field = splatted[:3]
    diagonal = 14.5 + 2.0 * splatted[3]

    shape = (bricks, ROWS, LANES)
    right_side = _local_call(_divergence_kernel, shape, [table, halo(vector_field)], 20 * bricks * 4096)

    def global_sum(parts):
        stacked = jnp.stack(parts)[None, :]
        spread = jnp.broadcast_to(stacked, (devices, stacked.shape[1]))
        gathered = lax.all_to_all(spread, ("wide", "narrow"), 0, 0, tiled=True)
        return jnp.sum(gathered, axis=0)

    residual = right_side
    solution = jnp.zeros_like(right_side)
    for iteration in range(ITERS):
        image_r = _local_call(_stencil_kernel, shape, [table, halo(residual), diagonal], 60 * bricks * 4096)
        sums = global_sum([jnp.sum(residual * residual), jnp.sum(residual * image_r)])
        norm_now, curvature = sums[0], sums[1]
        if iteration == 0:
            step_size = norm_now / curvature
            direction, image_field = residual, image_r
        else:
            ratio = norm_now / norm_before
            step_size = norm_now / (curvature - ratio * norm_now / step_before)
            direction = residual + ratio * direction
            image_field = image_r + ratio * image_field
        solution = solution + step_size * direction
        residual = residual - step_size * image_field
        norm_before, step_before = norm_now, step_size
    out = (1, 1, bricks, ROWS * LANES)
    return solution.reshape(out), residual.reshape(out)


def solution(mesh):
    return jax.shard_map(
        shards,
        mesh=mesh,
        in_specs=(
            P(("wide", "narrow"), None),
            P(("wide", "narrow")),
            P(None, ("wide", "narrow")),
            P(("wide", "narrow")),
            P("wide", "narrow", None, None),
        ),
        out_specs=(P("wide", "narrow", None, None), P("wide", "narrow", None, None)),
        check_vma=False,
    )
```

```python
import functools
import math

import jax
import jax.numpy as jnp
from jax import lax
from jax.experimental import pallas as pl
from jax.experimental.pallas import tpu as pltpu
from jax.sharding import PartitionSpec as P

ITERS = 3
CAP = 32
HIGHEST = lax.Precision.HIGHEST
ROWS, LANES = 16, 256
SHIFT, SPAN = 8.5, 8.0


def _solve(matrix, rhs):
    n = len(rhs)
    m = [list(r) + [v] for r, v in zip(matrix, rhs)]
    for k in range(n):
        for i in range(k + 1, n):
            f = m[i][k] / m[k][k]
            m[i] = [m[i][j] - f * m[k][j] if j > k else m[i][j] for j in range(n + 1)]
    x = [None] * n
    for i in reversed(range(n)):
        acc = m[i][n]
        for j in range(i + 1, n):
            acc = acc - m[i][j] * x[j]
        x[i] = acc / m[i][i]
    return x


def _masks():
    shape = (ROWS, LANES)
    lane = lax.broadcasted_iota(jnp.int32, shape, 1)
    row = lax.broadcasted_iota(jnp.int32, shape, 0)
    return row, lane >> 4, lane & 15


def _neighbour_x(c, m, p, row):
    lo = jnp.where(row == 0, pltpu.roll(m, 1, 0), pltpu.roll(c, 1, 0))
    hi = jnp.where(row == ROWS - 1, pltpu.roll(p, ROWS - 1, 0), pltpu.roll(c, ROWS - 1, 0))
    return lo, hi


def _neighbour_y(c, m, p, y):
    lo = jnp.where(y == 0, pltpu.roll(m, 16, 1), pltpu.roll(c, 16, 1))
    hi = jnp.where(y == 15, pltpu.roll(p, LANES - 16, 1), pltpu.roll(c, LANES - 16, 1))
    return lo, hi


def _neighbour_z(c, m, p, z):
    lo = jnp.where(z == 0, pltpu.roll(m, LANES - 15, 1), pltpu.roll(c, 1, 1))
    hi = jnp.where(z == 15, pltpu.roll(p, 15, 1), pltpu.roll(c, LANES - 1, 1))
    return lo, hi


def _column(ex, ey, ez):
    return (ex + 1) * 9 + (ey + 1) * 3 + (ez + 1)


def _stencil_kernel(tab_ref, src_ref, diag_ref, out_ref, shift=0.0, scale=1.0):
    row, y, z = _masks()
    bricks = out_ref.shape[0]
    for b in range(bricks):
        own = src_ref[4 * bricks + b]

        def brick(ex, ey, ez):
            if ex == 0 and ey == 0 and ez == 0:
                return own
            return src_ref[tab_ref[b * 27 + _column(ex, ey, ez)]]

        planes = {}
        for ex in (-1, 0, 1):
            lines = {}
            for ey in (-1, 0, 1):
                c = brick(ex, ey, 0)
                lo, hi = _neighbour_z(c, brick(ex, ey, -1), brick(ex, ey, 1), z)
                lines[ey] = c + 0.5 * (lo + hi)
            lo, hi = _neighbour_y(lines[0], lines[-1], lines[1], y)
            planes[ex] = lines[0] + 0.5 * (lo + hi)
        lo, hi = _neighbour_x(planes[0], planes[-1], planes[1], row)
        smoothed = planes[0] + 0.5 * (lo + hi)
        out_ref[b] = ((diag_ref[b] + (2.0 - shift)) * own - 2.0 * smoothed) * scale


def _divergence_kernel(tab_ref, src_ref, out_ref):
    row, y, z = _masks()
    bricks = out_ref.shape[0]
    for b in range(bricks):

        def brick(k, ex, ey, ez):
            if ex == 0 and ey == 0 and ez == 0:
                return src_ref[k, 4 * bricks + b]
            return src_ref[k, tab_ref[b * 27 + _column(ex, ey, ez)]]

        lo, hi = _neighbour_x(brick(0, 0, 0, 0), brick(0, -1, 0, 0), brick(0, 1, 0, 0), row)
        change_x = hi - lo
        lo, hi = _neighbour_y(brick(1, 0, 0, 0), brick(1, 0, -1, 0), brick(1, 0, 1, 0), y)
        change_y = hi - lo
        lo, hi = _neighbour_z(brick(2, 0, 0, 0), brick(2, 0, 0, -1), brick(2, 0, 0, 1), z)
        change_z = hi - lo
        out_ref[b] = -4.0 * ((change_x + change_y) + change_z)


def _local_call(kernel, out_shape, operands, flops):
    spaces = [pltpu.SMEM] + [pltpu.VMEM] * (len(operands) - 1)
    moved = sum(int(a.size) * 4 for a in operands) + math.prod(out_shape) * 4
    return pl.pallas_call(
        kernel,
        out_shape=jax.ShapeDtypeStruct(out_shape, jnp.float32),
        in_specs=[pl.BlockSpec(memory_space=s) for s in spaces],
        out_specs=pl.BlockSpec(memory_space=pltpu.VMEM),
        cost_estimate=pl.CostEstimate(flops=flops, bytes_accessed=moved, transcendentals=0),
    )(*operands)


def _shift(field, axis, step):
    size = lax.axis_size(axis)
    pairs = [(i + step, i) for i in range(size) if 0 <= i + step < size]
    return lax.ppermute(field, axis, pairs)


def halo(field):
    lead, bricks = field.shape[:-3], field.shape[-3]
    column = jnp.stack([_shift(field, "wide", -1), field, _shift(field, "wide", 1)], axis=-4)
    block = jnp.stack([_shift(column, "narrow", -1), column, _shift(column, "narrow", 1)], axis=-4)
    block = block.reshape(lead + (9 * bricks,) + field.shape[-2:])
    zero = jnp.zeros(lead + (1,) + field.shape[-2:], field.dtype)
    return jnp.concatenate([block, zero], axis=-3)


def shards(point_owner, point_cell, normals, strip_count, neighbours):
    owners = lax.axis_size("wide")
    devices = owners * lax.axis_size("narrow")
    point_total = point_cell.shape[0]
    bricks = neighbours.shape[2]
    table = neighbours.reshape(bricks * 27)

    owner = point_owner[:, 0]
    slots = jnp.arange(point_total, dtype=jnp.int32)
    is_live = slots < strip_count[0]
    code = jnp.where(is_live, point_cell + 1, 0).astype(jnp.float32)
    owner_hot = (owner[:, None] == jnp.arange(owners, dtype=jnp.int32)[None, :]).astype(jnp.bfloat16)
    earlier = (slots[None, :] < slots[:, None]).astype(jnp.bfloat16)
    before = jnp.dot(earlier, owner_hot, preferred_element_type=jnp.float32)
    rank = jnp.sum(before * owner_hot.astype(jnp.float32), axis=1).astype(jnp.int32)
    dest = owner * CAP + rank
    payload = jnp.concatenate([code[:, None], normals.T], axis=1)
    place_hot = (jnp.arange(owners * CAP, dtype=jnp.int32)[:, None] == dest[None, :]).astype(jnp.float32)
    send = jnp.dot(place_hot, payload, precision=HIGHEST, preferred_element_type=jnp.float32)
    got = lax.all_to_all(send.reshape(owners, CAP, 4), "wide", 0, 0, tiled=True).reshape(owners * CAP, 4)

    cell = got[:, 0].astype(jnp.int32) - 1
    brick_x = cell >> 8
    cell_yz = cell & (LANES - 1)
    bx_hot = (brick_x[:, None] == jnp.arange(bricks * ROWS, dtype=jnp.int32)[None, :]).astype(jnp.float32)
    yz_hot = (cell_yz[:, None] == jnp.arange(LANES, dtype=jnp.int32)[None, :]).astype(jnp.float32)
    weighted = jnp.concatenate([bx_hot * got[:, 1:2], bx_hot * got[:, 2:3], bx_hot * got[:, 3:4], bx_hot], axis=1)
    splatted = jnp.einsum("pa,pb->ab", weighted, yz_hot, precision=HIGHEST, preferred_element_type=jnp.float32)
    splatted = splatted.reshape(4, bricks, ROWS, LANES)
    vector_field = splatted[:3]
    diagonal = 14.5 + 2.0 * splatted[3]

    shape = (bricks, ROWS, LANES)
    right_side = _local_call(_divergence_kernel, shape, [table, halo(vector_field)], 20 * bricks * 4096)

    def global_sum(parts):
        stacked = jnp.stack(parts)[None, :]
        spread = jnp.broadcast_to(stacked, (devices, stacked.shape[1]))
        gathered = lax.all_to_all(spread, ("wide", "narrow"), 0, 0, tiled=True)
        return jnp.sum(gathered, axis=0)

    basis = [right_side]
    kernel = functools.partial(_stencil_kernel, shift=SHIFT, scale=1.0 / SPAN)
    for k in range(ITERS):
        image = _local_call(kernel, shape, [table, halo(basis[-1]), diagonal], 60 * bricks * 4096)
        basis.append(image if k == 0 else 2.0 * image - basis[-2])
    lift = [[0.0] * ITERS for _ in range(ITERS + 1)]
    for k in range(ITERS):
        lift[k][k] = SHIFT
        if k == 0:
            lift[1][0] = SPAN
        else:
            lift[k - 1][k] = lift[k + 1][k] = 0.5 * SPAN
    pairs = [(i, j) for i in range(ITERS + 1) for j in range(i, ITERS + 1)]
    sums = global_sum([jnp.sum(basis[i] * basis[j]) for i, j in pairs])
    gram = [[None] * (ITERS + 1) for _ in range(ITERS + 1)]
    for k, (i, j) in enumerate(pairs):
        gram[i][j] = gram[j][i] = sums[k]

    def lifted(i, j):
        terms = [lift[k][j] * gram[i][k] for k in range(ITERS + 1) if lift[k][j] != 0.0]
        return sum(terms[1:], terms[0])

    coeff = _solve([[lifted(i, j) for j in range(ITERS)] for i in range(ITERS)], [gram[i][0] for i in range(ITERS)])
    solution = coeff[0] * basis[0]
    for j in range(1, ITERS):
        solution = solution + coeff[j] * basis[j]
    weights = []
    for k in range(ITERS + 1):
        terms = [lift[k][j] * coeff[j] for j in range(ITERS) if lift[k][j] != 0.0]
        weights.append((1.0 if k == 0 else 0.0) - sum(terms[1:], terms[0]))
    residual = weights[0] * basis[0]
    for k in range(1, ITERS + 1):
        residual = residual + weights[k] * basis[k]
    out = (1, 1, bricks, ROWS * LANES)
    return solution.reshape(out), residual.reshape(out)


def solution(mesh):
    return jax.shard_map(
        shards,
        mesh=mesh,
        in_specs=(
            P(("wide", "narrow"), None),
            P(("wide", "narrow")),
            P(None, ("wide", "narrow")),
            P(("wide", "narrow")),
            P("wide", "narrow", None, None),
        ),
        out_specs=(P("wide", "narrow", None, None), P("wide", "narrow", None, None)),
        check_vma=False,
    )
```

```python
import math

import jax
import jax.numpy as jnp
from jax import lax
from jax.experimental import pallas as pl
from jax.experimental.pallas import tpu as pltpu
from jax.sharding import PartitionSpec as P

ITERS = 3
CAP = 32
HIGHEST = lax.Precision.HIGHEST
ROWS, LANES = 16, 256


def _masks():
    shape = (ROWS, LANES)
    lane = lax.broadcasted_iota(jnp.int32, shape, 1)
    row = lax.broadcasted_iota(jnp.int32, shape, 0)
    return row, lane >> 4, lane & 15


def _neighbour_x(c, m, p, row):
    lo = jnp.where(row == 0, pltpu.roll(m, 1, 0), pltpu.roll(c, 1, 0))
    hi = jnp.where(row == ROWS - 1, pltpu.roll(p, ROWS - 1, 0), pltpu.roll(c, ROWS - 1, 0))
    return lo, hi


def _neighbour_y(c, m, p, y):
    lo = jnp.where(y == 0, pltpu.roll(m, 16, 1), pltpu.roll(c, 16, 1))
    hi = jnp.where(y == 15, pltpu.roll(p, LANES - 16, 1), pltpu.roll(c, LANES - 16, 1))
    return lo, hi


def _neighbour_z(c, m, p, z):
    lo = jnp.where(z == 0, pltpu.roll(m, LANES - 15, 1), pltpu.roll(c, 1, 1))
    hi = jnp.where(z == 15, pltpu.roll(p, 15, 1), pltpu.roll(c, LANES - 1, 1))
    return lo, hi


def _column(ex, ey, ez):
    return (ex + 1) * 9 + (ey + 1) * 3 + (ez + 1)


def _stencil_kernel(tab_ref, src_ref, diag_ref, out_ref):
    row, y, z = _masks()
    bricks = out_ref.shape[0]
    for b in range(bricks):
        own = src_ref[4 * bricks + b]

        def brick(ex, ey, ez):
            if ex == 0 and ey == 0 and ez == 0:
                return own
            return src_ref[tab_ref[b * 27 + _column(ex, ey, ez)]]

        planes = {}
        for ex in (-1, 0, 1):
            lines = {}
            for ey in (-1, 0, 1):
                c = brick(ex, ey, 0)
                lo, hi = _neighbour_z(c, brick(ex, ey, -1), brick(ex, ey, 1), z)
                lines[ey] = c + 0.5 * (lo + hi)
            lo, hi = _neighbour_y(lines[0], lines[-1], lines[1], y)
            planes[ex] = lines[0] + 0.5 * (lo + hi)
        lo, hi = _neighbour_x(planes[0], planes[-1], planes[1], row)
        smoothed = planes[0] + 0.5 * (lo + hi)
        out_ref[b] = (diag_ref[b] + 2.0) * own - 2.0 * smoothed


def _divergence_kernel(tab_ref, src_ref, out_ref):
    row, y, z = _masks()
    bricks = out_ref.shape[0]
    for b in range(bricks):

        def brick(k, ex, ey, ez):
            if ex == 0 and ey == 0 and ez == 0:
                return src_ref[k, 4 * bricks + b]
            return src_ref[k, tab_ref[b * 27 + _column(ex, ey, ez)]]

        lo, hi = _neighbour_x(brick(0, 0, 0, 0), brick(0, -1, 0, 0), brick(0, 1, 0, 0), row)
        change_x = hi - lo
        lo, hi = _neighbour_y(brick(1, 0, 0, 0), brick(1, 0, -1, 0), brick(1, 0, 1, 0), y)
        change_y = hi - lo
        lo, hi = _neighbour_z(brick(2, 0, 0, 0), brick(2, 0, 0, -1), brick(2, 0, 0, 1), z)
        change_z = hi - lo
        out_ref[b] = -4.0 * ((change_x + change_y) + change_z)


def _local_call(kernel, out_shape, operands, flops):
    spaces = [pltpu.SMEM] + [pltpu.VMEM] * (len(operands) - 1)
    moved = sum(int(a.size) * 4 for a in operands) + math.prod(out_shape) * 4
    return pl.pallas_call(
        kernel,
        out_shape=jax.ShapeDtypeStruct(out_shape, jnp.float32),
        in_specs=[pl.BlockSpec(memory_space=s) for s in spaces],
        out_specs=pl.BlockSpec(memory_space=pltpu.VMEM),
        cost_estimate=pl.CostEstimate(flops=flops, bytes_accessed=moved, transcendentals=0),
    )(*operands)


def _shift(field, axis, step):
    size = lax.axis_size(axis)
    pairs = [(i + step, i) for i in range(size) if 0 <= i + step < size]
    return lax.ppermute(field, axis, pairs)


def halo(field):
    lead, bricks = field.shape[:-3], field.shape[-3]
    column = jnp.stack([_shift(field, "wide", -1), field, _shift(field, "wide", 1)], axis=-4)
    block = jnp.stack([_shift(column, "narrow", -1), column, _shift(column, "narrow", 1)], axis=-4)
    block = block.reshape(lead + (9 * bricks,) + field.shape[-2:])
    zero = jnp.zeros(lead + (1,) + field.shape[-2:], field.dtype)
    return jnp.concatenate([block, zero], axis=-3)


def shards(point_owner, point_cell, normals, strip_count, neighbours):
    owners = lax.axis_size("wide")
    devices = owners * lax.axis_size("narrow")
    point_total = point_cell.shape[0]
    bricks = neighbours.shape[2]
    table = neighbours.reshape(bricks * 27)

    owner = point_owner[:, 0]
    slots = jnp.arange(point_total, dtype=jnp.int32)
    is_live = slots < strip_count[0]
    code = jnp.where(is_live, point_cell + 1, 0).astype(jnp.float32)
    owner_hot = (owner[:, None] == jnp.arange(owners, dtype=jnp.int32)[None, :]).astype(jnp.bfloat16)
    earlier = (slots[None, :] < slots[:, None]).astype(jnp.bfloat16)
    before = jnp.dot(earlier, owner_hot, preferred_element_type=jnp.float32)
    rank = jnp.sum(before * owner_hot.astype(jnp.float32), axis=1).astype(jnp.int32)
    dest = owner * CAP + rank
    payload = jnp.concatenate([code[:, None], normals.T], axis=1)
    place_hot = (jnp.arange(owners * CAP, dtype=jnp.int32)[:, None] == dest[None, :]).astype(jnp.float32)
    send = jnp.dot(place_hot, payload, precision=HIGHEST, preferred_element_type=jnp.float32)
    got = lax.all_to_all(send.reshape(owners, CAP, 4), "wide", 0, 0, tiled=True).reshape(owners * CAP, 4)

    cell = got[:, 0].astype(jnp.int32) - 1
    brick_x = cell >> 8
    cell_yz = cell & (LANES - 1)
    bx_hot = (brick_x[:, None] == jnp.arange(bricks * ROWS, dtype=jnp.int32)[None, :]).astype(jnp.float32)
    yz_hot = (cell_yz[:, None] == jnp.arange(LANES, dtype=jnp.int32)[None, :]).astype(jnp.float32)
    weighted = jnp.concatenate([bx_hot * got[:, 1:2], bx_hot * got[:, 2:3], bx_hot * got[:, 3:4], bx_hot], axis=1)
    splatted = jnp.einsum("pa,pb->ab", weighted, yz_hot, precision=HIGHEST, preferred_element_type=jnp.float32)
    splatted = splatted.reshape(4, bricks, ROWS, LANES)
    vector_field = splatted[:3]
    diagonal = 14.5 + 2.0 * splatted[3]

    shape = (bricks, ROWS, LANES)
    right_side = _local_call(_divergence_kernel, shape, [table, halo(vector_field)], 20 * bricks * 4096)

    def global_sum(parts):
        stacked = jnp.stack(parts)[None, :]
        spread = jnp.broadcast_to(stacked, (devices, stacked.shape[1]))
        gathered = lax.all_to_all(spread, ("wide", "narrow"), 0, 0, tiled=True)
        return jnp.sum(gathered, axis=0)

    residual = right_side
    solution = jnp.zeros_like(right_side)
    for iteration in range(ITERS):
        image_r = _local_call(_stencil_kernel, shape, [table, halo(residual), diagonal], 60 * bricks * 4096)
        sums = global_sum([jnp.sum(residual * residual), jnp.sum(residual * image_r)])
        norm_now, curvature = sums[0], sums[1]
        if iteration == 0:
            step_size = norm_now / curvature
            direction, image_field = residual, image_r
        else:
            ratio = norm_now / norm_before
            step_size = norm_now / (curvature - ratio * norm_now / step_before)
            direction = residual + ratio * direction
            image_field = image_r + ratio * image_field
        solution = solution + step_size * direction
        residual = residual - step_size * image_field
        norm_before, step_before = norm_now, step_size
    out = (1, 1, bricks, ROWS * LANES)
    return solution.reshape(out), residual.reshape(out)


def solution(mesh):
    return jax.shard_map(
        shards,
        mesh=mesh,
        in_specs=(
            P(("wide", "narrow"), None),
            P(("wide", "narrow")),
            P(None, ("wide", "narrow")),
            P(("wide", "narrow")),
            P("wide", "narrow", None, None),
        ),
        out_specs=(P("wide", "narrow", None, None), P("wide", "narrow", None, None)),
        check_vma=False,
    )
```

```python
import functools
import math

import jax
import jax.numpy as jnp
from jax import lax
from jax.experimental import pallas as pl
from jax.experimental.pallas import tpu as pltpu
from jax.sharding import PartitionSpec as P

ITERS = 3
CAP = 32
HIGHEST = lax.Precision.HIGHEST
ROWS, LANES = 16, 256
SHIFT, SPAN = 8.0, 8.0


def _solve(matrix, rhs):
    n = len(rhs)
    m = [list(r) + [v] for r, v in zip(matrix, rhs)]
    for k in range(n):
        for i in range(k + 1, n):
            f = m[i][k] / m[k][k]
            m[i] = [m[i][j] - f * m[k][j] if j > k else m[i][j] for j in range(n + 1)]
    x = [None] * n
    for i in reversed(range(n)):
        acc = m[i][n]
        for j in range(i + 1, n):
            acc = acc - m[i][j] * x[j]
        x[i] = acc / m[i][i]
    return x


def _two_sum(a, b):
    total = a + b
    part = total - a
    return total, (a - (total - part)) + (b - part)


def _split(a):
    scaled = a * 4097.0
    high = scaled - (scaled - a)
    return high, a - high


def _two_prod(a, b):
    product = a * b
    ah, al = _split(a)
    bh, bl = _split(b)
    return product, ((ah * bh - product) + ah * bl + al * bh) + al * bl


def _halve(s, e, axis, stop):
    while s.shape[axis] > stop:
        h = s.shape[axis] // 2
        first = lax.slice_in_dim(s, 0, h, axis=axis)
        second = lax.slice_in_dim(s, h, 2 * h, axis=axis)
        s, err = _two_sum(first, second)
        e = lax.slice_in_dim(e, 0, h, axis=axis) + lax.slice_in_dim(e, h, 2 * h, axis=axis) + err
    return s, e


def _spread(s, e, axis):
    k = s.shape[axis] // 2
    while k >= 1:
        s, err = _two_sum(s, pltpu.roll(s, k, axis))
        e = e + pltpu.roll(e, k, axis) + err
        k //= 2
    return s, e


def _dd_add(x, y):
    s, e = _two_sum(x[0], y[0])
    return _two_sum(s, e + (x[1] + y[1]))


def _gram_kernel(basis_ref, out_ref):
    row = lax.broadcasted_iota(jnp.int32, out_ref.shape, 0)
    lane = lax.broadcasted_iota(jnp.int32, out_ref.shape, 1)
    count = basis_ref.shape[0]
    acc = jnp.zeros(out_ref.shape, jnp.float32)
    k = 0
    for i in range(count):
        for j in range(i, count):
            s, e = _two_prod(basis_ref[i], basis_ref[j])
            s, e = _halve(s, e, 0, 8)
            s, e = _halve(s, e, 1, 128)
            s, e = _spread(s, e, 0)
            s, e = _spread(s, e, 1)
            high, low = _two_sum(s, e)
            acc = jnp.where((row == 0) & (lane == k), high, acc)
            acc = jnp.where((row == 1) & (lane == k), low, acc)
            k += 1
    out_ref[...] = acc


def _galerkin_kernel(parts_ref, out_ref, lift=None):
    half = parts_ref.shape[0] // 2
    s, e = _halve(parts_ref[0:half, :], parts_ref[half:, :], 1, 128)
    s, e = _spread(s, e, 1)
    high, low = _two_sum(s, e)
    rows = lax.broadcasted_iota(jnp.int32, high.shape, 0)

    def pick(values, k):
        return jnp.sum(jnp.where(rows == k, values, 0.0), axis=0, keepdims=True)

    size = len(lift)
    pairs = [(i, j) for i in range(size) for j in range(i, size)]
    gram = {}
    for k, (i, j) in enumerate(pairs):
        gram[i, j] = gram[j, i] = (pick(high, k), pick(low, k))
    n = size - 1
    matrix = [[None] * n for _ in range(n)]
    for i in range(n):
        for j in range(n):
            entry = None
            for k in range(size):
                if lift[k][j] != 0.0:
                    term = (lift[k][j] * gram[i, k][0], lift[k][j] * gram[i, k][1])
                    entry = term if entry is None else _dd_add(entry, term)
            matrix[i][j] = entry
    wanted = [gram[i, 0] for i in range(n)]
    top = [[matrix[i][j][0] for j in range(n)] for i in range(n)]
    coeff = _solve(top, [w[0] for w in wanted])
    misfit = []
    for i in range(n):
        acc = wanted[i]
        for j in range(n):
            p, pe = _two_prod(matrix[i][j][0], coeff[j])
            acc = _dd_add(acc, (-p, -(pe + matrix[i][j][1] * coeff[j])))
        misfit.append(acc[0] + acc[1])
    coeff = [c + d for c, d in zip(coeff, _solve(top, misfit))]
    values = list(coeff)
    for k in range(size):
        terms = [lift[k][j] * coeff[j] for j in range(n) if lift[k][j] != 0.0]
        values.append((1.0 if k == 0 else 0.0) - sum(terms[1:], terms[0]))
    out_rows = lax.broadcasted_iota(jnp.int32, out_ref.shape, 0)
    out = jnp.zeros(out_ref.shape, jnp.float32)
    for k, v in enumerate(values):
        out = jnp.where(out_rows == k, v, out)
    out_ref[...] = out


def _masks():
    shape = (ROWS, LANES)
    lane = lax.broadcasted_iota(jnp.int32, shape, 1)
    row = lax.broadcasted_iota(jnp.int32, shape, 0)
    return row, lane >> 4, lane & 15


def _neighbour_x(c, m, p, row):
    lo = jnp.where(row == 0, pltpu.roll(m, 1, 0), pltpu.roll(c, 1, 0))
    hi = jnp.where(row == ROWS - 1, pltpu.roll(p, ROWS - 1, 0), pltpu.roll(c, ROWS - 1, 0))
    return lo, hi


def _neighbour_y(c, m, p, y):
    lo = jnp.where(y == 0, pltpu.roll(m, 16, 1), pltpu.roll(c, 16, 1))
    hi = jnp.where(y == 15, pltpu.roll(p, LANES - 16, 1), pltpu.roll(c, LANES - 16, 1))
    return lo, hi


def _neighbour_z(c, m, p, z):
    lo = jnp.where(z == 0, pltpu.roll(m, LANES - 15, 1), pltpu.roll(c, 1, 1))
    hi = jnp.where(z == 15, pltpu.roll(p, 15, 1), pltpu.roll(c, LANES - 1, 1))
    return lo, hi


def _column(ex, ey, ez):
    return (ex + 1) * 9 + (ey + 1) * 3 + (ez + 1)


def _stencil_kernel(tab_ref, src_ref, diag_ref, out_ref, shift=0.0, scale=1.0):
    row, y, z = _masks()
    bricks = out_ref.shape[0]
    for b in range(bricks):
        own = src_ref[4 * bricks + b]

        def brick(ex, ey, ez):
            if ex == 0 and ey == 0 and ez == 0:
                return own
            return src_ref[tab_ref[b * 27 + _column(ex, ey, ez)]]

        planes = {}
        for ex in (-1, 0, 1):
            lines = {}
            for ey in (-1, 0, 1):
                c = brick(ex, ey, 0)
                lo, hi = _neighbour_z(c, brick(ex, ey, -1), brick(ex, ey, 1), z)
                lines[ey] = c + 0.5 * (lo + hi)
            lo, hi = _neighbour_y(lines[0], lines[-1], lines[1], y)
            planes[ex] = lines[0] + 0.5 * (lo + hi)
        lo, hi = _neighbour_x(planes[0], planes[-1], planes[1], row)
        smoothed = planes[0] + 0.5 * (lo + hi)
        out_ref[b] = ((diag_ref[b] + (2.0 - shift)) * own - 2.0 * smoothed) * scale


def _divergence_kernel(tab_ref, src_ref, out_ref):
    row, y, z = _masks()
    bricks = out_ref.shape[0]
    for b in range(bricks):

        def brick(k, ex, ey, ez):
            if ex == 0 and ey == 0 and ez == 0:
                return src_ref[k, 4 * bricks + b]
            return src_ref[k, tab_ref[b * 27 + _column(ex, ey, ez)]]

        lo, hi = _neighbour_x(brick(0, 0, 0, 0), brick(0, -1, 0, 0), brick(0, 1, 0, 0), row)
        change_x = hi - lo
        lo, hi = _neighbour_y(brick(1, 0, 0, 0), brick(1, 0, -1, 0), brick(1, 0, 1, 0), y)
        change_y = hi - lo
        lo, hi = _neighbour_z(brick(2, 0, 0, 0), brick(2, 0, 0, -1), brick(2, 0, 0, 1), z)
        change_z = hi - lo
        out_ref[b] = -4.0 * ((change_x + change_y) + change_z)


def _local_call(kernel, out_shape, operands, flops):
    spaces = [pltpu.SMEM] + [pltpu.VMEM] * (len(operands) - 1)
    moved = sum(int(a.size) * 4 for a in operands) + math.prod(out_shape) * 4
    return pl.pallas_call(
        kernel,
        out_shape=jax.ShapeDtypeStruct(out_shape, jnp.float32),
        in_specs=[pl.BlockSpec(memory_space=s) for s in spaces],
        out_specs=pl.BlockSpec(memory_space=pltpu.VMEM),
        cost_estimate=pl.CostEstimate(flops=flops, bytes_accessed=moved, transcendentals=0),
    )(*operands)


def _shift(field, axis, step):
    size = lax.axis_size(axis)
    pairs = [(i + step, i) for i in range(size) if 0 <= i + step < size]
    return lax.ppermute(field, axis, pairs)


def halo(field):
    lead, bricks = field.shape[:-3], field.shape[-3]
    column = jnp.stack([_shift(field, "wide", -1), field, _shift(field, "wide", 1)], axis=-4)
    block = jnp.stack([_shift(column, "narrow", -1), column, _shift(column, "narrow", 1)], axis=-4)
    block = block.reshape(lead + (9 * bricks,) + field.shape[-2:])
    zero = jnp.zeros(lead + (1,) + field.shape[-2:], field.dtype)
    return jnp.concatenate([block, zero], axis=-3)


def shards(point_owner, point_cell, normals, strip_count, neighbours):
    owners = lax.axis_size("wide")
    devices = owners * lax.axis_size("narrow")
    point_total = point_cell.shape[0]
    bricks = neighbours.shape[2]
    table = neighbours.reshape(bricks * 27)

    owner = point_owner[:, 0]
    slots = jnp.arange(point_total, dtype=jnp.int32)
    is_live = slots < strip_count[0]
    code = jnp.where(is_live, point_cell + 1, 0).astype(jnp.float32)
    owner_hot = (owner[:, None] == jnp.arange(owners, dtype=jnp.int32)[None, :]).astype(jnp.bfloat16)
    earlier = (slots[None, :] < slots[:, None]).astype(jnp.bfloat16)
    before = jnp.dot(earlier, owner_hot, preferred_element_type=jnp.float32)
    rank = jnp.sum(before * owner_hot.astype(jnp.float32), axis=1).astype(jnp.int32)
    dest = owner * CAP + rank
    payload = jnp.concatenate([code[:, None], normals.T], axis=1)
    place_hot = (jnp.arange(owners * CAP, dtype=jnp.int32)[:, None] == dest[None, :]).astype(jnp.float32)
    send = jnp.dot(place_hot, payload, precision=HIGHEST, preferred_element_type=jnp.float32)
    got = lax.all_to_all(send.reshape(owners, CAP, 4), "wide", 0, 0, tiled=True).reshape(owners * CAP, 4)

    cell = got[:, 0].astype(jnp.int32) - 1
    brick_x = cell >> 8
    cell_yz = cell & (LANES - 1)
    bx_hot = (brick_x[:, None] == jnp.arange(bricks * ROWS, dtype=jnp.int32)[None, :]).astype(jnp.float32)
    yz_hot = (cell_yz[:, None] == jnp.arange(LANES, dtype=jnp.int32)[None, :]).astype(jnp.float32)
    weighted = jnp.concatenate([bx_hot * got[:, 1:2], bx_hot * got[:, 2:3], bx_hot * got[:, 3:4], bx_hot], axis=1)
    splatted = jnp.einsum("pa,pb->ab", weighted, yz_hot, precision=HIGHEST, preferred_element_type=jnp.float32)
    splatted = splatted.reshape(4, bricks, ROWS, LANES)
    vector_field = splatted[:3]
    diagonal = 14.5 + 2.0 * splatted[3]

    shape = (bricks, ROWS, LANES)
    right_side = _local_call(_divergence_kernel, shape, [table, halo(vector_field)], 20 * bricks * 4096)

    basis = [right_side]
    kernel = functools.partial(_stencil_kernel, shift=SHIFT, scale=1.0 / SPAN)
    for k in range(ITERS):
        image = _local_call(kernel, shape, [table, halo(basis[-1]), diagonal], 60 * bricks * 4096)
        basis.append(image if k == 0 else 2.0 * image - basis[-2])
    lift = [[0.0] * ITERS for _ in range(ITERS + 1)]
    for k in range(ITERS):
        lift[k][k] = SHIFT
        if k == 0:
            lift[1][0] = SPAN
        else:
            lift[k - 1][k] = lift[k + 1][k] = 0.5 * SPAN
    vmem = pl.BlockSpec(memory_space=pltpu.VMEM)
    stacked = jnp.stack(basis).reshape(ITERS + 1, bricks * ROWS, LANES)
    partial_sums = pl.pallas_call(
        _gram_kernel, out_shape=jax.ShapeDtypeStruct((8, 128), jnp.float32), in_specs=[vmem], out_specs=vmem
    )(stacked)
    payload = partial_sums[0:2, 0:16].reshape(1, 32)
    gathered = lax.all_to_all(jnp.broadcast_to(payload, (devices, 32)), ("wide", "narrow"), 0, 0, tiled=True)
    found = pl.pallas_call(
        functools.partial(_galerkin_kernel, lift=lift),
        out_shape=jax.ShapeDtypeStruct((8, 128), jnp.float32),
        in_specs=[vmem],
        out_specs=vmem,
    )(jnp.pad(gathered.T, ((0, 0), (0, max(0, 128 - devices)))))
    coeff = [found[k, 0] for k in range(ITERS)]
    weights = [found[ITERS + k, 0] for k in range(ITERS + 1)]
    solution = coeff[0] * basis[0]
    for j in range(1, ITERS):
        solution = solution + coeff[j] * basis[j]
    residual = weights[0] * basis[0]
    for k in range(1, ITERS + 1):
        residual = residual + weights[k] * basis[k]
    out = (1, 1, bricks, ROWS * LANES)
    return solution.reshape(out), residual.reshape(out)


def solution(mesh):
    return jax.shard_map(
        shards,
        mesh=mesh,
        in_specs=(
            P(("wide", "narrow"), None),
            P(("wide", "narrow")),
            P(None, ("wide", "narrow")),
            P(("wide", "narrow")),
            P("wide", "narrow", None, None),
        ),
        out_specs=(P("wide", "narrow", None, None), P("wide", "narrow", None, None)),
        check_vma=False,
    )
```

```python
import functools
import math

import jax
import jax.numpy as jnp
from jax import lax
from jax.experimental import pallas as pl
from jax.experimental.pallas import tpu as pltpu
from jax.sharding import PartitionSpec as P

ITERS = 3
CAP = 32
HIGHEST = lax.Precision.HIGHEST
ROWS, LANES = 16, 256
SHIFT, SPAN = 8.0, 8.0


def _solve(matrix, rhs):
    n = len(rhs)
    m = [list(r) + [v] for r, v in zip(matrix, rhs)]
    for k in range(n):
        for i in range(k + 1, n):
            f = m[i][k] / m[k][k]
            m[i] = [m[i][j] - f * m[k][j] if j > k else m[i][j] for j in range(n + 1)]
    x = [None] * n
    for i in reversed(range(n)):
        acc = m[i][n]
        for j in range(i + 1, n):
            acc = acc - m[i][j] * x[j]
        x[i] = acc / m[i][i]
    return x


def _two_sum(a, b):
    total = a + b
    part = total - a
    return total, (a - (total - part)) + (b - part)


def _split(a):
    scaled = a * 4097.0
    high = scaled - (scaled - a)
    return high, a - high


def _two_prod(a, b):
    product = a * b
    ah, al = _split(a)
    bh, bl = _split(b)
    return product, ((ah * bh - product) + ah * bl + al * bh) + al * bl


def _halve(s, e, axis, stop):
    while s.shape[axis] > stop:
        h = s.shape[axis] // 2
        first = lax.slice_in_dim(s, 0, h, axis=axis)
        second = lax.slice_in_dim(s, h, 2 * h, axis=axis)
        s, err = _two_sum(first, second)
        e = lax.slice_in_dim(e, 0, h, axis=axis) + lax.slice_in_dim(e, h, 2 * h, axis=axis) + err
    return s, e


def _spread(s, e, axis):
    k = s.shape[axis] // 2
    while k >= 1:
        s, err = _two_sum(s, pltpu.roll(s, k, axis))
        e = e + pltpu.roll(e, k, axis) + err
        k //= 2
    return s, e


def _dd_add(x, y):
    s, e = _two_sum(x[0], y[0])
    return _two_sum(s, e + (x[1] + y[1]))


def _gram_kernel(basis_ref, out_ref):
    row = lax.broadcasted_iota(jnp.int32, out_ref.shape, 0)
    lane = lax.broadcasted_iota(jnp.int32, out_ref.shape, 1)
    count = basis_ref.shape[0]
    acc = jnp.zeros(out_ref.shape, jnp.float32)
    k = 0
    for i in range(count):
        for j in range(i, count):
            s, e = _two_prod(basis_ref[i], basis_ref[j])
            s, e = _halve(s, e, 0, 8)
            s, e = _halve(s, e, 1, 128)
            s, e = _spread(s, e, 0)
            s, e = _spread(s, e, 1)
            high, low = _two_sum(s, e)
            acc = jnp.where((row == 0) & (lane == k), high, acc)
            acc = jnp.where((row == 1) & (lane == k), low, acc)
            k += 1
    out_ref[...] = acc


def _galerkin_kernel(parts_ref, basis_ref, solution_ref, residual_ref, lift=None):
    half = parts_ref.shape[0] // 2
    s, e = _halve(parts_ref[0:half, :], parts_ref[half:, :], 1, 128)
    s, e = _spread(s, e, 1)
    high, low = _two_sum(s, e)
    rows = lax.broadcasted_iota(jnp.int32, high.shape, 0)

    def pick(values, k):
        return jnp.sum(jnp.where(rows == k, values, 0.0), axis=0, keepdims=True)

    size = len(lift)
    pairs = [(i, j) for i in range(size) for j in range(i, size)]
    gram = {}
    for k, (i, j) in enumerate(pairs):
        gram[i, j] = gram[j, i] = (pick(high, k), pick(low, k))
    n = size - 1
    matrix = [[None] * n for _ in range(n)]
    for i in range(n):
        for j in range(n):
            entry = None
            for k in range(size):
                if lift[k][j] != 0.0:
                    term = (lift[k][j] * gram[i, k][0], lift[k][j] * gram[i, k][1])
                    entry = term if entry is None else _dd_add(entry, term)
            matrix[i][j] = entry
    wanted = [gram[i, 0] for i in range(n)]
    top = [[matrix[i][j][0] for j in range(n)] for i in range(n)]
    coeff = _solve(top, [w[0] for w in wanted])
    misfit = []
    for i in range(n):
        acc = wanted[i]
        for j in range(n):
            p, pe = _two_prod(matrix[i][j][0], coeff[j])
            acc = _dd_add(acc, (-p, -(pe + matrix[i][j][1] * coeff[j])))
        misfit.append(acc[0] + acc[1])
    coeff = [c + d for c, d in zip(coeff, _solve(top, misfit))]
    weights = []
    for k in range(size):
        terms = [lift[k][j] * coeff[j] for j in range(n) if lift[k][j] != 0.0]
        weights.append((1.0 if k == 0 else 0.0) - sum(terms[1:], terms[0]))
    shape = solution_ref.shape

    def wide(v):
        v = jnp.broadcast_to(v, (shape[0], v.shape[1]))
        return jnp.concatenate([v] * (shape[1] // v.shape[1]), axis=1)

    total = wide(coeff[0]) * basis_ref[0]
    for j in range(1, n):
        total = total + wide(coeff[j]) * basis_ref[j]
    solution_ref[...] = total
    total = wide(weights[0]) * basis_ref[0]
    for k in range(1, size):
        total = total + wide(weights[k]) * basis_ref[k]
    residual_ref[...] = total


def _masks():
    shape = (ROWS, LANES)
    lane = lax.broadcasted_iota(jnp.int32, shape, 1)
    row = lax.broadcasted_iota(jnp.int32, shape, 0)
    return row, lane >> 4, lane & 15


def _neighbour_x(c, m, p, row):
    lo = jnp.where(row == 0, pltpu.roll(m, 1, 0), pltpu.roll(c, 1, 0))
    hi = jnp.where(row == ROWS - 1, pltpu.roll(p, ROWS - 1, 0), pltpu.roll(c, ROWS - 1, 0))
    return lo, hi


def _neighbour_y(c, m, p, y):
    lo = jnp.where(y == 0, pltpu.roll(m, 16, 1), pltpu.roll(c, 16, 1))
    hi = jnp.where(y == 15, pltpu.roll(p, LANES - 16, 1), pltpu.roll(c, LANES - 16, 1))
    return lo, hi


def _neighbour_z(c, m, p, z):
    lo = jnp.where(z == 0, pltpu.roll(m, LANES - 15, 1), pltpu.roll(c, 1, 1))
    hi = jnp.where(z == 15, pltpu.roll(p, 15, 1), pltpu.roll(c, LANES - 1, 1))
    return lo, hi


def _column(ex, ey, ez):
    return (ex + 1) * 9 + (ey + 1) * 3 + (ez + 1)


def _stencil_kernel(tab_ref, src_ref, diag_ref, out_ref, shift=0.0, scale=1.0):
    row, y, z = _masks()
    bricks = out_ref.shape[0]
    for b in range(bricks):
        own = src_ref[4 * bricks + b]

        def brick(ex, ey, ez):
            if ex == 0 and ey == 0 and ez == 0:
                return own
            return src_ref[tab_ref[b * 27 + _column(ex, ey, ez)]]

        planes = {}
        for ex in (-1, 0, 1):
            lines = {}
            for ey in (-1, 0, 1):
                c = brick(ex, ey, 0)
                lo, hi = _neighbour_z(c, brick(ex, ey, -1), brick(ex, ey, 1), z)
                lines[ey] = c + 0.5 * (lo + hi)
            lo, hi = _neighbour_y(lines[0], lines[-1], lines[1], y)
            planes[ex] = lines[0] + 0.5 * (lo + hi)
        lo, hi = _neighbour_x(planes[0], planes[-1], planes[1], row)
        smoothed = planes[0] + 0.5 * (lo + hi)
        out_ref[b] = ((diag_ref[b] + (2.0 - shift)) * own - 2.0 * smoothed) * scale


def _divergence_kernel(tab_ref, src_ref, out_ref):
    row, y, z = _masks()
    bricks = out_ref.shape[0]
    for b in range(bricks):

        def brick(k, ex, ey, ez):
            if ex == 0 and ey == 0 and ez == 0:
                return src_ref[k, 4 * bricks + b]
            return src_ref[k, tab_ref[b * 27 + _column(ex, ey, ez)]]

        lo, hi = _neighbour_x(brick(0, 0, 0, 0), brick(0, -1, 0, 0), brick(0, 1, 0, 0), row)
        change_x = hi - lo
        lo, hi = _neighbour_y(brick(1, 0, 0, 0), brick(1, 0, -1, 0), brick(1, 0, 1, 0), y)
        change_y = hi - lo
        lo, hi = _neighbour_z(brick(2, 0, 0, 0), brick(2, 0, 0, -1), brick(2, 0, 0, 1), z)
        change_z = hi - lo
        out_ref[b] = -4.0 * ((change_x + change_y) + change_z)


def _local_call(kernel, out_shape, operands, flops):
    spaces = [pltpu.SMEM] + [pltpu.VMEM] * (len(operands) - 1)
    moved = sum(int(a.size) * 4 for a in operands) + math.prod(out_shape) * 4
    return pl.pallas_call(
        kernel,
        out_shape=jax.ShapeDtypeStruct(out_shape, jnp.float32),
        in_specs=[pl.BlockSpec(memory_space=s) for s in spaces],
        out_specs=pl.BlockSpec(memory_space=pltpu.VMEM),
        cost_estimate=pl.CostEstimate(flops=flops, bytes_accessed=moved, transcendentals=0),
    )(*operands)


def _shift(field, axis, step):
    size = lax.axis_size(axis)
    pairs = [(i + step, i) for i in range(size) if 0 <= i + step < size]
    return lax.ppermute(field, axis, pairs)


def halo(field):
    lead, bricks = field.shape[:-3], field.shape[-3]
    column = jnp.stack([_shift(field, "wide", -1), field, _shift(field, "wide", 1)], axis=-4)
    block = jnp.stack([_shift(column, "narrow", -1), column, _shift(column, "narrow", 1)], axis=-4)
    block = block.reshape(lead + (9 * bricks,) + field.shape[-2:])
    zero = jnp.zeros(lead + (1,) + field.shape[-2:], field.dtype)
    return jnp.concatenate([block, zero], axis=-3)


def shards(point_owner, point_cell, normals, strip_count, neighbours):
    owners = lax.axis_size("wide")
    devices = owners * lax.axis_size("narrow")
    point_total = point_cell.shape[0]
    bricks = neighbours.shape[2]
    table = neighbours.reshape(bricks * 27)

    owner = point_owner[:, 0]
    slots = jnp.arange(point_total, dtype=jnp.int32)
    is_live = slots < strip_count[0]
    code = jnp.where(is_live, point_cell + 1, 0).astype(jnp.float32)
    owner_hot = (owner[:, None] == jnp.arange(owners, dtype=jnp.int32)[None, :]).astype(jnp.bfloat16)
    earlier = (slots[None, :] < slots[:, None]).astype(jnp.bfloat16)
    before = jnp.dot(earlier, owner_hot, preferred_element_type=jnp.float32)
    rank = jnp.sum(before * owner_hot.astype(jnp.float32), axis=1).astype(jnp.int32)
    dest = owner * CAP + rank
    payload = jnp.concatenate([code[:, None], normals.T], axis=1)
    place_hot = (jnp.arange(owners * CAP, dtype=jnp.int32)[:, None] == dest[None, :]).astype(jnp.float32)
    send = jnp.dot(place_hot, payload, precision=HIGHEST, preferred_element_type=jnp.float32)
    got = lax.all_to_all(send.reshape(owners, CAP, 4), "wide", 0, 0, tiled=True).reshape(owners * CAP, 4)

    cell = got[:, 0].astype(jnp.int32) - 1
    brick_x = cell >> 8
    cell_yz = cell & (LANES - 1)
    bx_hot = (brick_x[:, None] == jnp.arange(bricks * ROWS, dtype=jnp.int32)[None, :]).astype(jnp.float32)
    yz_hot = (cell_yz[:, None] == jnp.arange(LANES, dtype=jnp.int32)[None, :]).astype(jnp.float32)
    weighted = jnp.concatenate([bx_hot * got[:, 1:2], bx_hot * got[:, 2:3], bx_hot * got[:, 3:4], bx_hot], axis=1)
    splatted = jnp.einsum("pa,pb->ab", weighted, yz_hot, precision=HIGHEST, preferred_element_type=jnp.float32)
    splatted = splatted.reshape(4, bricks, ROWS, LANES)
    vector_field = splatted[:3]
    diagonal = 14.5 + 2.0 * splatted[3]

    shape = (bricks, ROWS, LANES)
    right_side = _local_call(_divergence_kernel, shape, [table, halo(vector_field)], 20 * bricks * 4096)

    basis = [right_side]
    kernel = functools.partial(_stencil_kernel, shift=SHIFT, scale=1.0 / SPAN)
    for k in range(ITERS):
        image = _local_call(kernel, shape, [table, halo(basis[-1]), diagonal], 60 * bricks * 4096)
        basis.append(image if k == 0 else 2.0 * image - basis[-2])
    lift = [[0.0] * ITERS for _ in range(ITERS + 1)]
    for k in range(ITERS):
        lift[k][k] = SHIFT
        if k == 0:
            lift[1][0] = SPAN
        else:
            lift[k - 1][k] = lift[k + 1][k] = 0.5 * SPAN
    vmem = pl.BlockSpec(memory_space=pltpu.VMEM)
    stacked = jnp.stack(basis).reshape(ITERS + 1, bricks * ROWS, LANES)
    partial_sums = pl.pallas_call(
        _gram_kernel, out_shape=jax.ShapeDtypeStruct((8, 128), jnp.float32), in_specs=[vmem], out_specs=vmem
    )(stacked)
    payload = partial_sums[0:2, 0:16].reshape(1, 32)
    gathered = lax.all_to_all(jnp.broadcast_to(payload, (devices, 32)), ("wide", "narrow"), 0, 0, tiled=True)
    flat = jax.ShapeDtypeStruct((bricks * ROWS, LANES), jnp.float32)
    solution, residual = pl.pallas_call(
        functools.partial(_galerkin_kernel, lift=lift),
        out_shape=(flat, flat),
        in_specs=[vmem, vmem],
        out_specs=(vmem, vmem),
    )(jnp.pad(gathered.T, ((0, 0), (0, max(0, 128 - devices)))), stacked)
    out = (1, 1, bricks, ROWS * LANES)
    return solution.reshape(out), residual.reshape(out)


def solution(mesh):
    return jax.shard_map(
        shards,
        mesh=mesh,
        in_specs=(
            P(("wide", "narrow"), None),
            P(("wide", "narrow")),
            P(None, ("wide", "narrow")),
            P(("wide", "narrow")),
            P("wide", "narrow", None, None),
        ),
        out_specs=(P("wide", "narrow", None, None), P("wide", "narrow", None, None)),
        check_vma=False,
    )
```

```python
import functools
import math

import jax
import jax.numpy as jnp
from jax import lax
from jax.experimental import pallas as pl
from jax.experimental.pallas import tpu as pltpu
from jax.sharding import PartitionSpec as P

ITERS = 3
CAP = 32
HIGHEST = lax.Precision.HIGHEST
ROWS, LANES = 16, 256
SHIFT, SPAN = 8.0, 8.0


def _solve(matrix, rhs):
    n = len(rhs)
    m = [list(r) + [v] for r, v in zip(matrix, rhs)]
    for k in range(n):
        for i in range(k + 1, n):
            f = m[i][k] / m[k][k]
            m[i] = [m[i][j] - f * m[k][j] if j > k else m[i][j] for j in range(n + 1)]
    x = [None] * n
    for i in reversed(range(n)):
        acc = m[i][n]
        for j in range(i + 1, n):
            acc = acc - m[i][j] * x[j]
        x[i] = acc / m[i][i]
    return x


def _two_sum(a, b):
    total = a + b
    part = total - a
    return total, (a - (total - part)) + (b - part)


def _split(a):
    scaled = a * 4097.0
    high = scaled - (scaled - a)
    return high, a - high


def _two_prod(a, b):
    product = a * b
    ah, al = _split(a)
    bh, bl = _split(b)
    return product, ((ah * bh - product) + ah * bl + al * bh) + al * bl


def _halve(s, e, axis, stop):
    while s.shape[axis] > stop:
        h = s.shape[axis] // 2
        first = lax.slice_in_dim(s, 0, h, axis=axis)
        second = lax.slice_in_dim(s, h, 2 * h, axis=axis)
        s, err = _two_sum(first, second)
        e = lax.slice_in_dim(e, 0, h, axis=axis) + lax.slice_in_dim(e, h, 2 * h, axis=axis) + err
    return s, e


def _spread(s, e, axis):
    k = s.shape[axis] // 2
    while k >= 1:
        s, err = _two_sum(s, pltpu.roll(s, k, axis))
        e = e + pltpu.roll(e, k, axis) + err
        k //= 2
    return s, e


def _dd_add(x, y):
    s, e = _two_sum(x[0], y[0])
    return _two_sum(s, e + (x[1] + y[1]))


def _gram_kernel(basis_ref, out_ref):
    row = lax.broadcasted_iota(jnp.int32, out_ref.shape, 0)
    lane = lax.broadcasted_iota(jnp.int32, out_ref.shape, 1)
    count = basis_ref.shape[0]
    acc = jnp.zeros(out_ref.shape, jnp.float32)
    k = 0
    for i in range(count):
        for j in range(i, count):
            s, e = _two_prod(basis_ref[i], basis_ref[j])
            s, e = _halve(s, e, 0, 8)
            s, e = _halve(s, e, 1, 128)
            s, e = _spread(s, e, 0)
            s, e = _spread(s, e, 1)
            high, low = _two_sum(s, e)
            acc = jnp.where((row == 0) & (lane == k), high, acc)
            acc = jnp.where((row == 1) & (lane == k), low, acc)
            k += 1
    out_ref[...] = acc


def _galerkin_kernel(parts_ref, basis_ref, solution_ref, residual_ref, lift=None):
    half = parts_ref.shape[0] // 2
    s, e = _halve(parts_ref[0:half, :], parts_ref[half:, :], 1, 128)
    s, e = _spread(s, e, 1)
    high, low = _two_sum(s, e)
    rows = lax.broadcasted_iota(jnp.int32, high.shape, 0)

    def pick(values, k):
        return jnp.sum(jnp.where(rows == k, values, 0.0), axis=0, keepdims=True)

    size = len(lift)
    pairs = [(i, j) for i in range(size) for j in range(i, size)]
    gram = {}
    for k, (i, j) in enumerate(pairs):
        gram[i, j] = gram[j, i] = (pick(high, k), pick(low, k))
    n = size - 1
    matrix = [[None] * n for _ in range(n)]
    for i in range(n):
        for j in range(n):
            entry = None
            for k in range(size):
                if lift[k][j] != 0.0:
                    term = (lift[k][j] * gram[i, k][0], lift[k][j] * gram[i, k][1])
                    entry = term if entry is None else _dd_add(entry, term)
            matrix[i][j] = entry
    wanted = [gram[i, 0] for i in range(n)]
    top = [[matrix[i][j][0] for j in range(n)] for i in range(n)]
    coeff = _solve(top, [w[0] for w in wanted])
    misfit = []
    for i in range(n):
        acc = wanted[i]
        for j in range(n):
            p, pe = _two_prod(matrix[i][j][0], coeff[j])
            acc = _dd_add(acc, (-p, -(pe + matrix[i][j][1] * coeff[j])))
        misfit.append(acc[0] + acc[1])
    coeff = [c + d for c, d in zip(coeff, _solve(top, misfit))]
    weights = []
    for k in range(size):
        terms = [lift[k][j] * coeff[j] for j in range(n) if lift[k][j] != 0.0]
        weights.append((1.0 if k == 0 else 0.0) - sum(terms[1:], terms[0]))
    shape = solution_ref.shape

    def wide(v):
        v = jnp.broadcast_to(v, (shape[0], v.shape[1]))
        return jnp.concatenate([v] * (shape[1] // v.shape[1]), axis=1)

    total = wide(coeff[0]) * basis_ref[0]
    for j in range(1, n):
        total = total + wide(coeff[j]) * basis_ref[j]
    solution_ref[...] = total
    total = wide(weights[0]) * basis_ref[0]
    for k in range(1, size):
        total = total + wide(weights[k]) * basis_ref[k]
    residual_ref[...] = total


def _masks():
    shape = (ROWS, LANES)
    lane = lax.broadcasted_iota(jnp.int32, shape, 1)
    row = lax.broadcasted_iota(jnp.int32, shape, 0)
    return row, lane >> 4, lane & 15


def _neighbour_x(c, m, p, row):
    lo = jnp.where(row == 0, pltpu.roll(m, 1, 0), pltpu.roll(c, 1, 0))
    hi = jnp.where(row == ROWS - 1, pltpu.roll(p, ROWS - 1, 0), pltpu.roll(c, ROWS - 1, 0))
    return lo, hi


def _neighbour_y(c, m, p, y):
    lo = jnp.where(y == 0, pltpu.roll(m, 16, 1), pltpu.roll(c, 16, 1))
    hi = jnp.where(y == 15, pltpu.roll(p, LANES - 16, 1), pltpu.roll(c, LANES - 16, 1))
    return lo, hi


def _neighbour_z(c, m, p, z):
    lo = jnp.where(z == 0, pltpu.roll(m, LANES - 15, 1), pltpu.roll(c, 1, 1))
    hi = jnp.where(z == 15, pltpu.roll(p, 15, 1), pltpu.roll(c, LANES - 1, 1))
    return lo, hi


def _column(ex, ey, ez):
    return (ex + 1) * 9 + (ey + 1) * 3 + (ez + 1)


def _stencil_kernel(tab_ref, src_ref, diag_ref, out_ref, shift=0.0, scale=1.0):
    row, y, z = _masks()
    bricks = out_ref.shape[0]
    for b in range(bricks):
        own = src_ref[4 * bricks + b]

        def brick(ex, ey, ez):
            if ex == 0 and ey == 0 and ez == 0:
                return own
            return src_ref[tab_ref[b * 27 + _column(ex, ey, ez)]]

        planes = {}
        for ex in (-1, 0, 1):
            lines = {}
            for ey in (-1, 0, 1):
                c = brick(ex, ey, 0)
                lo, hi = _neighbour_z(c, brick(ex, ey, -1), brick(ex, ey, 1), z)
                lines[ey] = c + 0.5 * (lo + hi)
            lo, hi = _neighbour_y(lines[0], lines[-1], lines[1], y)
            planes[ex] = lines[0] + 0.5 * (lo + hi)
        lo, hi = _neighbour_x(planes[0], planes[-1], planes[1], row)
        smoothed = planes[0] + 0.5 * (lo + hi)
        out_ref[b] = ((diag_ref[b] + (2.0 - shift)) * own - 2.0 * smoothed) * scale


def _divergence_kernel(tab_ref, src_ref, out_ref):
    row, y, z = _masks()
    bricks = out_ref.shape[0]
    for b in range(bricks):

        def brick(k, ex, ey, ez):
            if ex == 0 and ey == 0 and ez == 0:
                return src_ref[k, 4 * bricks + b]
            return src_ref[k, tab_ref[b * 27 + _column(ex, ey, ez)]]

        lo, hi = _neighbour_x(brick(0, 0, 0, 0), brick(0, -1, 0, 0), brick(0, 1, 0, 0), row)
        change_x = hi - lo
        lo, hi = _neighbour_y(brick(1, 0, 0, 0), brick(1, 0, -1, 0), brick(1, 0, 1, 0), y)
        change_y = hi - lo
        lo, hi = _neighbour_z(brick(2, 0, 0, 0), brick(2, 0, 0, -1), brick(2, 0, 0, 1), z)
        change_z = hi - lo
        out_ref[b] = -4.0 * ((change_x + change_y) + change_z)


def _local_call(kernel, out_shape, operands, flops):
    spaces = [pltpu.SMEM] + [pltpu.VMEM] * (len(operands) - 1)
    moved = sum(int(a.size) * 4 for a in operands) + math.prod(out_shape) * 4
    return pl.pallas_call(
        kernel,
        out_shape=jax.ShapeDtypeStruct(out_shape, jnp.float32),
        in_specs=[pl.BlockSpec(memory_space=s) for s in spaces],
        out_specs=pl.BlockSpec(memory_space=pltpu.VMEM),
        cost_estimate=pl.CostEstimate(flops=flops, bytes_accessed=moved, transcendentals=0),
    )(*operands)


def _shift(field, axis, step):
    size = lax.axis_size(axis)
    pairs = [(i + step, i) for i in range(size) if 0 <= i + step < size]
    return lax.ppermute(field, axis, pairs)


def halo(field):
    lead, bricks = field.shape[:-3], field.shape[-3]
    column = jnp.stack([_shift(field, "narrow", -1), field, _shift(field, "narrow", 1)], axis=-4)
    block = jnp.stack([_shift(column, "wide", -1), column, _shift(column, "wide", 1)], axis=-5)
    block = block.reshape(lead + (9 * bricks,) + field.shape[-2:])
    zero = jnp.zeros(lead + (1,) + field.shape[-2:], field.dtype)
    return jnp.concatenate([block, zero], axis=-3)


def shards(point_owner, point_cell, normals, strip_count, neighbours):
    owners = lax.axis_size("wide")
    devices = owners * lax.axis_size("narrow")
    point_total = point_cell.shape[0]
    bricks = neighbours.shape[2]
    table = neighbours.reshape(bricks * 27)

    owner = point_owner[:, 0]
    slots = jnp.arange(point_total, dtype=jnp.int32)
    is_live = slots < strip_count[0]
    code = jnp.where(is_live, point_cell + 1, 0).astype(jnp.float32)
    owner_hot = (owner[:, None] == jnp.arange(owners, dtype=jnp.int32)[None, :]).astype(jnp.bfloat16)
    earlier = (slots[None, :] < slots[:, None]).astype(jnp.bfloat16)
    before = jnp.dot(earlier, owner_hot, preferred_element_type=jnp.float32)
    rank = jnp.sum(before * owner_hot.astype(jnp.float32), axis=1).astype(jnp.int32)
    dest = owner * CAP + rank
    payload = jnp.concatenate([code[:, None], normals.T], axis=1)
    place_hot = (jnp.arange(owners * CAP, dtype=jnp.int32)[:, None] == dest[None, :]).astype(jnp.float32)
    send = jnp.dot(place_hot, payload, precision=HIGHEST, preferred_element_type=jnp.float32)
    got = lax.all_to_all(send.reshape(owners, CAP, 4), "wide", 0, 0, tiled=True).reshape(owners * CAP, 4)

    cell = got[:, 0].astype(jnp.int32) - 1
    brick_x = cell >> 8
    cell_yz = cell & (LANES - 1)
    bx_hot = (brick_x[:, None] == jnp.arange(bricks * ROWS, dtype=jnp.int32)[None, :]).astype(jnp.float32)
    yz_hot = (cell_yz[:, None] == jnp.arange(LANES, dtype=jnp.int32)[None, :]).astype(jnp.float32)
    weighted = jnp.concatenate([bx_hot * got[:, 1:2], bx_hot * got[:, 2:3], bx_hot * got[:, 3:4], bx_hot], axis=1)
    splatted = jnp.einsum("pa,pb->ab", weighted, yz_hot, precision=HIGHEST, preferred_element_type=jnp.float32)
    splatted = splatted.reshape(4, bricks, ROWS, LANES)
    vector_field = splatted[:3]
    diagonal = 14.5 + 2.0 * splatted[3]

    shape = (bricks, ROWS, LANES)
    right_side = _local_call(_divergence_kernel, shape, [table, halo(vector_field)], 20 * bricks * 4096)

    basis = [right_side]
    kernel = functools.partial(_stencil_kernel, shift=SHIFT, scale=1.0 / SPAN)
    for k in range(ITERS):
        image = _local_call(kernel, shape, [table, halo(basis[-1]), diagonal], 60 * bricks * 4096)
        basis.append(image if k == 0 else 2.0 * image - basis[-2])
    lift = [[0.0] * ITERS for _ in range(ITERS + 1)]
    for k in range(ITERS):
        lift[k][k] = SHIFT
        if k == 0:
            lift[1][0] = SPAN
        else:
            lift[k - 1][k] = lift[k + 1][k] = 0.5 * SPAN
    vmem = pl.BlockSpec(memory_space=pltpu.VMEM)
    stacked = jnp.stack(basis).reshape(ITERS + 1, bricks * ROWS, LANES)
    partial_sums = pl.pallas_call(
        _gram_kernel, out_shape=jax.ShapeDtypeStruct((8, 128), jnp.float32), in_specs=[vmem], out_specs=vmem
    )(stacked)
    payload = partial_sums[0:2, 0:16].reshape(1, 32)
    gathered = lax.all_to_all(jnp.broadcast_to(payload, (devices, 32)), ("wide", "narrow"), 0, 0, tiled=True)
    flat = jax.ShapeDtypeStruct((bricks * ROWS, LANES), jnp.float32)
    solution, residual = pl.pallas_call(
        functools.partial(_galerkin_kernel, lift=lift),
        out_shape=(flat, flat),
        in_specs=[vmem, vmem],
        out_specs=(vmem, vmem),
    )(jnp.pad(gathered.T, ((0, 0), (0, max(0, 128 - devices)))), stacked)
    out = (1, 1, bricks, ROWS * LANES)
    return solution.reshape(out), residual.reshape(out)


def solution(mesh):
    return jax.shard_map(
        shards,
        mesh=mesh,
        in_specs=(
            P(("wide", "narrow"), None),
            P(("wide", "narrow")),
            P(None, ("wide", "narrow")),
            P(("wide", "narrow")),
            P("wide", "narrow", None, None),
        ),
        out_specs=(P("wide", "narrow", None, None), P("wide", "narrow", None, None)),
        check_vma=False,
    )
```

```python
import functools
import math

import jax
import jax.numpy as jnp
from jax import lax
from jax.experimental import pallas as pl
from jax.experimental.pallas import tpu as pltpu
from jax.sharding import PartitionSpec as P

ITERS = 3
CAP = 32
HIGHEST = lax.Precision.HIGHEST
ROWS, LANES = 16, 256
SHIFT, SPAN = 8.0, 8.0


def _solve(matrix, rhs):
    n = len(rhs)
    m = [list(r) + [v] for r, v in zip(matrix, rhs)]
    for k in range(n):
        for i in range(k + 1, n):
            f = m[i][k] / m[k][k]
            m[i] = [m[i][j] - f * m[k][j] if j > k else m[i][j] for j in range(n + 1)]
    x = [None] * n
    for i in reversed(range(n)):
        acc = m[i][n]
        for j in range(i + 1, n):
            acc = acc - m[i][j] * x[j]
        x[i] = acc / m[i][i]
    return x


def _two_sum(a, b):
    total = a + b
    part = total - a
    return total, (a - (total - part)) + (b - part)


def _split(a):
    scaled = a * 4097.0
    high = scaled - (scaled - a)
    return high, a - high


def _two_prod(a, b):
    product = a * b
    ah, al = _split(a)
    bh, bl = _split(b)
    return product, ((ah * bh - product) + ah * bl + al * bh) + al * bl


def _halve(s, e, axis, stop):
    while s.shape[axis] > stop:
        h = s.shape[axis] // 2
        first = lax.slice_in_dim(s, 0, h, axis=axis)
        second = lax.slice_in_dim(s, h, 2 * h, axis=axis)
        s, err = _two_sum(first, second)
        e = lax.slice_in_dim(e, 0, h, axis=axis) + lax.slice_in_dim(e, h, 2 * h, axis=axis) + err
    return s, e


def _spread(s, e, axis):
    k = s.shape[axis] // 2
    while k >= 1:
        s, err = _two_sum(s, pltpu.roll(s, k, axis))
        e = e + pltpu.roll(e, k, axis) + err
        k //= 2
    return s, e


def _dd_add(x, y):
    s, e = _two_sum(x[0], y[0])
    return _two_sum(s, e + (x[1] + y[1]))


def _rows(ref):
    return jnp.concatenate([ref[b] for b in range(ref.shape[0])], axis=0)


def _gram_kernel(*refs):
    basis_ref, out_ref = refs[:-1], refs[-1]
    row = lax.broadcasted_iota(jnp.int32, out_ref.shape, 0)
    lane = lax.broadcasted_iota(jnp.int32, out_ref.shape, 1)
    count = len(basis_ref)
    acc = jnp.zeros(out_ref.shape, jnp.float32)
    k = 0
    for i in range(count):
        for j in range(i, count):
            s, e = _two_prod(_rows(basis_ref[i]), _rows(basis_ref[j]))
            s, e = _halve(s, e, 0, 8)
            s, e = _halve(s, e, 1, 128)
            s, e = _spread(s, e, 0)
            s, e = _spread(s, e, 1)
            high, low = _two_sum(s, e)
            acc = jnp.where((row == 0) & (lane == k), high, acc)
            acc = jnp.where((row == 1) & (lane == k), low, acc)
            k += 1
    out_ref[...] = acc


def _galerkin_kernel(parts_ref, *refs, lift=None):
    basis_ref, (solution_ref, residual_ref) = refs[:-2], refs[-2:]
    half = parts_ref.shape[0] // 2
    s, e = _halve(parts_ref[0:half, :], parts_ref[half:, :], 1, 128)
    s, e = _spread(s, e, 1)
    high, low = _two_sum(s, e)
    rows = lax.broadcasted_iota(jnp.int32, high.shape, 0)

    def pick(values, k):
        return jnp.sum(jnp.where(rows == k, values, 0.0), axis=0, keepdims=True)

    size = len(lift)
    pairs = [(i, j) for i in range(size) for j in range(i, size)]
    gram = {}
    for k, (i, j) in enumerate(pairs):
        gram[i, j] = gram[j, i] = (pick(high, k), pick(low, k))
    n = size - 1
    matrix = [[None] * n for _ in range(n)]
    for i in range(n):
        for j in range(n):
            entry = None
            for k in range(size):
                if lift[k][j] != 0.0:
                    term = (lift[k][j] * gram[i, k][0], lift[k][j] * gram[i, k][1])
                    entry = term if entry is None else _dd_add(entry, term)
            matrix[i][j] = entry
    wanted = [gram[i, 0] for i in range(n)]
    top = [[matrix[i][j][0] for j in range(n)] for i in range(n)]
    coeff = _solve(top, [w[0] for w in wanted])
    misfit = []
    for i in range(n):
        acc = wanted[i]
        for j in range(n):
            p, pe = _two_prod(matrix[i][j][0], coeff[j])
            acc = _dd_add(acc, (-p, -(pe + matrix[i][j][1] * coeff[j])))
        misfit.append(acc[0] + acc[1])
    coeff = [c + d for c, d in zip(coeff, _solve(top, misfit))]
    weights = []
    for k in range(size):
        terms = [lift[k][j] * coeff[j] for j in range(n) if lift[k][j] != 0.0]
        weights.append((1.0 if k == 0 else 0.0) - sum(terms[1:], terms[0]))
    blocks = [_rows(r) for r in basis_ref]
    shape = blocks[0].shape

    def wide(v):
        v = jnp.broadcast_to(v, (shape[0], v.shape[1]))
        return jnp.concatenate([v] * (shape[1] // v.shape[1]), axis=1)

    def store(out_ref, total):
        for r in range(shape[0]):
            b, x = divmod(r, ROWS)
            out_ref[pl.ds(b, 1), pl.ds(x * LANES, LANES)] = total[r : r + 1, :]

    total = wide(coeff[0]) * blocks[0]
    for j in range(1, n):
        total = total + wide(coeff[j]) * blocks[j]
    store(solution_ref, total)
    total = wide(weights[0]) * blocks[0]
    for k in range(1, size):
        total = total + wide(weights[k]) * blocks[k]
    store(residual_ref, total)


def _masks():
    shape = (ROWS, LANES)
    lane = lax.broadcasted_iota(jnp.int32, shape, 1)
    row = lax.broadcasted_iota(jnp.int32, shape, 0)
    return row, lane >> 4, lane & 15


def _neighbour_x(c, m, p, row):
    lo = jnp.where(row == 0, pltpu.roll(m, 1, 0), pltpu.roll(c, 1, 0))
    hi = jnp.where(row == ROWS - 1, pltpu.roll(p, ROWS - 1, 0), pltpu.roll(c, ROWS - 1, 0))
    return lo, hi


def _neighbour_y(c, m, p, y):
    lo = jnp.where(y == 0, pltpu.roll(m, 16, 1), pltpu.roll(c, 16, 1))
    hi = jnp.where(y == 15, pltpu.roll(p, LANES - 16, 1), pltpu.roll(c, LANES - 16, 1))
    return lo, hi


def _neighbour_z(c, m, p, z):
    lo = jnp.where(z == 0, pltpu.roll(m, LANES - 15, 1), pltpu.roll(c, 1, 1))
    hi = jnp.where(z == 15, pltpu.roll(p, 15, 1), pltpu.roll(c, LANES - 1, 1))
    return lo, hi


def _column(ex, ey, ez):
    return (ex + 1) * 9 + (ey + 1) * 3 + (ez + 1)


def _stencil_kernel(tab_ref, src_ref, diag_ref, out_ref, shift=0.0, scale=1.0):
    row, y, z = _masks()
    bricks = out_ref.shape[0]
    for b in range(bricks):
        own = src_ref[4 * bricks + b]

        def brick(ex, ey, ez):
            if ex == 0 and ey == 0 and ez == 0:
                return own
            return src_ref[tab_ref[b * 27 + _column(ex, ey, ez)]]

        planes = {}
        for ex in (-1, 0, 1):
            lines = {}
            for ey in (-1, 0, 1):
                c = brick(ex, ey, 0)
                lo, hi = _neighbour_z(c, brick(ex, ey, -1), brick(ex, ey, 1), z)
                lines[ey] = c + 0.5 * (lo + hi)
            lo, hi = _neighbour_y(lines[0], lines[-1], lines[1], y)
            planes[ex] = lines[0] + 0.5 * (lo + hi)
        lo, hi = _neighbour_x(planes[0], planes[-1], planes[1], row)
        smoothed = planes[0] + 0.5 * (lo + hi)
        out_ref[b] = ((diag_ref[b] + (2.0 - shift)) * own - 2.0 * smoothed) * scale


def _divergence_kernel(tab_ref, src_ref, out_ref):
    row, y, z = _masks()
    bricks = out_ref.shape[0]
    for b in range(bricks):

        def brick(k, ex, ey, ez):
            if ex == 0 and ey == 0 and ez == 0:
                return src_ref[k, 4 * bricks + b]
            return src_ref[k, tab_ref[b * 27 + _column(ex, ey, ez)]]

        lo, hi = _neighbour_x(brick(0, 0, 0, 0), brick(0, -1, 0, 0), brick(0, 1, 0, 0), row)
        change_x = hi - lo
        lo, hi = _neighbour_y(brick(1, 0, 0, 0), brick(1, 0, -1, 0), brick(1, 0, 1, 0), y)
        change_y = hi - lo
        lo, hi = _neighbour_z(brick(2, 0, 0, 0), brick(2, 0, 0, -1), brick(2, 0, 0, 1), z)
        change_z = hi - lo
        out_ref[b] = -4.0 * ((change_x + change_y) + change_z)


def _local_call(kernel, out_shape, operands, flops):
    spaces = [pltpu.SMEM] + [pltpu.VMEM] * (len(operands) - 1)
    moved = sum(int(a.size) * 4 for a in operands) + math.prod(out_shape) * 4
    return pl.pallas_call(
        kernel,
        out_shape=jax.ShapeDtypeStruct(out_shape, jnp.float32),
        in_specs=[pl.BlockSpec(memory_space=s) for s in spaces],
        out_specs=pl.BlockSpec(memory_space=pltpu.VMEM),
        cost_estimate=pl.CostEstimate(flops=flops, bytes_accessed=moved, transcendentals=0),
    )(*operands)


def _shift(field, axis, step):
    size = lax.axis_size(axis)
    pairs = [(i + step, i) for i in range(size) if 0 <= i + step < size]
    return lax.ppermute(field, axis, pairs)


def halo(field):
    lead, bricks = field.shape[:-3], field.shape[-3]
    column = jnp.stack([_shift(field, "wide", -1), field, _shift(field, "wide", 1)], axis=-4)
    block = jnp.stack([_shift(column, "narrow", -1), column, _shift(column, "narrow", 1)], axis=-4)
    block = block.reshape(lead + (9 * bricks,) + field.shape[-2:])
    zero = jnp.zeros(lead + (1,) + field.shape[-2:], field.dtype)
    return jnp.concatenate([block, zero], axis=-3)


def shards(point_owner, point_cell, normals, strip_count, neighbours):
    owners = lax.axis_size("wide")
    devices = owners * lax.axis_size("narrow")
    point_total = point_cell.shape[0]
    bricks = neighbours.shape[2]
    table = neighbours.reshape(bricks * 27)

    owner = point_owner[:, 0]
    slots = jnp.arange(point_total, dtype=jnp.int32)
    is_live = slots < strip_count[0]
    code = jnp.where(is_live, point_cell + 1, 0).astype(jnp.float32)
    owner_hot = (owner[:, None] == jnp.arange(owners, dtype=jnp.int32)[None, :]).astype(jnp.bfloat16)
    earlier = (slots[None, :] < slots[:, None]).astype(jnp.bfloat16)
    before = jnp.dot(earlier, owner_hot, preferred_element_type=jnp.float32)
    rank = jnp.sum(before * owner_hot.astype(jnp.float32), axis=1).astype(jnp.int32)
    dest = owner * CAP + rank
    payload = jnp.concatenate([code[:, None], normals.T], axis=1)
    place_hot = (jnp.arange(owners * CAP, dtype=jnp.int32)[:, None] == dest[None, :]).astype(jnp.float32)
    send = jnp.dot(place_hot, payload, precision=HIGHEST, preferred_element_type=jnp.float32)
    got = lax.all_to_all(send.reshape(owners, CAP, 4), "wide", 0, 0, tiled=True).reshape(owners * CAP, 4)

    cell = got[:, 0].astype(jnp.int32) - 1
    brick_x = cell >> 8
    cell_yz = cell & (LANES - 1)
    bx_hot = (brick_x[:, None] == jnp.arange(bricks * ROWS, dtype=jnp.int32)[None, :]).astype(jnp.float32)
    yz_hot = (cell_yz[:, None] == jnp.arange(LANES, dtype=jnp.int32)[None, :]).astype(jnp.float32)
    weighted = jnp.concatenate([bx_hot * got[:, 1:2], bx_hot * got[:, 2:3], bx_hot * got[:, 3:4], bx_hot], axis=1)
    splatted = jnp.einsum("pa,pb->ab", weighted, yz_hot, precision=HIGHEST, preferred_element_type=jnp.float32)
    splatted = splatted.reshape(4, bricks, ROWS, LANES)
    vector_field = splatted[:3]
    diagonal = 14.5 + 2.0 * splatted[3]

    shape = (bricks, ROWS, LANES)
    right_side = _local_call(_divergence_kernel, shape, [table, halo(vector_field)], 20 * bricks * 4096)

    basis = [right_side]
    kernel = functools.partial(_stencil_kernel, shift=SHIFT, scale=1.0 / SPAN)
    for k in range(ITERS):
        image = _local_call(kernel, shape, [table, halo(basis[-1]), diagonal], 60 * bricks * 4096)
        basis.append(image if k == 0 else 2.0 * image - basis[-2])
    lift = [[0.0] * ITERS for _ in range(ITERS + 1)]
    for k in range(ITERS):
        lift[k][k] = SHIFT
        if k == 0:
            lift[1][0] = SPAN
        else:
            lift[k - 1][k] = lift[k + 1][k] = 0.5 * SPAN
    vmem = pl.BlockSpec(memory_space=pltpu.VMEM)
    partial_sums = pl.pallas_call(
        _gram_kernel, out_shape=jax.ShapeDtypeStruct((8, 128), jnp.float32), in_specs=[vmem] * len(basis), out_specs=vmem
    )(*basis)
    payload = partial_sums[0:2, 0:16].reshape(1, 32)
    gathered = lax.all_to_all(jnp.broadcast_to(payload, (devices, 32)), ("wide", "narrow"), 0, 0, tiled=True)
    flat = jax.ShapeDtypeStruct((bricks, ROWS * LANES), jnp.float32)
    solution, residual = pl.pallas_call(
        functools.partial(_galerkin_kernel, lift=lift),
        out_shape=(flat, flat),
        in_specs=[vmem] * (1 + len(basis)),
        out_specs=(vmem, vmem),
    )(jnp.pad(gathered.T, ((0, 0), (0, max(0, 128 - devices)))), *basis)
    out = (1, 1, bricks, ROWS * LANES)
    return solution.reshape(out), residual.reshape(out)


def solution(mesh):
    return jax.shard_map(
        shards,
        mesh=mesh,
        in_specs=(
            P(("wide", "narrow"), None),
            P(("wide", "narrow")),
            P(None, ("wide", "narrow")),
            P(("wide", "narrow")),
            P("wide", "narrow", None, None),
        ),
        out_specs=(P("wide", "narrow", None, None), P("wide", "narrow", None, None)),
        check_vma=False,
    )
```

```python
import functools
import math

import jax
import jax.numpy as jnp
from jax import lax
from jax.experimental import pallas as pl
from jax.experimental.pallas import tpu as pltpu
from jax.sharding import PartitionSpec as P

ITERS = 3
CAP = 32
HIGHEST = lax.Precision.HIGHEST
ROWS, LANES = 16, 256
SHIFT, SPAN = 8.0, 8.0


def _solve(matrix, rhs):
    n = len(rhs)
    m = [list(r) + [v] for r, v in zip(matrix, rhs)]
    for k in range(n):
        for i in range(k + 1, n):
            f = m[i][k] / m[k][k]
            m[i] = [m[i][j] - f * m[k][j] if j > k else m[i][j] for j in range(n + 1)]
    x = [None] * n
    for i in reversed(range(n)):
        acc = m[i][n]
        for j in range(i + 1, n):
            acc = acc - m[i][j] * x[j]
        x[i] = acc / m[i][i]
    return x


def _two_sum(a, b):
    total = a + b
    part = total - a
    return total, (a - (total - part)) + (b - part)


def _split(a):
    scaled = a * 4097.0
    high = scaled - (scaled - a)
    return high, a - high


def _two_prod(a, b):
    product = a * b
    ah, al = _split(a)
    bh, bl = _split(b)
    return product, ((ah * bh - product) + ah * bl + al * bh) + al * bl


def _halve(s, e, axis, stop):
    while s.shape[axis] > stop:
        h = s.shape[axis] // 2
        first = lax.slice_in_dim(s, 0, h, axis=axis)
        second = lax.slice_in_dim(s, h, 2 * h, axis=axis)
        s, err = _two_sum(first, second)
        e = lax.slice_in_dim(e, 0, h, axis=axis) + lax.slice_in_dim(e, h, 2 * h, axis=axis) + err
    return s, e


def _spread(s, e, axis):
    k = s.shape[axis] // 2
    while k >= 1:
        s, err = _two_sum(s, pltpu.roll(s, k, axis))
        e = e + pltpu.roll(e, k, axis) + err
        k //= 2
    return s, e


def _dd_add(x, y):
    s, e = _two_sum(x[0], y[0])
    return _two_sum(s, e + (x[1] + y[1]))


def _rows(ref):
    return jnp.concatenate([ref[b] for b in range(ref.shape[0])], axis=0)


def _gram_kernel(*refs):
    basis_ref, out_ref = refs[:-1], refs[-1]
    lane = lax.broadcasted_iota(jnp.int32, (1, 128), 1)
    count = len(basis_ref)
    acc = jnp.zeros((1, 128), jnp.float32)
    k = 0
    for i in range(count):
        for j in range(i, count):
            s, e = _two_prod(_rows(basis_ref[i]), _rows(basis_ref[j]))
            s, e = _halve(s, e, 0, 8)
            s, e = _halve(s, e, 1, 128)
            s, e = _spread(s, e, 0)
            s, e = _spread(s, e, 1)
            high, low = _two_sum(s, e)
            acc = jnp.where(lane == k, high[0:1, :], acc)
            acc = jnp.where(lane == 16 + k, low[0:1, :], acc)
            k += 1
    out_ref[...] = acc[:, 0 : out_ref.shape[1]]


def _galerkin_kernel(parts_ref, *refs, lift=None):
    basis_ref, (solution_ref, residual_ref) = refs[:-2], refs[-2:]
    half = parts_ref.shape[0] // 2
    s, e = _halve(parts_ref[0:half, :], parts_ref[half:, :], 1, 128)
    s, e = _spread(s, e, 1)
    high, low = _two_sum(s, e)
    rows = lax.broadcasted_iota(jnp.int32, high.shape, 0)

    def pick(values, k):
        return jnp.sum(jnp.where(rows == k, values, 0.0), axis=0, keepdims=True)

    size = len(lift)
    pairs = [(i, j) for i in range(size) for j in range(i, size)]
    gram = {}
    for k, (i, j) in enumerate(pairs):
        gram[i, j] = gram[j, i] = (pick(high, k), pick(low, k))
    n = size - 1
    matrix = [[None] * n for _ in range(n)]
    for i in range(n):
        for j in range(n):
            entry = None
            for k in range(size):
                if lift[k][j] != 0.0:
                    term = (lift[k][j] * gram[i, k][0], lift[k][j] * gram[i, k][1])
                    entry = term if entry is None else _dd_add(entry, term)
            matrix[i][j] = entry
    wanted = [gram[i, 0] for i in range(n)]
    top = [[matrix[i][j][0] for j in range(n)] for i in range(n)]
    coeff = _solve(top, [w[0] for w in wanted])
    misfit = []
    for i in range(n):
        acc = wanted[i]
        for j in range(n):
            p, pe = _two_prod(matrix[i][j][0], coeff[j])
            acc = _dd_add(acc, (-p, -(pe + matrix[i][j][1] * coeff[j])))
        misfit.append(acc[0] + acc[1])
    coeff = [c + d for c, d in zip(coeff, _solve(top, misfit))]
    weights = []
    for k in range(size):
        terms = [lift[k][j] * coeff[j] for j in range(n) if lift[k][j] != 0.0]
        weights.append((1.0 if k == 0 else 0.0) - sum(terms[1:], terms[0]))
    blocks = [_rows(r) for r in basis_ref]
    shape = blocks[0].shape

    def wide(v):
        v = jnp.broadcast_to(v, (shape[0], v.shape[1]))
        return jnp.concatenate([v] * (shape[1] // v.shape[1]), axis=1)

    def store(out_ref, total):
        for r in range(shape[0]):
            b, x = divmod(r, ROWS)
            out_ref[pl.ds(b, 1), pl.ds(x * LANES, LANES)] = total[r : r + 1, :]

    total = wide(coeff[0]) * blocks[0]
    for j in range(1, n):
        total = total + wide(coeff[j]) * blocks[j]
    store(solution_ref, total)
    total = wide(weights[0]) * blocks[0]
    for k in range(1, size):
        total = total + wide(weights[k]) * blocks[k]
    store(residual_ref, total)


def _masks():
    shape = (ROWS, LANES)
    lane = lax.broadcasted_iota(jnp.int32, shape, 1)
    row = lax.broadcasted_iota(jnp.int32, shape, 0)
    return row, lane >> 4, lane & 15


def _neighbour_x(c, m, p, row):
    lo = jnp.where(row == 0, pltpu.roll(m, 1, 0), pltpu.roll(c, 1, 0))
    hi = jnp.where(row == ROWS - 1, pltpu.roll(p, ROWS - 1, 0), pltpu.roll(c, ROWS - 1, 0))
    return lo, hi


def _neighbour_y(c, m, p, y):
    lo = jnp.where(y == 0, pltpu.roll(m, 16, 1), pltpu.roll(c, 16, 1))
    hi = jnp.where(y == 15, pltpu.roll(p, LANES - 16, 1), pltpu.roll(c, LANES - 16, 1))
    return lo, hi


def _neighbour_z(c, m, p, z):
    lo = jnp.where(z == 0, pltpu.roll(m, LANES - 15, 1), pltpu.roll(c, 1, 1))
    hi = jnp.where(z == 15, pltpu.roll(p, 15, 1), pltpu.roll(c, LANES - 1, 1))
    return lo, hi


def _column(ex, ey, ez):
    return (ex + 1) * 9 + (ey + 1) * 3 + (ez + 1)


def _stencil_kernel(tab_ref, src_ref, diag_ref, *rest, shift=0.0, scale=1.0):
    previous, out_ref = rest[:-1], rest[-1]
    row, y, z = _masks()
    bricks = out_ref.shape[0]
    for b in range(bricks):
        own = src_ref[4 * bricks + b]

        def brick(ex, ey, ez):
            if ex == 0 and ey == 0 and ez == 0:
                return own
            return src_ref[tab_ref[b * 27 + _column(ex, ey, ez)]]

        planes = {}
        for ex in (-1, 0, 1):
            lines = {}
            for ey in (-1, 0, 1):
                c = brick(ex, ey, 0)
                lo, hi = _neighbour_z(c, brick(ex, ey, -1), brick(ex, ey, 1), z)
                lines[ey] = c + 0.5 * (lo + hi)
            lo, hi = _neighbour_y(lines[0], lines[-1], lines[1], y)
            planes[ex] = lines[0] + 0.5 * (lo + hi)
        lo, hi = _neighbour_x(planes[0], planes[-1], planes[1], row)
        smoothed = planes[0] + 0.5 * (lo + hi)
        image = ((diag_ref[b] + (2.0 - shift)) * own - 2.0 * smoothed) * scale
        out_ref[b] = 2.0 * image - previous[0][b] if previous else image


def _divergence_kernel(tab_ref, src_ref, out_ref):
    row, y, z = _masks()
    bricks = out_ref.shape[0]
    for b in range(bricks):

        def brick(k, ex, ey, ez):
            if ex == 0 and ey == 0 and ez == 0:
                return src_ref[k, 4 * bricks + b]
            return src_ref[k, tab_ref[b * 27 + _column(ex, ey, ez)]]

        lo, hi = _neighbour_x(brick(0, 0, 0, 0), brick(0, -1, 0, 0), brick(0, 1, 0, 0), row)
        change_x = hi - lo
        lo, hi = _neighbour_y(brick(1, 0, 0, 0), brick(1, 0, -1, 0), brick(1, 0, 1, 0), y)
        change_y = hi - lo
        lo, hi = _neighbour_z(brick(2, 0, 0, 0), brick(2, 0, 0, -1), brick(2, 0, 0, 1), z)
        change_z = hi - lo
        out_ref[b] = -4.0 * ((change_x + change_y) + change_z)


def _local_call(kernel, out_shape, operands, flops):
    spaces = [pltpu.SMEM] + [pltpu.VMEM] * (len(operands) - 1)
    moved = sum(int(a.size) * 4 for a in operands) + math.prod(out_shape) * 4
    return pl.pallas_call(
        kernel,
        out_shape=jax.ShapeDtypeStruct(out_shape, jnp.float32),
        in_specs=[pl.BlockSpec(memory_space=s) for s in spaces],
        out_specs=pl.BlockSpec(memory_space=pltpu.VMEM),
        cost_estimate=pl.CostEstimate(flops=flops, bytes_accessed=moved, transcendentals=0),
    )(*operands)


def _shift(field, axis, step):
    size = lax.axis_size(axis)
    pairs = [(i + step, i) for i in range(size) if 0 <= i + step < size]
    return lax.ppermute(field, axis, pairs)


def halo(field):
    lead, bricks = field.shape[:-3], field.shape[-3]
    column = jnp.stack([_shift(field, "wide", -1), field, _shift(field, "wide", 1)], axis=-4)
    block = jnp.stack([_shift(column, "narrow", -1), column, _shift(column, "narrow", 1)], axis=-4)
    block = block.reshape(lead + (9 * bricks,) + field.shape[-2:])
    zero = jnp.zeros(lead + (1,) + field.shape[-2:], field.dtype)
    return jnp.concatenate([block, zero], axis=-3)


def shards(point_owner, point_cell, normals, strip_count, neighbours):
    owners = lax.axis_size("wide")
    devices = owners * lax.axis_size("narrow")
    point_total = point_cell.shape[0]
    bricks = neighbours.shape[2]
    table = neighbours.reshape(bricks * 27)

    owner = point_owner[:, 0]
    slots = jnp.arange(point_total, dtype=jnp.int32)
    is_live = slots < strip_count[0]
    code = jnp.where(is_live, point_cell + 1, 0).astype(jnp.float32)
    owner_hot = (owner[:, None] == jnp.arange(owners, dtype=jnp.int32)[None, :]).astype(jnp.bfloat16)
    earlier = (slots[None, :] < slots[:, None]).astype(jnp.bfloat16)
    before = jnp.dot(earlier, owner_hot, preferred_element_type=jnp.float32)
    rank = jnp.sum(before * owner_hot.astype(jnp.float32), axis=1).astype(jnp.int32)
    dest = owner * CAP + rank
    payload = jnp.concatenate([code[:, None], normals.T], axis=1)
    place_hot = (jnp.arange(owners * CAP, dtype=jnp.int32)[:, None] == dest[None, :]).astype(jnp.float32)
    send = jnp.dot(place_hot, payload, precision=HIGHEST, preferred_element_type=jnp.float32)
    got = lax.all_to_all(send.reshape(owners, CAP, 4), "wide", 0, 0, tiled=True).reshape(owners * CAP, 4)

    cell = got[:, 0].astype(jnp.int32) - 1
    brick_x = cell >> 8
    cell_yz = cell & (LANES - 1)
    bx_hot = (brick_x[:, None] == jnp.arange(bricks * ROWS, dtype=jnp.int32)[None, :]).astype(jnp.float32)
    yz_hot = (cell_yz[:, None] == jnp.arange(LANES, dtype=jnp.int32)[None, :]).astype(jnp.float32)
    weighted = jnp.concatenate([bx_hot * got[:, 1:2], bx_hot * got[:, 2:3], bx_hot * got[:, 3:4], bx_hot], axis=1)
    splatted = jnp.einsum("pa,pb->ab", weighted, yz_hot, precision=HIGHEST, preferred_element_type=jnp.float32)
    splatted = splatted.reshape(4, bricks, ROWS, LANES)
    vector_field = splatted[:3]
    diagonal = 14.5 + 2.0 * splatted[3]

    shape = (bricks, ROWS, LANES)
    right_side = _local_call(_divergence_kernel, shape, [table, halo(vector_field)], 20 * bricks * 4096)

    basis = [right_side]
    kernel = functools.partial(_stencil_kernel, shift=SHIFT, scale=1.0 / SPAN)
    for k in range(ITERS):
        operands = [table, halo(basis[-1]), diagonal] + ([basis[-2]] if k > 0 else [])
        basis.append(_local_call(kernel, shape, operands, 60 * bricks * 4096))
    lift = [[0.0] * ITERS for _ in range(ITERS + 1)]
    for k in range(ITERS):
        lift[k][k] = SHIFT
        if k == 0:
            lift[1][0] = SPAN
        else:
            lift[k - 1][k] = lift[k + 1][k] = 0.5 * SPAN
    vmem = pl.BlockSpec(memory_space=pltpu.VMEM)
    payload = pl.pallas_call(
        _gram_kernel, out_shape=jax.ShapeDtypeStruct((1, 32), jnp.float32), in_specs=[vmem] * len(basis), out_specs=vmem
    )(*basis)
    gathered = lax.all_to_all(jnp.broadcast_to(payload, (devices, 32)), ("wide", "narrow"), 0, 0, tiled=True)
    flat = jax.ShapeDtypeStruct((bricks, ROWS * LANES), jnp.float32)
    solution, residual = pl.pallas_call(
        functools.partial(_galerkin_kernel, lift=lift),
        out_shape=(flat, flat),
        in_specs=[vmem] * (1 + len(basis)),
        out_specs=(vmem, vmem),
    )(jnp.pad(gathered.T, ((0, 0), (0, max(0, 128 - devices)))), *basis)
    out = (1, 1, bricks, ROWS * LANES)
    return solution.reshape(out), residual.reshape(out)


def solution(mesh):
    return jax.shard_map(
        shards,
        mesh=mesh,
        in_specs=(
            P(("wide", "narrow"), None),
            P(("wide", "narrow")),
            P(None, ("wide", "narrow")),
            P(("wide", "narrow")),
            P("wide", "narrow", None, None),
        ),
        out_specs=(P("wide", "narrow", None, None), P("wide", "narrow", None, None)),
        check_vma=False,
    )
```

```python
import functools
import math

import jax
import jax.numpy as jnp
from jax import lax
from jax.experimental import pallas as pl
from jax.experimental.pallas import tpu as pltpu
from jax.sharding import PartitionSpec as P

ITERS = 3
CAP = 32
HIGHEST = lax.Precision.HIGHEST
ROWS, LANES = 16, 256
SHIFT, SPAN = 8.0, 8.0


def _solve(matrix, rhs):
    n = len(rhs)
    m = [list(r) + [v] for r, v in zip(matrix, rhs)]
    for k in range(n):
        for i in range(k + 1, n):
            f = m[i][k] / m[k][k]
            m[i] = [m[i][j] - f * m[k][j] if j > k else m[i][j] for j in range(n + 1)]
    x = [None] * n
    for i in reversed(range(n)):
        acc = m[i][n]
        for j in range(i + 1, n):
            acc = acc - m[i][j] * x[j]
        x[i] = acc / m[i][i]
    return x


def _two_sum(a, b):
    total = a + b
    part = total - a
    return total, (a - (total - part)) + (b - part)


def _split(a):
    scaled = a * 4097.0
    high = scaled - (scaled - a)
    return high, a - high


def _two_prod(a, b):
    product = a * b
    ah, al = _split(a)
    bh, bl = _split(b)
    return product, ((ah * bh - product) + ah * bl + al * bh) + al * bl


def _halve(s, e, axis, stop):
    while s.shape[axis] > stop:
        h = s.shape[axis] // 2
        first = lax.slice_in_dim(s, 0, h, axis=axis)
        second = lax.slice_in_dim(s, h, 2 * h, axis=axis)
        s, err = _two_sum(first, second)
        e = lax.slice_in_dim(e, 0, h, axis=axis) + lax.slice_in_dim(e, h, 2 * h, axis=axis) + err
    return s, e


def _spread(s, e, axis):
    k = s.shape[axis] // 2
    while k >= 1:
        s, err = _two_sum(s, pltpu.roll(s, k, axis))
        e = e + pltpu.roll(e, k, axis) + err
        k //= 2
    return s, e


def _dd_add(x, y):
    s, e = _two_sum(x[0], y[0])
    return _two_sum(s, e + (x[1] + y[1]))


def _rows(ref):
    return jnp.concatenate([ref[b] for b in range(ref.shape[0])], axis=0)


def _gram_kernel(*refs):
    basis_ref, out_ref = refs[:-1], refs[-1]
    lane = lax.broadcasted_iota(jnp.int32, (1, 128), 1)
    count = len(basis_ref)
    acc = jnp.zeros((1, 128), jnp.float32)
    k = 0
    for i in range(count):
        for j in range(i, count):
            s, e = _two_prod(_rows(basis_ref[i]), _rows(basis_ref[j]))
            s, e = _halve(s, e, 0, 8)
            s, e = _halve(s, e, 1, 128)
            s, e = _spread(s, e, 0)
            s, e = _spread(s, e, 1)
            high, low = _two_sum(s, e)
            acc = jnp.where(lane == k, high[0:1, :], acc)
            acc = jnp.where(lane == 16 + k, low[0:1, :], acc)
            k += 1
    out_ref[...] = acc[:, 0 : out_ref.shape[1]]


def _galerkin_kernel(parts_ref, *refs, lift=None):
    basis_ref, (solution_ref, residual_ref) = refs[:-2], refs[-2:]
    half = parts_ref.shape[0] // 2
    s, e = _halve(parts_ref[0:half, :], parts_ref[half:, :], 1, 128)
    s, e = _spread(s, e, 1)
    high, low = _two_sum(s, e)
    rows = lax.broadcasted_iota(jnp.int32, high.shape, 0)

    def pick(values, k):
        return jnp.sum(jnp.where(rows == k, values, 0.0), axis=0, keepdims=True)

    size = len(lift)
    pairs = [(i, j) for i in range(size) for j in range(i, size)]
    gram = {}
    for k, (i, j) in enumerate(pairs):
        gram[i, j] = gram[j, i] = (pick(high, k), pick(low, k))
    n = size - 1
    matrix = [[None] * n for _ in range(n)]
    for i in range(n):
        for j in range(n):
            entry = None
            for k in range(size):
                if lift[k][j] != 0.0:
                    term = (lift[k][j] * gram[i, k][0], lift[k][j] * gram[i, k][1])
                    entry = term if entry is None else _dd_add(entry, term)
            matrix[i][j] = entry
    wanted = [gram[i, 0] for i in range(n)]
    top = [[matrix[i][j][0] for j in range(n)] for i in range(n)]
    coeff = _solve(top, [w[0] for w in wanted])
    misfit = []
    for i in range(n):
        acc = wanted[i]
        for j in range(n):
            p, pe = _two_prod(matrix[i][j][0], coeff[j])
            acc = _dd_add(acc, (-p, -(pe + matrix[i][j][1] * coeff[j])))
        misfit.append(acc[0] + acc[1])
    coeff = [c + d for c, d in zip(coeff, _solve(top, misfit))]
    weights = []
    for k in range(size):
        terms = [lift[k][j] * coeff[j] for j in range(n) if lift[k][j] != 0.0]
        weights.append((1.0 if k == 0 else 0.0) - sum(terms[1:], terms[0]))
    blocks = [_rows(r) for r in basis_ref]
    shape = blocks[0].shape

    def wide(v):
        v = jnp.broadcast_to(v, (shape[0], v.shape[1]))
        return jnp.concatenate([v] * (shape[1] // v.shape[1]), axis=1)

    def store(out_ref, total):
        for r in range(shape[0]):
            b, x = divmod(r, ROWS)
            out_ref[pl.ds(b, 1), pl.ds(x * LANES, LANES)] = total[r : r + 1, :]

    total = wide(coeff[0]) * blocks[0]
    for j in range(1, n):
        total = total + wide(coeff[j]) * blocks[j]
    store(solution_ref, total)
    total = wide(weights[0]) * blocks[0]
    for k in range(1, size):
        total = total + wide(weights[k]) * blocks[k]
    store(residual_ref, total)


def _masks():
    shape = (ROWS, LANES)
    lane = lax.broadcasted_iota(jnp.int32, shape, 1)
    row = lax.broadcasted_iota(jnp.int32, shape, 0)
    return row, lane >> 4, lane & 15


def _neighbour_x(c, m, p, row):
    lo = jnp.where(row == 0, pltpu.roll(m, 1, 0), pltpu.roll(c, 1, 0))
    hi = jnp.where(row == ROWS - 1, pltpu.roll(p, ROWS - 1, 0), pltpu.roll(c, ROWS - 1, 0))
    return lo, hi


def _neighbour_y(c, m, p, y):
    lo = jnp.where(y == 0, pltpu.roll(m, 16, 1), pltpu.roll(c, 16, 1))
    hi = jnp.where(y == 15, pltpu.roll(p, LANES - 16, 1), pltpu.roll(c, LANES - 16, 1))
    return lo, hi


def _neighbour_z(c, m, p, z):
    lo = jnp.where(z == 0, pltpu.roll(m, LANES - 15, 1), pltpu.roll(c, 1, 1))
    hi = jnp.where(z == 15, pltpu.roll(p, 15, 1), pltpu.roll(c, LANES - 1, 1))
    return lo, hi


def _column(ex, ey, ez):
    return (ex + 1) * 9 + (ey + 1) * 3 + (ez + 1)


def _stencil_kernel(tab_ref, low_ref, mid_ref, high_ref, diag_ref, *rest, shift=0.0, scale=1.0):
    previous, out_ref = rest[:-1], rest[-1]
    row, y, z = _masks()
    bricks = out_ref.shape[0]
    pieces = (low_ref, mid_ref, high_ref)
    for b in range(bricks):
        own = mid_ref[bricks + b]

        def brick(ex, ey, ez):
            if ex == 0 and ey == 0 and ez == 0:
                return own
            return _lookup(pieces, tab_ref[b * 27 + _column(ex, ey, ez)], bricks)

        planes = {}
        for ex in (-1, 0, 1):
            lines = {}
            for ey in (-1, 0, 1):
                c = brick(ex, ey, 0)
                lo, hi = _neighbour_z(c, brick(ex, ey, -1), brick(ex, ey, 1), z)
                lines[ey] = c + 0.5 * (lo + hi)
            lo, hi = _neighbour_y(lines[0], lines[-1], lines[1], y)
            planes[ex] = lines[0] + 0.5 * (lo + hi)
        lo, hi = _neighbour_x(planes[0], planes[-1], planes[1], row)
        smoothed = planes[0] + 0.5 * (lo + hi)
        image = ((diag_ref[b] + (2.0 - shift)) * own - 2.0 * smoothed) * scale
        out_ref[b] = 2.0 * image - previous[0][b] if previous else image


def _divergence_kernel(tab_ref, low_ref, mid_ref, high_ref, out_ref):
    row, y, z = _masks()
    bricks = out_ref.shape[0]
    pieces = (low_ref, mid_ref, high_ref)
    for b in range(bricks):

        def brick(k, ex, ey, ez):
            if ex == 0 and ey == 0 and ez == 0:
                return mid_ref[k, bricks + b]
            return _lookup(pieces, tab_ref[b * 27 + _column(ex, ey, ez)], bricks, (k,))

        lo, hi = _neighbour_x(brick(0, 0, 0, 0), brick(0, -1, 0, 0), brick(0, 1, 0, 0), row)
        change_x = hi - lo
        lo, hi = _neighbour_y(brick(1, 0, 0, 0), brick(1, 0, -1, 0), brick(1, 0, 1, 0), y)
        change_y = hi - lo
        lo, hi = _neighbour_z(brick(2, 0, 0, 0), brick(2, 0, 0, -1), brick(2, 0, 0, 1), z)
        change_z = hi - lo
        out_ref[b] = -4.0 * ((change_x + change_y) + change_z)


def _local_call(kernel, out_shape, operands, flops):
    spaces = [pltpu.SMEM] + [pltpu.VMEM] * (len(operands) - 1)
    moved = sum(int(a.size) * 4 for a in operands) + math.prod(out_shape) * 4
    return pl.pallas_call(
        kernel,
        out_shape=jax.ShapeDtypeStruct(out_shape, jnp.float32),
        in_specs=[pl.BlockSpec(memory_space=s) for s in spaces],
        out_specs=pl.BlockSpec(memory_space=pltpu.VMEM),
        cost_estimate=pl.CostEstimate(flops=flops, bytes_accessed=moved, transcendentals=0),
    )(*operands)


def _shift(field, axis, step):
    size = lax.axis_size(axis)
    pairs = [(i + step, i) for i in range(size) if 0 <= i + step < size]
    return lax.ppermute(field, axis, pairs)


def halo(field):
    lead, bricks = field.shape[:-3], field.shape[-3]
    column = jnp.stack([_shift(field, "wide", -1), field, _shift(field, "wide", 1)], axis=-4)
    pieces = [_shift(column, "narrow", -1), column, _shift(column, "narrow", 1)]
    return [p.reshape(lead + (3 * bricks,) + field.shape[-2:]) for p in pieces]


def _lookup(pieces, k, bricks, lead=()):
    q = k // bricks
    j = jnp.minimum((q // 3) * bricks + (k - q * bricks), 3 * bricks - 1)
    piece = q % 3
    value = jnp.where(piece == 0, pieces[0][lead + (j,)], jnp.where(piece == 1, pieces[1][lead + (j,)], pieces[2][lead + (j,)]))
    return jnp.where(k >= 9 * bricks, 0.0, value)


def shards(point_owner, point_cell, normals, strip_count, neighbours):
    owners = lax.axis_size("wide")
    devices = owners * lax.axis_size("narrow")
    point_total = point_cell.shape[0]
    bricks = neighbours.shape[2]
    table = neighbours.reshape(bricks * 27)

    owner = point_owner[:, 0]
    slots = jnp.arange(point_total, dtype=jnp.int32)
    is_live = slots < strip_count[0]
    code = jnp.where(is_live, point_cell + 1, 0).astype(jnp.float32)
    owner_hot = (owner[:, None] == jnp.arange(owners, dtype=jnp.int32)[None, :]).astype(jnp.bfloat16)
    earlier = (slots[None, :] < slots[:, None]).astype(jnp.bfloat16)
    before = jnp.dot(earlier, owner_hot, preferred_element_type=jnp.float32)
    rank = jnp.sum(before * owner_hot.astype(jnp.float32), axis=1).astype(jnp.int32)
    dest = owner * CAP + rank
    payload = jnp.concatenate([code[:, None], normals.T], axis=1)
    place_hot = (jnp.arange(owners * CAP, dtype=jnp.int32)[:, None] == dest[None, :]).astype(jnp.float32)
    send = jnp.dot(place_hot, payload, precision=HIGHEST, preferred_element_type=jnp.float32)
    got = lax.all_to_all(send.reshape(owners, CAP, 4), "wide", 0, 0, tiled=True).reshape(owners * CAP, 4)

    cell = got[:, 0].astype(jnp.int32) - 1
    brick_x = cell >> 8
    cell_yz = cell & (LANES - 1)
    bx_hot = (brick_x[:, None] == jnp.arange(bricks * ROWS, dtype=jnp.int32)[None, :]).astype(jnp.float32)
    yz_hot = (cell_yz[:, None] == jnp.arange(LANES, dtype=jnp.int32)[None, :]).astype(jnp.float32)
    weighted = jnp.concatenate([bx_hot * got[:, 1:2], bx_hot * got[:, 2:3], bx_hot * got[:, 3:4], bx_hot], axis=1)
    splatted = jnp.einsum("pa,pb->ab", weighted, yz_hot, precision=HIGHEST, preferred_element_type=jnp.float32)
    splatted = splatted.reshape(4, bricks, ROWS, LANES)
    vector_field = splatted[:3]
    diagonal = 14.5 + 2.0 * splatted[3]

    shape = (bricks, ROWS, LANES)
    right_side = _local_call(_divergence_kernel, shape, [table, *halo(vector_field)], 20 * bricks * 4096)

    basis = [right_side]
    kernel = functools.partial(_stencil_kernel, shift=SHIFT, scale=1.0 / SPAN)
    for k in range(ITERS):
        operands = [table, *halo(basis[-1]), diagonal] + ([basis[-2]] if k > 0 else [])
        basis.append(_local_call(kernel, shape, operands, 60 * bricks * 4096))
    lift = [[0.0] * ITERS for _ in range(ITERS + 1)]
    for k in range(ITERS):
        lift[k][k] = SHIFT
        if k == 0:
            lift[1][0] = SPAN
        else:
            lift[k - 1][k] = lift[k + 1][k] = 0.5 * SPAN
    vmem = pl.BlockSpec(memory_space=pltpu.VMEM)
    payload = pl.pallas_call(
        _gram_kernel, out_shape=jax.ShapeDtypeStruct((1, 32), jnp.float32), in_specs=[vmem] * len(basis), out_specs=vmem
    )(*basis)
    gathered = lax.all_to_all(jnp.broadcast_to(payload, (devices, 32)), ("wide", "narrow"), 0, 0, tiled=True)
    flat = jax.ShapeDtypeStruct((bricks, ROWS * LANES), jnp.float32)
    solution, residual = pl.pallas_call(
        functools.partial(_galerkin_kernel, lift=lift),
        out_shape=(flat, flat),
        in_specs=[vmem] * (1 + len(basis)),
        out_specs=(vmem, vmem),
    )(jnp.pad(gathered.T, ((0, 0), (0, max(0, 128 - devices)))), *basis)
    out = (1, 1, bricks, ROWS * LANES)
    return solution.reshape(out), residual.reshape(out)


def solution(mesh):
    return jax.shard_map(
        shards,
        mesh=mesh,
        in_specs=(
            P(("wide", "narrow"), None),
            P(("wide", "narrow")),
            P(None, ("wide", "narrow")),
            P(("wide", "narrow")),
            P("wide", "narrow", None, None),
        ),
        out_specs=(P("wide", "narrow", None, None), P("wide", "narrow", None, None)),
        check_vma=False,
    )
```

```python
import functools
import math

import jax
import jax.numpy as jnp
from jax import lax
from jax.experimental import pallas as pl
from jax.experimental.pallas import tpu as pltpu
from jax.sharding import PartitionSpec as P

ITERS = 3
CAP = 32
HIGHEST = lax.Precision.HIGHEST
ROWS, LANES = 16, 256
SHIFT, SPAN = 8.0, 8.0


def _solve(matrix, rhs):
    n = len(rhs)
    m = [list(r) + [v] for r, v in zip(matrix, rhs)]
    for k in range(n):
        for i in range(k + 1, n):
            f = m[i][k] / m[k][k]
            m[i] = [m[i][j] - f * m[k][j] if j > k else m[i][j] for j in range(n + 1)]
    x = [None] * n
    for i in reversed(range(n)):
        acc = m[i][n]
        for j in range(i + 1, n):
            acc = acc - m[i][j] * x[j]
        x[i] = acc / m[i][i]
    return x


def _two_sum(a, b):
    total = a + b
    part = total - a
    return total, (a - (total - part)) + (b - part)


def _split(a):
    scaled = a * 4097.0
    high = scaled - (scaled - a)
    return high, a - high


def _two_prod(a, b):
    product = a * b
    ah, al = _split(a)
    bh, bl = _split(b)
    return product, ((ah * bh - product) + ah * bl + al * bh) + al * bl


def _halve(s, e, axis, stop):
    while s.shape[axis] > stop:
        h = s.shape[axis] // 2
        first = lax.slice_in_dim(s, 0, h, axis=axis)
        second = lax.slice_in_dim(s, h, 2 * h, axis=axis)
        s, err = _two_sum(first, second)
        e = lax.slice_in_dim(e, 0, h, axis=axis) + lax.slice_in_dim(e, h, 2 * h, axis=axis) + err
    return s, e


def _spread(s, e, axis):
    k = s.shape[axis] // 2
    while k >= 1:
        s, err = _two_sum(s, pltpu.roll(s, k, axis))
        e = e + pltpu.roll(e, k, axis) + err
        k //= 2
    return s, e


def _dd_add(x, y):
    s, e = _two_sum(x[0], y[0])
    return _two_sum(s, e + (x[1] + y[1]))


def _rows(ref):
    return jnp.concatenate([ref[b] for b in range(ref.shape[0])], axis=0)


def _gram_kernel(*refs):
    basis_ref, out_ref = refs[:-1], refs[-1]
    lane = lax.broadcasted_iota(jnp.int32, (1, 128), 1)
    count = len(basis_ref)
    acc = jnp.zeros((1, 128), jnp.float32)
    k = 0
    for i in range(count):
        for j in range(i, count):
            s, e = _two_prod(_rows(basis_ref[i]), _rows(basis_ref[j]))
            s, e = _halve(s, e, 0, 8)
            s, e = _halve(s, e, 1, 128)
            s, e = _spread(s, e, 0)
            s, e = _spread(s, e, 1)
            high, low = _two_sum(s, e)
            acc = jnp.where(lane == k, high[0:1, :], acc)
            acc = jnp.where(lane == 16 + k, low[0:1, :], acc)
            k += 1
    out_ref[...] = acc[:, 0 : out_ref.shape[1]]


def _galerkin_kernel(parts_ref, *refs, lift=None):
    basis_ref, (solution_ref, residual_ref) = refs[:-2], refs[-2:]
    half = parts_ref.shape[0] // 2
    s, e = _halve(parts_ref[0:half, :], parts_ref[half:, :], 1, 128)
    s, e = _spread(s, e, 1)
    high, low = _two_sum(s, e)
    rows = lax.broadcasted_iota(jnp.int32, high.shape, 0)

    def pick(values, k):
        return jnp.sum(jnp.where(rows == k, values, 0.0), axis=0, keepdims=True)

    size = len(lift)
    pairs = [(i, j) for i in range(size) for j in range(i, size)]
    gram = {}
    for k, (i, j) in enumerate(pairs):
        gram[i, j] = gram[j, i] = (pick(high, k), pick(low, k))
    n = size - 1
    matrix = [[None] * n for _ in range(n)]
    for i in range(n):
        for j in range(n):
            entry = None
            for k in range(size):
                if lift[k][j] != 0.0:
                    term = (lift[k][j] * gram[i, k][0], lift[k][j] * gram[i, k][1])
                    entry = term if entry is None else _dd_add(entry, term)
            matrix[i][j] = entry
    wanted = [gram[i, 0] for i in range(n)]
    top = [[matrix[i][j][0] for j in range(n)] for i in range(n)]
    coeff = _solve(top, [w[0] for w in wanted])
    misfit = []
    for i in range(n):
        acc = wanted[i]
        for j in range(n):
            p, pe = _two_prod(matrix[i][j][0], coeff[j])
            acc = _dd_add(acc, (-p, -(pe + matrix[i][j][1] * coeff[j])))
        misfit.append(acc[0] + acc[1])
    coeff = [c + d for c, d in zip(coeff, _solve(top, misfit))]
    weights = []
    for k in range(size):
        terms = [lift[k][j] * coeff[j] for j in range(n) if lift[k][j] != 0.0]
        weights.append((1.0 if k == 0 else 0.0) - sum(terms[1:], terms[0]))
    blocks = [_rows(r) for r in basis_ref]
    shape = blocks[0].shape

    def wide(v):
        v = jnp.broadcast_to(v, (shape[0], v.shape[1]))
        return jnp.concatenate([v] * (shape[1] // v.shape[1]), axis=1)

    def store(out_ref, total):
        for r in range(shape[0]):
            b, x = divmod(r, ROWS)
            out_ref[pl.ds(b, 1), pl.ds(x * LANES, LANES)] = total[r : r + 1, :]

    total = wide(coeff[0]) * blocks[0]
    for j in range(1, n):
        total = total + wide(coeff[j]) * blocks[j]
    store(solution_ref, total)
    total = wide(weights[0]) * blocks[0]
    for k in range(1, size):
        total = total + wide(weights[k]) * blocks[k]
    store(residual_ref, total)


def _bf16_parts(x):
    high = lax.reduce_precision(x, exponent_bits=8, mantissa_bits=7)
    rest = x - high
    middle = lax.reduce_precision(rest, exponent_bits=8, mantissa_bits=7)
    return [high, middle, rest - middle]


def _exact_rows(hot, values):
    parts = _bf16_parts(values)
    width = values.shape[1]
    stacked = jnp.concatenate(parts, axis=1).astype(jnp.bfloat16)
    picked = jnp.dot(hot, stacked, preferred_element_type=jnp.float32)
    high, middle, low = (picked[:, i * width : (i + 1) * width] for i in range(3))
    return (high + middle) + low


def _masks():
    shape = (ROWS, LANES)
    lane = lax.broadcasted_iota(jnp.int32, shape, 1)
    row = lax.broadcasted_iota(jnp.int32, shape, 0)
    return row, lane >> 4, lane & 15


def _neighbour_x(c, m, p, row):
    lo = jnp.where(row == 0, pltpu.roll(m, 1, 0), pltpu.roll(c, 1, 0))
    hi = jnp.where(row == ROWS - 1, pltpu.roll(p, ROWS - 1, 0), pltpu.roll(c, ROWS - 1, 0))
    return lo, hi


def _neighbour_y(c, m, p, y):
    lo = jnp.where(y == 0, pltpu.roll(m, 16, 1), pltpu.roll(c, 16, 1))
    hi = jnp.where(y == 15, pltpu.roll(p, LANES - 16, 1), pltpu.roll(c, LANES - 16, 1))
    return lo, hi


def _neighbour_z(c, m, p, z):
    lo = jnp.where(z == 0, pltpu.roll(m, LANES - 15, 1), pltpu.roll(c, 1, 1))
    hi = jnp.where(z == 15, pltpu.roll(p, 15, 1), pltpu.roll(c, LANES - 1, 1))
    return lo, hi


def _column(ex, ey, ez):
    return (ex + 1) * 9 + (ey + 1) * 3 + (ez + 1)


def _stencil_kernel(tab_ref, src_ref, diag_ref, *rest, shift=0.0, scale=1.0):
    previous, out_ref = rest[:-1], rest[-1]
    row, y, z = _masks()
    bricks = out_ref.shape[0]
    for b in range(bricks):
        own = src_ref[4 * bricks + b]

        def brick(ex, ey, ez):
            if ex == 0 and ey == 0 and ez == 0:
                return own
            return src_ref[tab_ref[b * 27 + _column(ex, ey, ez)]]

        planes = {}
        for ex in (-1, 0, 1):
            lines = {}
            for ey in (-1, 0, 1):
                c = brick(ex, ey, 0)
                lo, hi = _neighbour_z(c, brick(ex, ey, -1), brick(ex, ey, 1), z)
                lines[ey] = c + 0.5 * (lo + hi)
            lo, hi = _neighbour_y(lines[0], lines[-1], lines[1], y)
            planes[ex] = lines[0] + 0.5 * (lo + hi)
        lo, hi = _neighbour_x(planes[0], planes[-1], planes[1], row)
        smoothed = planes[0] + 0.5 * (lo + hi)
        image = ((diag_ref[b] + (2.0 - shift)) * own - 2.0 * smoothed) * scale
        out_ref[b] = 2.0 * image - previous[0][b] if previous else image


def _divergence_kernel(tab_ref, src_ref, out_ref):
    row, y, z = _masks()
    bricks = out_ref.shape[0]
    for b in range(bricks):

        def brick(k, ex, ey, ez):
            if ex == 0 and ey == 0 and ez == 0:
                return src_ref[k, 4 * bricks + b]
            return src_ref[k, tab_ref[b * 27 + _column(ex, ey, ez)]]

        lo, hi = _neighbour_x(brick(0, 0, 0, 0), brick(0, -1, 0, 0), brick(0, 1, 0, 0), row)
        change_x = hi - lo
        lo, hi = _neighbour_y(brick(1, 0, 0, 0), brick(1, 0, -1, 0), brick(1, 0, 1, 0), y)
        change_y = hi - lo
        lo, hi = _neighbour_z(brick(2, 0, 0, 0), brick(2, 0, 0, -1), brick(2, 0, 0, 1), z)
        change_z = hi - lo
        out_ref[b] = -4.0 * ((change_x + change_y) + change_z)


def _local_call(kernel, out_shape, operands, flops):
    spaces = [pltpu.SMEM] + [pltpu.VMEM] * (len(operands) - 1)
    moved = sum(int(a.size) * 4 for a in operands) + math.prod(out_shape) * 4
    return pl.pallas_call(
        kernel,
        out_shape=jax.ShapeDtypeStruct(out_shape, jnp.float32),
        in_specs=[pl.BlockSpec(memory_space=s) for s in spaces],
        out_specs=pl.BlockSpec(memory_space=pltpu.VMEM),
        cost_estimate=pl.CostEstimate(flops=flops, bytes_accessed=moved, transcendentals=0),
    )(*operands)


def _shift(field, axis, step):
    size = lax.axis_size(axis)
    pairs = [(i + step, i) for i in range(size) if 0 <= i + step < size]
    return lax.ppermute(field, axis, pairs)


def halo(field):
    lead, bricks = field.shape[:-3], field.shape[-3]
    column = jnp.stack([_shift(field, "wide", -1), field, _shift(field, "wide", 1)], axis=-4)
    block = jnp.stack([_shift(column, "narrow", -1), column, _shift(column, "narrow", 1)], axis=-4)
    block = block.reshape(lead + (9 * bricks,) + field.shape[-2:])
    zero = jnp.zeros(lead + (1,) + field.shape[-2:], field.dtype)
    return jnp.concatenate([block, zero], axis=-3)


def shards(point_owner, point_cell, normals, strip_count, neighbours):
    owners = lax.axis_size("wide")
    devices = owners * lax.axis_size("narrow")
    point_total = point_cell.shape[0]
    bricks = neighbours.shape[2]
    table = neighbours.reshape(bricks * 27)

    owner = point_owner[:, 0]
    slots = jnp.arange(point_total, dtype=jnp.int32)
    is_live = slots < strip_count[0]
    code = jnp.where(is_live, point_cell + 1, 0).astype(jnp.float32)
    owner_hot = (owner[:, None] == jnp.arange(owners, dtype=jnp.int32)[None, :]).astype(jnp.bfloat16)
    earlier = (slots[None, :] < slots[:, None]).astype(jnp.bfloat16)
    before = jnp.dot(earlier, owner_hot, preferred_element_type=jnp.float32)
    rank = jnp.sum(before * owner_hot.astype(jnp.float32), axis=1).astype(jnp.int32)
    dest = owner * CAP + rank
    payload = jnp.concatenate([code[:, None], normals.T], axis=1)
    place_hot = (jnp.arange(owners * CAP, dtype=jnp.int32)[:, None] == dest[None, :]).astype(jnp.bfloat16)
    send = _exact_rows(place_hot, payload)
    got = lax.all_to_all(send.reshape(owners, CAP, 4), "wide", 0, 0, tiled=True).reshape(owners * CAP, 4)

    cell = got[:, 0].astype(jnp.int32) - 1
    brick_x = cell >> 8
    cell_yz = cell & (LANES - 1)
    bx_hot = (brick_x[:, None] == jnp.arange(bricks * ROWS, dtype=jnp.int32)[None, :]).astype(jnp.float32)
    yz_hot = (cell_yz[:, None] == jnp.arange(LANES, dtype=jnp.int32)[None, :]).astype(jnp.float32)
    weighted = jnp.concatenate([bx_hot * got[:, 1:2], bx_hot * got[:, 2:3], bx_hot * got[:, 3:4], bx_hot], axis=1)
    splatted = jnp.einsum("pa,pb->ab", weighted, yz_hot, precision=HIGHEST, preferred_element_type=jnp.float32)
    splatted = splatted.reshape(4, bricks, ROWS, LANES)
    vector_field = splatted[:3]
    diagonal = 14.5 + 2.0 * splatted[3]

    shape = (bricks, ROWS, LANES)
    right_side = _local_call(_divergence_kernel, shape, [table, halo(vector_field)], 20 * bricks * 4096)

    basis = [right_side]
    kernel = functools.partial(_stencil_kernel, shift=SHIFT, scale=1.0 / SPAN)
    for k in range(ITERS):
        operands = [table, halo(basis[-1]), diagonal] + ([basis[-2]] if k > 0 else [])
        basis.append(_local_call(kernel, shape, operands, 60 * bricks * 4096))
    lift = [[0.0] * ITERS for _ in range(ITERS + 1)]
    for k in range(ITERS):
        lift[k][k] = SHIFT
        if k == 0:
            lift[1][0] = SPAN
        else:
            lift[k - 1][k] = lift[k + 1][k] = 0.5 * SPAN
    vmem = pl.BlockSpec(memory_space=pltpu.VMEM)
    payload = pl.pallas_call(
        _gram_kernel, out_shape=jax.ShapeDtypeStruct((1, 32), jnp.float32), in_specs=[vmem] * len(basis), out_specs=vmem
    )(*basis)
    gathered = lax.all_to_all(jnp.broadcast_to(payload, (devices, 32)), ("wide", "narrow"), 0, 0, tiled=True)
    flat = jax.ShapeDtypeStruct((bricks, ROWS * LANES), jnp.float32)
    solution, residual = pl.pallas_call(
        functools.partial(_galerkin_kernel, lift=lift),
        out_shape=(flat, flat),
        in_specs=[vmem] * (1 + len(basis)),
        out_specs=(vmem, vmem),
    )(jnp.pad(gathered.T, ((0, 0), (0, max(0, 128 - devices)))), *basis)
    out = (1, 1, bricks, ROWS * LANES)
    return solution.reshape(out), residual.reshape(out)


def solution(mesh):
    return jax.shard_map(
        shards,
        mesh=mesh,
        in_specs=(
            P(("wide", "narrow"), None),
            P(("wide", "narrow")),
            P(None, ("wide", "narrow")),
            P(("wide", "narrow")),
            P("wide", "narrow", None, None),
        ),
        out_specs=(P("wide", "narrow", None, None), P("wide", "narrow", None, None)),
        check_vma=False,
    )
```

```python
import functools
import math

import jax
import jax.numpy as jnp
from jax import lax
from jax.experimental import pallas as pl
from jax.experimental.pallas import tpu as pltpu
from jax.sharding import PartitionSpec as P

ITERS = 3
CAP = 32
HIGHEST = lax.Precision.HIGHEST
ROWS, LANES = 16, 256
SHIFT, SPAN = 8.0, 8.0


def _solve(matrix, rhs):
    n = len(rhs)
    m = [list(r) + [v] for r, v in zip(matrix, rhs)]
    for k in range(n):
        for i in range(k + 1, n):
            f = m[i][k] / m[k][k]
            m[i] = [m[i][j] - f * m[k][j] if j > k else m[i][j] for j in range(n + 1)]
    x = [None] * n
    for i in reversed(range(n)):
        acc = m[i][n]
        for j in range(i + 1, n):
            acc = acc - m[i][j] * x[j]
        x[i] = acc / m[i][i]
    return x


def _two_sum(a, b):
    total = a + b
    part = total - a
    return total, (a - (total - part)) + (b - part)


def _split(a):
    scaled = a * 4097.0
    high = scaled - (scaled - a)
    return high, a - high


def _two_prod(a, b):
    product = a * b
    ah, al = _split(a)
    bh, bl = _split(b)
    return product, ((ah * bh - product) + ah * bl + al * bh) + al * bl


def _halve(s, e, axis, stop):
    while s.shape[axis] > stop:
        h = s.shape[axis] // 2
        first = lax.slice_in_dim(s, 0, h, axis=axis)
        second = lax.slice_in_dim(s, h, 2 * h, axis=axis)
        s, err = _two_sum(first, second)
        e = lax.slice_in_dim(e, 0, h, axis=axis) + lax.slice_in_dim(e, h, 2 * h, axis=axis) + err
    return s, e


def _spread(s, e, axis):
    k = s.shape[axis] // 2
    while k >= 1:
        s, err = _two_sum(s, pltpu.roll(s, k, axis))
        e = e + pltpu.roll(e, k, axis) + err
        k //= 2
    return s, e


def _dd_add(x, y):
    s, e = _two_sum(x[0], y[0])
    return _two_sum(s, e + (x[1] + y[1]))


def _rows(ref):
    return jnp.concatenate([ref[b] for b in range(ref.shape[0])], axis=0)


def _gram_kernel(*refs):
    basis_ref, out_ref = refs[:-1], refs[-1]
    lane = lax.broadcasted_iota(jnp.int32, (1, 128), 1)
    count = len(basis_ref)
    acc = jnp.zeros((1, 128), jnp.float32)
    k = 0
    for i in range(count):
        for j in range(i, count):
            s, e = _two_prod(_rows(basis_ref[i]), _rows(basis_ref[j]))
            s, e = _halve(s, e, 0, 8)
            s, e = _halve(s, e, 1, 128)
            s, e = _spread(s, e, 0)
            s, e = _spread(s, e, 1)
            high, low = _two_sum(s, e)
            acc = jnp.where(lane == k, high[0:1, :], acc)
            acc = jnp.where(lane == 16 + k, low[0:1, :], acc)
            k += 1
    out_ref[...] = acc[:, 0 : out_ref.shape[1]]


def _galerkin_kernel(parts_ref, *refs, lift=None):
    basis_ref, (solution_ref, residual_ref) = refs[:-2], refs[-2:]
    half = parts_ref.shape[0] // 2
    s, e = _halve(parts_ref[0:half, :], parts_ref[half:, :], 1, 128)
    s, e = _spread(s, e, 1)
    high, low = _two_sum(s, e)
    rows = lax.broadcasted_iota(jnp.int32, high.shape, 0)

    def pick(values, k):
        return jnp.sum(jnp.where(rows == k, values, 0.0), axis=0, keepdims=True)

    size = len(lift)
    pairs = [(i, j) for i in range(size) for j in range(i, size)]
    gram = {}
    for k, (i, j) in enumerate(pairs):
        gram[i, j] = gram[j, i] = (pick(high, k), pick(low, k))
    n = size - 1
    matrix = [[None] * n for _ in range(n)]
    for i in range(n):
        for j in range(n):
            entry = None
            for k in range(size):
                if lift[k][j] != 0.0:
                    term = (lift[k][j] * gram[i, k][0], lift[k][j] * gram[i, k][1])
                    entry = term if entry is None else _dd_add(entry, term)
            matrix[i][j] = entry
    wanted = [gram[i, 0] for i in range(n)]
    top = [[matrix[i][j][0] for j in range(n)] for i in range(n)]
    coeff = _solve(top, [w[0] for w in wanted])
    misfit = []
    for i in range(n):
        acc = wanted[i]
        for j in range(n):
            p, pe = _two_prod(matrix[i][j][0], coeff[j])
            acc = _dd_add(acc, (-p, -(pe + matrix[i][j][1] * coeff[j])))
        misfit.append(acc[0] + acc[1])
    coeff = [c + d for c, d in zip(coeff, _solve(top, misfit))]
    weights = []
    for k in range(size):
        terms = [lift[k][j] * coeff[j] for j in range(n) if lift[k][j] != 0.0]
        weights.append((1.0 if k == 0 else 0.0) - sum(terms[1:], terms[0]))
    blocks = [_rows(r) for r in basis_ref]
    shape = blocks[0].shape

    def wide(v):
        v = jnp.broadcast_to(v, (shape[0], v.shape[1]))
        return jnp.concatenate([v] * (shape[1] // v.shape[1]), axis=1)

    def store(out_ref, total):
        for r in range(shape[0]):
            b, x = divmod(r, ROWS)
            out_ref[pl.ds(b, 1), pl.ds(x * LANES, LANES)] = total[r : r + 1, :]

    total = wide(coeff[0]) * blocks[0]
    for j in range(1, n):
        total = total + wide(coeff[j]) * blocks[j]
    store(solution_ref, total)
    total = wide(weights[0]) * blocks[0]
    for k in range(1, size):
        total = total + wide(weights[k]) * blocks[k]
    store(residual_ref, total)


def _bf16_parts(x):
    high = lax.reduce_precision(x, exponent_bits=8, mantissa_bits=7)
    rest = x - high
    middle = lax.reduce_precision(rest, exponent_bits=8, mantissa_bits=7)
    return [high, middle, rest - middle]


def _exact_rows(hot, values):
    parts = _bf16_parts(values)
    width = values.shape[1]
    stacked = jnp.concatenate(parts, axis=1).astype(jnp.bfloat16)
    picked = jnp.dot(hot, stacked, preferred_element_type=jnp.float32)
    high, middle, low = (picked[:, i * width : (i + 1) * width] for i in range(3))
    return (high + middle) + low


def _masks():
    shape = (ROWS, LANES)
    lane = lax.broadcasted_iota(jnp.int32, shape, 1)
    row = lax.broadcasted_iota(jnp.int32, shape, 0)
    return row, lane >> 4, lane & 15


def _neighbour_x(c, m, p, row):
    lo = jnp.where(row == 0, pltpu.roll(m, 1, 0), pltpu.roll(c, 1, 0))
    hi = jnp.where(row == ROWS - 1, pltpu.roll(p, ROWS - 1, 0), pltpu.roll(c, ROWS - 1, 0))
    return lo, hi


def _neighbour_y(c, m, p, y):
    lo = jnp.where(y == 0, pltpu.roll(m, 16, 1), pltpu.roll(c, 16, 1))
    hi = jnp.where(y == 15, pltpu.roll(p, LANES - 16, 1), pltpu.roll(c, LANES - 16, 1))
    return lo, hi


def _neighbour_z(c, m, p, z):
    lo = jnp.where(z == 0, pltpu.roll(m, LANES - 15, 1), pltpu.roll(c, 1, 1))
    hi = jnp.where(z == 15, pltpu.roll(p, 15, 1), pltpu.roll(c, LANES - 1, 1))
    return lo, hi


def _column(ex, ey, ez):
    return (ex + 1) * 9 + (ey + 1) * 3 + (ez + 1)


def _stencil_kernel(tab_ref, src_ref, diag_ref, *rest, shift=0.0, scale=1.0):
    previous, out_ref = rest[:-1], rest[-1]
    row, y, z = _masks()
    bricks = out_ref.shape[0]
    for b in range(bricks):
        own = src_ref[4 * bricks + b]

        def brick(ex, ey, ez):
            if ex == 0 and ey == 0 and ez == 0:
                return own
            return src_ref[tab_ref[b * 27 + _column(ex, ey, ez)]]

        planes = {}
        for ex in (-1, 0, 1):
            lines = {}
            for ey in (-1, 0, 1):
                c = brick(ex, ey, 0)
                lo, hi = _neighbour_z(c, brick(ex, ey, -1), brick(ex, ey, 1), z)
                lines[ey] = c + 0.5 * (lo + hi)
            lo, hi = _neighbour_y(lines[0], lines[-1], lines[1], y)
            planes[ex] = lines[0] + 0.5 * (lo + hi)
        lo, hi = _neighbour_x(planes[0], planes[-1], planes[1], row)
        smoothed = planes[0] + 0.5 * (lo + hi)
        image = ((diag_ref[b] + (2.0 - shift)) * own - 2.0 * smoothed) * scale
        out_ref[b] = 2.0 * image - previous[0][b] if previous else image


def _divergence_kernel(tab_ref, src_ref, out_ref):
    row, y, z = _masks()
    bricks = out_ref.shape[0]
    for b in range(bricks):

        def brick(k, ex, ey, ez):
            if ex == 0 and ey == 0 and ez == 0:
                return src_ref[k, 4 * bricks + b]
            return src_ref[k, tab_ref[b * 27 + _column(ex, ey, ez)]]

        lo, hi = _neighbour_x(brick(0, 0, 0, 0), brick(0, -1, 0, 0), brick(0, 1, 0, 0), row)
        change_x = hi - lo
        lo, hi = _neighbour_y(brick(1, 0, 0, 0), brick(1, 0, -1, 0), brick(1, 0, 1, 0), y)
        change_y = hi - lo
        lo, hi = _neighbour_z(brick(2, 0, 0, 0), brick(2, 0, 0, -1), brick(2, 0, 0, 1), z)
        change_z = hi - lo
        out_ref[b] = -4.0 * ((change_x + change_y) + change_z)


def _local_call(kernel, out_shape, operands, flops):
    spaces = [pltpu.SMEM] + [pltpu.VMEM] * (len(operands) - 1)
    moved = sum(int(a.size) * 4 for a in operands) + math.prod(out_shape) * 4
    return pl.pallas_call(
        kernel,
        out_shape=jax.ShapeDtypeStruct(out_shape, jnp.float32),
        in_specs=[pl.BlockSpec(memory_space=s) for s in spaces],
        out_specs=pl.BlockSpec(memory_space=pltpu.VMEM),
        cost_estimate=pl.CostEstimate(flops=flops, bytes_accessed=moved, transcendentals=0),
    )(*operands)


def _shift(field, axis, step):
    size = lax.axis_size(axis)
    pairs = [(i + step, i) for i in range(size) if 0 <= i + step < size]
    return lax.ppermute(field, axis, pairs)


def halo(field):
    lead, bricks = field.shape[:-3], field.shape[-3]
    column = jnp.stack([_shift(field, "wide", -1), field, _shift(field, "wide", 1)], axis=-4)
    block = jnp.stack([_shift(column, "narrow", -1), column, _shift(column, "narrow", 1)], axis=-4)
    block = block.reshape(lead + (9 * bricks,) + field.shape[-2:])
    zero = jnp.zeros(lead + (1,) + field.shape[-2:], field.dtype)
    return jnp.concatenate([block, zero], axis=-3)


def shards(point_owner, point_cell, normals, strip_count, neighbours):
    owners = lax.axis_size("wide")
    devices = owners * lax.axis_size("narrow")
    point_total = point_cell.shape[0]
    bricks = neighbours.shape[2]
    table = neighbours.reshape(bricks * 27)

    owner = point_owner[:, 0]
    slots = jnp.arange(point_total, dtype=jnp.int32)
    is_live = slots < strip_count[0]
    code = jnp.where(is_live, point_cell + 1, 0).astype(jnp.float32)
    owner_hot = (owner[:, None] == jnp.arange(owners, dtype=jnp.int32)[None, :]).astype(jnp.bfloat16)
    earlier = (slots[None, :] < slots[:, None]).astype(jnp.bfloat16)
    before = jnp.dot(earlier, owner_hot, preferred_element_type=jnp.float32)
    rank = jnp.sum(before * owner_hot.astype(jnp.float32), axis=1).astype(jnp.int32)
    dest = owner * CAP + rank
    payload = jnp.concatenate([code[:, None], normals.T], axis=1)
    place_hot = (jnp.arange(owners * CAP, dtype=jnp.int32)[:, None] == dest[None, :]).astype(jnp.bfloat16)
    send = _exact_rows(place_hot, payload)
    got = lax.all_to_all(send.reshape(owners, CAP, 4), "wide", 0, 0, tiled=True).reshape(owners * CAP, 4)

    cell = got[:, 0].astype(jnp.int32) - 1
    brick_x = cell >> 8
    cell_yz = cell & (LANES - 1)
    bx_hot = (brick_x[:, None] == jnp.arange(bricks * ROWS, dtype=jnp.int32)[None, :]).astype(jnp.float32)
    yz_hot = (cell_yz[:, None] == jnp.arange(LANES, dtype=jnp.int32)[None, :]).astype(jnp.float32)
    parts = _bf16_parts(got[:, 1:4])
    weighted = jnp.concatenate([bx_hot * p[:, c : c + 1] for p in parts for c in range(3)] + [bx_hot], axis=1)
    splatted = jnp.einsum(
        "pa,pb->ab", weighted.astype(jnp.bfloat16), yz_hot.astype(jnp.bfloat16), preferred_element_type=jnp.float32
    )
    splatted = splatted.reshape(10, bricks, ROWS, LANES)
    vector_field = (splatted[0:3] + splatted[3:6]) + splatted[6:9]
    diagonal = 14.5 + 2.0 * splatted[9]

    shape = (bricks, ROWS, LANES)
    right_side = _local_call(_divergence_kernel, shape, [table, halo(vector_field)], 20 * bricks * 4096)

    basis = [right_side]
    kernel = functools.partial(_stencil_kernel, shift=SHIFT, scale=1.0 / SPAN)
    for k in range(ITERS):
        operands = [table, halo(basis[-1]), diagonal] + ([basis[-2]] if k > 0 else [])
        basis.append(_local_call(kernel, shape, operands, 60 * bricks * 4096))
    lift = [[0.0] * ITERS for _ in range(ITERS + 1)]
    for k in range(ITERS):
        lift[k][k] = SHIFT
        if k == 0:
            lift[1][0] = SPAN
        else:
            lift[k - 1][k] = lift[k + 1][k] = 0.5 * SPAN
    vmem = pl.BlockSpec(memory_space=pltpu.VMEM)
    payload = pl.pallas_call(
        _gram_kernel, out_shape=jax.ShapeDtypeStruct((1, 32), jnp.float32), in_specs=[vmem] * len(basis), out_specs=vmem
    )(*basis)
    gathered = lax.all_to_all(jnp.broadcast_to(payload, (devices, 32)), ("wide", "narrow"), 0, 0, tiled=True)
    flat = jax.ShapeDtypeStruct((bricks, ROWS * LANES), jnp.float32)
    solution, residual = pl.pallas_call(
        functools.partial(_galerkin_kernel, lift=lift),
        out_shape=(flat, flat),
        in_specs=[vmem] * (1 + len(basis)),
        out_specs=(vmem, vmem),
    )(jnp.pad(gathered.T, ((0, 0), (0, max(0, 128 - devices)))), *basis)
    out = (1, 1, bricks, ROWS * LANES)
    return solution.reshape(out), residual.reshape(out)


def solution(mesh):
    return jax.shard_map(
        shards,
        mesh=mesh,
        in_specs=(
            P(("wide", "narrow"), None),
            P(("wide", "narrow")),
            P(None, ("wide", "narrow")),
            P(("wide", "narrow")),
            P("wide", "narrow", None, None),
        ),
        out_specs=(P("wide", "narrow", None, None), P("wide", "narrow", None, None)),
        check_vma=False,
    )
```

```python
import functools
import math

import jax
import jax.numpy as jnp
from jax import lax
from jax.experimental import pallas as pl
from jax.experimental.pallas import tpu as pltpu
from jax.sharding import PartitionSpec as P

ITERS = 3
CAP = 32
HIGHEST = lax.Precision.HIGHEST
ROWS, LANES = 16, 256
SHIFT, SPAN = 8.0, 8.0


def _solve(matrix, rhs):
    n = len(rhs)
    m = [list(r) + [v] for r, v in zip(matrix, rhs)]
    for k in range(n):
        for i in range(k + 1, n):
            f = m[i][k] / m[k][k]
            m[i] = [m[i][j] - f * m[k][j] if j > k else m[i][j] for j in range(n + 1)]
    x = [None] * n
    for i in reversed(range(n)):
        acc = m[i][n]
        for j in range(i + 1, n):
            acc = acc - m[i][j] * x[j]
        x[i] = acc / m[i][i]
    return x


def _two_sum(a, b):
    total = a + b
    part = total - a
    return total, (a - (total - part)) + (b - part)


def _split(a):
    scaled = a * 4097.0
    high = scaled - (scaled - a)
    return high, a - high


def _two_prod(a, b):
    product = a * b
    ah, al = _split(a)
    bh, bl = _split(b)
    return product, ((ah * bh - product) + ah * bl + al * bh) + al * bl


def _halve(s, e, axis, stop):
    while s.shape[axis] > stop:
        h = s.shape[axis] // 2
        first = lax.slice_in_dim(s, 0, h, axis=axis)
        second = lax.slice_in_dim(s, h, 2 * h, axis=axis)
        s, err = _two_sum(first, second)
        e = lax.slice_in_dim(e, 0, h, axis=axis) + lax.slice_in_dim(e, h, 2 * h, axis=axis) + err
    return s, e


def _spread(s, e, axis):
    k = s.shape[axis] // 2
    while k >= 1:
        s, err = _two_sum(s, pltpu.roll(s, k, axis))
        e = e + pltpu.roll(e, k, axis) + err
        k //= 2
    return s, e


def _dd_add(x, y):
    s, e = _two_sum(x[0], y[0])
    return _two_sum(s, e + (x[1] + y[1]))


def _rows(ref):
    return jnp.concatenate([ref[b] for b in range(ref.shape[0])], axis=0)


def _gram_kernel(*refs):
    basis_ref, out_ref = refs[:-1], refs[-1]
    lane = lax.broadcasted_iota(jnp.int32, (1, 128), 1)
    count = len(basis_ref)
    acc = jnp.zeros((1, 128), jnp.float32)
    k = 0
    for i in range(count):
        for j in range(i, count):
            s, e = _two_prod(_rows(basis_ref[i]), _rows(basis_ref[j]))
            s, e = _halve(s, e, 0, 8)
            s, e = _halve(s, e, 1, 128)
            s, e = _spread(s, e, 0)
            s, e = _spread(s, e, 1)
            high, low = _two_sum(s, e)
            acc = jnp.where(lane == k, high[0:1, :], acc)
            acc = jnp.where(lane == 16 + k, low[0:1, :], acc)
            k += 1
    out_ref[...] = acc[:, 0 : out_ref.shape[1]]


def _galerkin_kernel(parts_ref, *refs, lift=None):
    basis_ref, (solution_ref, residual_ref) = refs[:-2], refs[-2:]
    half = parts_ref.shape[0] // 2
    s, e = _halve(parts_ref[0:half, :], parts_ref[half:, :], 1, 128)
    s, e = _spread(s, e, 1)
    high, low = _two_sum(s, e)
    rows = lax.broadcasted_iota(jnp.int32, high.shape, 0)

    def pick(values, k):
        return jnp.sum(jnp.where(rows == k, values, 0.0), axis=0, keepdims=True)

    size = len(lift)
    pairs = [(i, j) for i in range(size) for j in range(i, size)]
    gram = {}
    for k, (i, j) in enumerate(pairs):
        gram[i, j] = gram[j, i] = (pick(high, k), pick(low, k))
    n = size - 1
    matrix = [[None] * n for _ in range(n)]
    for i in range(n):
        for j in range(n):
            entry = None
            for k in range(size):
                if lift[k][j] != 0.0:
                    term = (lift[k][j] * gram[i, k][0], lift[k][j] * gram[i, k][1])
                    entry = term if entry is None else _dd_add(entry, term)
            matrix[i][j] = entry
    wanted = [gram[i, 0] for i in range(n)]
    top = [[matrix[i][j][0] for j in range(n)] for i in range(n)]
    coeff = _solve(top, [w[0] for w in wanted])
    misfit = []
    for i in range(n):
        acc = wanted[i]
        for j in range(n):
            p, pe = _two_prod(matrix[i][j][0], coeff[j])
            acc = _dd_add(acc, (-p, -(pe + matrix[i][j][1] * coeff[j])))
        misfit.append(acc[0] + acc[1])
    coeff = [c + d for c, d in zip(coeff, _solve(top, misfit))]
    weights = []
    for k in range(size):
        terms = [lift[k][j] * coeff[j] for j in range(n) if lift[k][j] != 0.0]
        weights.append((1.0 if k == 0 else 0.0) - sum(terms[1:], terms[0]))
    blocks = [_rows(r) for r in basis_ref]
    shape = blocks[0].shape

    def wide(v):
        v = jnp.broadcast_to(v, (shape[0], v.shape[1]))
        return jnp.concatenate([v] * (shape[1] // v.shape[1]), axis=1)

    def store(out_ref, total):
        for r in range(shape[0]):
            b, x = divmod(r, ROWS)
            out_ref[pl.ds(b, 1), pl.ds(x * LANES, LANES)] = total[r : r + 1, :]

    total = wide(coeff[0]) * blocks[0]
    for j in range(1, n):
        total = total + wide(coeff[j]) * blocks[j]
    store(solution_ref, total)
    total = wide(weights[0]) * blocks[0]
    for k in range(1, size):
        total = total + wide(weights[k]) * blocks[k]
    store(residual_ref, total)


def _bf16_parts(x):
    high = lax.reduce_precision(x, exponent_bits=8, mantissa_bits=7)
    rest = x - high
    middle = lax.reduce_precision(rest, exponent_bits=8, mantissa_bits=7)
    return [high, middle, rest - middle]


def _exact_rows(hot, values):
    parts = _bf16_parts(values)
    width = values.shape[1]
    stacked = jnp.concatenate(parts, axis=1).astype(jnp.bfloat16)
    picked = jnp.dot(hot, stacked, preferred_element_type=jnp.float32)
    high, middle, low = (picked[:, i * width : (i + 1) * width] for i in range(3))
    return (high + middle) + low


def _masks():
    shape = (ROWS, LANES)
    lane = lax.broadcasted_iota(jnp.int32, shape, 1)
    row = lax.broadcasted_iota(jnp.int32, shape, 0)
    return row, lane >> 4, lane & 15


def _neighbour_x(c, m, p, row):
    lo = jnp.where(row == 0, pltpu.roll(m, 1, 0), pltpu.roll(c, 1, 0))
    hi = jnp.where(row == ROWS - 1, pltpu.roll(p, ROWS - 1, 0), pltpu.roll(c, ROWS - 1, 0))
    return lo, hi


def _neighbour_y(c, m, p, y):
    lo = jnp.where(y == 0, pltpu.roll(m, 16, 1), pltpu.roll(c, 16, 1))
    hi = jnp.where(y == 15, pltpu.roll(p, LANES - 16, 1), pltpu.roll(c, LANES - 16, 1))
    return lo, hi


def _neighbour_z(c, m, p, z):
    lo = jnp.where(z == 0, pltpu.roll(m, LANES - 15, 1), pltpu.roll(c, 1, 1))
    hi = jnp.where(z == 15, pltpu.roll(p, 15, 1), pltpu.roll(c, LANES - 1, 1))
    return lo, hi


def _column(ex, ey, ez):
    return (ex + 1) * 9 + (ey + 1) * 3 + (ez + 1)


def _stencil_kernel(tab_ref, src_ref, diag_ref, *rest, shift=0.0, scale=1.0):
    previous, out_ref = rest[:-1], rest[-1]
    row, y, z = _masks()
    bricks = out_ref.shape[0]
    for b in range(bricks):
        own = src_ref[4 * bricks + b]

        def brick(ex, ey, ez):
            if ex == 0 and ey == 0 and ez == 0:
                return own
            return src_ref[tab_ref[b * 27 + _column(ex, ey, ez)]]

        planes = {}
        for ex in (-1, 0, 1):
            lines = {}
            for ey in (-1, 0, 1):
                c = brick(ex, ey, 0)
                lo, hi = _neighbour_z(c, brick(ex, ey, -1), brick(ex, ey, 1), z)
                lines[ey] = c + 0.5 * (lo + hi)
            lo, hi = _neighbour_y(lines[0], lines[-1], lines[1], y)
            planes[ex] = lines[0] + 0.5 * (lo + hi)
        lo, hi = _neighbour_x(planes[0], planes[-1], planes[1], row)
        smoothed = planes[0] + 0.5 * (lo + hi)
        image = ((diag_ref[b] + (2.0 - shift)) * own - 2.0 * smoothed) * scale
        out_ref[b] = 2.0 * image - previous[0][b] if previous else image


def _divergence_kernel(tab_ref, src_ref, out_ref):
    row, y, z = _masks()
    bricks = out_ref.shape[0]
    for b in range(bricks):

        def brick(k, ex, ey, ez):
            if ex == 0 and ey == 0 and ez == 0:
                return src_ref[k, 4 * bricks + b]
            return src_ref[k, tab_ref[b * 27 + _column(ex, ey, ez)]]

        lo, hi = _neighbour_x(brick(0, 0, 0, 0), brick(0, -1, 0, 0), brick(0, 1, 0, 0), row)
        change_x = hi - lo
        lo, hi = _neighbour_y(brick(1, 0, 0, 0), brick(1, 0, -1, 0), brick(1, 0, 1, 0), y)
        change_y = hi - lo
        lo, hi = _neighbour_z(brick(2, 0, 0, 0), brick(2, 0, 0, -1), brick(2, 0, 0, 1), z)
        change_z = hi - lo
        out_ref[b] = -4.0 * ((change_x + change_y) + change_z)


def _local_call(kernel, out_shape, operands, flops):
    spaces = [pltpu.SMEM] + [pltpu.VMEM] * (len(operands) - 1)
    moved = sum(int(a.size) * 4 for a in operands) + math.prod(out_shape) * 4
    return pl.pallas_call(
        kernel,
        out_shape=jax.ShapeDtypeStruct(out_shape, jnp.float32),
        in_specs=[pl.BlockSpec(memory_space=s) for s in spaces],
        out_specs=pl.BlockSpec(memory_space=pltpu.VMEM),
        cost_estimate=pl.CostEstimate(flops=flops, bytes_accessed=moved, transcendentals=0),
    )(*operands)


def _shift(field, axis, step):
    size = lax.axis_size(axis)
    pairs = [(i + step, i) for i in range(size) if 0 <= i + step < size]
    return lax.ppermute(field, axis, pairs)


def halo(field):
    lead, bricks = field.shape[:-3], field.shape[-3]
    column = jnp.stack([_shift(field, "wide", -1), field, _shift(field, "wide", 1)], axis=-4)
    block = jnp.stack([_shift(column, "narrow", -1), column, _shift(column, "narrow", 1)], axis=-4)
    block = block.reshape(lead + (9 * bricks,) + field.shape[-2:])
    zero = jnp.zeros(lead + (1,) + field.shape[-2:], field.dtype)
    return jnp.concatenate([block, zero], axis=-3)


def shards(point_owner, point_cell, normals, strip_count, neighbours):
    owners = lax.axis_size("wide")
    devices = owners * lax.axis_size("narrow")
    point_total = point_cell.shape[0]
    bricks = neighbours.shape[2]
    table = neighbours.reshape(bricks * 27)

    owner = point_owner[:, 0]
    slots = jnp.arange(point_total, dtype=jnp.int32)
    is_live = slots < strip_count[0]
    code = jnp.where(is_live, point_cell + 1, 0).astype(jnp.float32)
    owner_hot = (owner[:, None] == jnp.arange(owners, dtype=jnp.int32)[None, :]).astype(jnp.int32)
    rank = jnp.sum((jnp.cumsum(owner_hot, axis=0) - owner_hot) * owner_hot, axis=1)
    dest = owner * CAP + rank
    payload = jnp.concatenate([code[:, None], normals.T], axis=1)
    place_hot = (jnp.arange(owners * CAP, dtype=jnp.int32)[:, None] == dest[None, :]).astype(jnp.bfloat16)
    send = _exact_rows(place_hot, payload)
    got = lax.all_to_all(send.reshape(owners, CAP, 4), "wide", 0, 0, tiled=True).reshape(owners * CAP, 4)

    cell = got[:, 0].astype(jnp.int32) - 1
    brick_x = cell >> 8
    cell_yz = cell & (LANES - 1)
    bx_hot = (brick_x[:, None] == jnp.arange(bricks * ROWS, dtype=jnp.int32)[None, :]).astype(jnp.float32)
    yz_hot = (cell_yz[:, None] == jnp.arange(LANES, dtype=jnp.int32)[None, :]).astype(jnp.float32)
    weighted = jnp.concatenate([bx_hot * got[:, 1:2], bx_hot * got[:, 2:3], bx_hot * got[:, 3:4], bx_hot], axis=1)
    splatted = jnp.einsum("pa,pb->ab", weighted, yz_hot, precision=HIGHEST, preferred_element_type=jnp.float32)
    splatted = splatted.reshape(4, bricks, ROWS, LANES)
    vector_field = splatted[:3]
    diagonal = 14.5 + 2.0 * splatted[3]

    shape = (bricks, ROWS, LANES)
    right_side = _local_call(_divergence_kernel, shape, [table, halo(vector_field)], 20 * bricks * 4096)

    basis = [right_side]
    kernel = functools.partial(_stencil_kernel, shift=SHIFT, scale=1.0 / SPAN)
    for k in range(ITERS):
        operands = [table, halo(basis[-1]), diagonal] + ([basis[-2]] if k > 0 else [])
        basis.append(_local_call(kernel, shape, operands, 60 * bricks * 4096))
    lift = [[0.0] * ITERS for _ in range(ITERS + 1)]
    for k in range(ITERS):
        lift[k][k] = SHIFT
        if k == 0:
            lift[1][0] = SPAN
        else:
            lift[k - 1][k] = lift[k + 1][k] = 0.5 * SPAN
    vmem = pl.BlockSpec(memory_space=pltpu.VMEM)
    payload = pl.pallas_call(
        _gram_kernel, out_shape=jax.ShapeDtypeStruct((1, 32), jnp.float32), in_specs=[vmem] * len(basis), out_specs=vmem
    )(*basis)
    gathered = lax.all_to_all(jnp.broadcast_to(payload, (devices, 32)), ("wide", "narrow"), 0, 0, tiled=True)
    flat = jax.ShapeDtypeStruct((bricks, ROWS * LANES), jnp.float32)
    solution, residual = pl.pallas_call(
        functools.partial(_galerkin_kernel, lift=lift),
        out_shape=(flat, flat),
        in_specs=[vmem] * (1 + len(basis)),
        out_specs=(vmem, vmem),
    )(jnp.pad(gathered.T, ((0, 0), (0, max(0, 128 - devices)))), *basis)
    out = (1, 1, bricks, ROWS * LANES)
    return solution.reshape(out), residual.reshape(out)


def solution(mesh):
    return jax.shard_map(
        shards,
        mesh=mesh,
        in_specs=(
            P(("wide", "narrow"), None),
            P(("wide", "narrow")),
            P(None, ("wide", "narrow")),
            P(("wide", "narrow")),
            P("wide", "narrow", None, None),
        ),
        out_specs=(P("wide", "narrow", None, None), P("wide", "narrow", None, None)),
        check_vma=False,
    )
```

```python
import functools
import math

import jax
import jax.numpy as jnp
from jax import lax
from jax.experimental import pallas as pl
from jax.experimental.pallas import tpu as pltpu
from jax.sharding import PartitionSpec as P

ITERS = 3
CAP = 32
HIGHEST = lax.Precision.HIGHEST
ROWS, LANES = 16, 256
SHIFT, SPAN = 8.0, 8.0


def _solve(matrix, rhs):
    n = len(rhs)
    m = [list(r) + [v] for r, v in zip(matrix, rhs)]
    for k in range(n):
        for i in range(k + 1, n):
            f = m[i][k] / m[k][k]
            m[i] = [m[i][j] - f * m[k][j] if j > k else m[i][j] for j in range(n + 1)]
    x = [None] * n
    for i in reversed(range(n)):
        acc = m[i][n]
        for j in range(i + 1, n):
            acc = acc - m[i][j] * x[j]
        x[i] = acc / m[i][i]
    return x


def _two_sum(a, b):
    total = a + b
    part = total - a
    return total, (a - (total - part)) + (b - part)


def _split(a):
    scaled = a * 4097.0
    high = scaled - (scaled - a)
    return high, a - high


def _two_prod(a, b):
    product = a * b
    ah, al = _split(a)
    bh, bl = _split(b)
    return product, ((ah * bh - product) + ah * bl + al * bh) + al * bl


def _halve(s, e, axis, stop):
    while s.shape[axis] > stop:
        h = s.shape[axis] // 2
        first = lax.slice_in_dim(s, 0, h, axis=axis)
        second = lax.slice_in_dim(s, h, 2 * h, axis=axis)
        s, err = _two_sum(first, second)
        e = lax.slice_in_dim(e, 0, h, axis=axis) + lax.slice_in_dim(e, h, 2 * h, axis=axis) + err
    return s, e


def _spread(s, e, axis):
    k = s.shape[axis] // 2
    while k >= 1:
        s, err = _two_sum(s, pltpu.roll(s, k, axis))
        e = e + pltpu.roll(e, k, axis) + err
        k //= 2
    return s, e


def _dd_add(x, y):
    s, e = _two_sum(x[0], y[0])
    return _two_sum(s, e + (x[1] + y[1]))


def _rows(ref):
    return jnp.concatenate([ref[b] for b in range(ref.shape[0])], axis=0)


def _gram_kernel(*refs):
    basis_ref, out_ref = refs[:-1], refs[-1]
    lane = lax.broadcasted_iota(jnp.int32, (1, 128), 1)
    count = len(basis_ref)
    acc = jnp.zeros((1, 128), jnp.float32)
    k = 0
    for i in range(count):
        for j in range(i, count):
            s, e = _two_prod(_rows(basis_ref[i]), _rows(basis_ref[j]))
            s, e = _halve(s, e, 0, 8)
            s, e = _halve(s, e, 1, 128)
            s, e = _spread(s, e, 0)
            s, e = _spread(s, e, 1)
            high, low = _two_sum(s, e)
            acc = jnp.where(lane == k, high[0:1, :], acc)
            acc = jnp.where(lane == 16 + k, low[0:1, :], acc)
            k += 1
    out_ref[...] = acc[:, 0 : out_ref.shape[1]]


def _galerkin_kernel(parts_ref, *refs, lift=None):
    basis_ref, (solution_ref, residual_ref) = refs[:-2], refs[-2:]
    half = parts_ref.shape[0] // 2
    s, e = _halve(parts_ref[0:half, :], parts_ref[half:, :], 1, 128)
    s, e = _spread(s, e, 1)
    high, low = _two_sum(s, e)
    rows = lax.broadcasted_iota(jnp.int32, high.shape, 0)

    def pick(values, k):
        return jnp.sum(jnp.where(rows == k, values, 0.0), axis=0, keepdims=True)

    size = len(lift)
    pairs = [(i, j) for i in range(size) for j in range(i, size)]
    gram = {}
    for k, (i, j) in enumerate(pairs):
        gram[i, j] = gram[j, i] = (pick(high, k), pick(low, k))
    n = size - 1
    matrix = [[None] * n for _ in range(n)]
    for i in range(n):
        for j in range(n):
            entry = None
            for k in range(size):
                if lift[k][j] != 0.0:
                    term = (lift[k][j] * gram[i, k][0], lift[k][j] * gram[i, k][1])
                    entry = term if entry is None else _dd_add(entry, term)
            matrix[i][j] = entry
    wanted = [gram[i, 0] for i in range(n)]
    top = [[matrix[i][j][0] for j in range(n)] for i in range(n)]
    coeff = _solve(top, [w[0] for w in wanted])
    misfit = []
    for i in range(n):
        acc = wanted[i]
        for j in range(n):
            p, pe = _two_prod(matrix[i][j][0], coeff[j])
            acc = _dd_add(acc, (-p, -(pe + matrix[i][j][1] * coeff[j])))
        misfit.append(acc[0] + acc[1])
    coeff = [c + d for c, d in zip(coeff, _solve(top, misfit))]
    weights = []
    for k in range(size):
        terms = [lift[k][j] * coeff[j] for j in range(n) if lift[k][j] != 0.0]
        weights.append((1.0 if k == 0 else 0.0) - sum(terms[1:], terms[0]))
    blocks = [_rows(r) for r in basis_ref]
    shape = blocks[0].shape

    def wide(v):
        v = jnp.broadcast_to(v, (shape[0], v.shape[1]))
        return jnp.concatenate([v] * (shape[1] // v.shape[1]), axis=1)

    def store(out_ref, total):
        for r in range(shape[0]):
            b, x = divmod(r, ROWS)
            out_ref[pl.ds(b, 1), pl.ds(x * LANES, LANES)] = total[r : r + 1, :]

    total = wide(coeff[0]) * blocks[0]
    for j in range(1, n):
        total = total + wide(coeff[j]) * blocks[j]
    store(solution_ref, total)
    total = wide(weights[0]) * blocks[0]
    for k in range(1, size):
        total = total + wide(weights[k]) * blocks[k]
    store(residual_ref, total)


def _bf16_parts(x):
    high = lax.reduce_precision(x, exponent_bits=8, mantissa_bits=7)
    rest = x - high
    middle = lax.reduce_precision(rest, exponent_bits=8, mantissa_bits=7)
    return [high, middle, rest - middle]


def _exact_rows(hot, values):
    parts = _bf16_parts(values)
    width = values.shape[1]
    stacked = jnp.concatenate(parts, axis=1).astype(jnp.bfloat16)
    picked = jnp.dot(hot, stacked, preferred_element_type=jnp.float32)
    high, middle, low = (picked[:, i * width : (i + 1) * width] for i in range(3))
    return (high + middle) + low


def _masks():
    shape = (ROWS, LANES)
    lane = lax.broadcasted_iota(jnp.int32, shape, 1)
    row = lax.broadcasted_iota(jnp.int32, shape, 0)
    return row, lane >> 4, lane & 15


def _neighbour_x(c, m, p, row):
    lo = jnp.where(row == 0, pltpu.roll(m, 1, 0), pltpu.roll(c, 1, 0))
    hi = jnp.where(row == ROWS - 1, pltpu.roll(p, ROWS - 1, 0), pltpu.roll(c, ROWS - 1, 0))
    return lo, hi


def _neighbour_y(c, m, p, y):
    lo = jnp.where(y == 0, pltpu.roll(m, 16, 1), pltpu.roll(c, 16, 1))
    hi = jnp.where(y == 15, pltpu.roll(p, LANES - 16, 1), pltpu.roll(c, LANES - 16, 1))
    return lo, hi


def _neighbour_z(c, m, p, z):
    lo = jnp.where(z == 0, pltpu.roll(m, LANES - 15, 1), pltpu.roll(c, 1, 1))
    hi = jnp.where(z == 15, pltpu.roll(p, 15, 1), pltpu.roll(c, LANES - 1, 1))
    return lo, hi


def _column(ex, ey, ez):
    return (ex + 1) * 9 + (ey + 1) * 3 + (ez + 1)


def _stencil_kernel(tab_ref, src_ref, diag_ref, *rest, shift=0.0, scale=1.0):
    previous, out_ref = rest[:-1], rest[-1]
    row, y, z = _masks()
    bricks = out_ref.shape[0]
    for b in range(bricks):
        own = src_ref[4 * bricks + b]

        def brick(ex, ey, ez):
            if ex == 0 and ey == 0 and ez == 0:
                return own
            return src_ref[tab_ref[b * 27 + _column(ex, ey, ez)]]

        planes = {}
        for ex in (-1, 0, 1):
            face = {-1: slice(ROWS - 1, ROWS), 0: slice(0, ROWS), 1: slice(0, 1)}[ex]
            lines = {}
            for ey in (-1, 0, 1):
                c, m, p = (brick(ex, ey, ez)[face] for ez in (0, -1, 1))
                lo, hi = _neighbour_z(c, m, p, z[face])
                lines[ey] = c + 0.5 * (lo + hi)
            lo, hi = _neighbour_y(lines[0], lines[-1], lines[1], y[face])
            planes[ex] = lines[0] + 0.5 * (lo + hi)
        lo = jnp.where(row == 0, planes[-1], pltpu.roll(planes[0], 1, 0))
        hi = jnp.where(row == ROWS - 1, planes[1], pltpu.roll(planes[0], ROWS - 1, 0))
        smoothed = planes[0] + 0.5 * (lo + hi)
        image = ((diag_ref[b] + (2.0 - shift)) * own - 2.0 * smoothed) * scale
        out_ref[b] = 2.0 * image - previous[0][b] if previous else image


def _divergence_kernel(tab_ref, src_ref, out_ref):
    row, y, z = _masks()
    bricks = out_ref.shape[0]
    for b in range(bricks):

        def brick(k, ex, ey, ez):
            if ex == 0 and ey == 0 and ez == 0:
                return src_ref[k, 4 * bricks + b]
            return src_ref[k, tab_ref[b * 27 + _column(ex, ey, ez)]]

        lo, hi = _neighbour_x(brick(0, 0, 0, 0), brick(0, -1, 0, 0), brick(0, 1, 0, 0), row)
        change_x = hi - lo
        lo, hi = _neighbour_y(brick(1, 0, 0, 0), brick(1, 0, -1, 0), brick(1, 0, 1, 0), y)
        change_y = hi - lo
        lo, hi = _neighbour_z(brick(2, 0, 0, 0), brick(2, 0, 0, -1), brick(2, 0, 0, 1), z)
        change_z = hi - lo
        out_ref[b] = -4.0 * ((change_x + change_y) + change_z)


def _local_call(kernel, out_shape, operands, flops):
    spaces = [pltpu.SMEM] + [pltpu.VMEM] * (len(operands) - 1)
    moved = sum(int(a.size) * 4 for a in operands) + math.prod(out_shape) * 4
    return pl.pallas_call(
        kernel,
        out_shape=jax.ShapeDtypeStruct(out_shape, jnp.float32),
        in_specs=[pl.BlockSpec(memory_space=s) for s in spaces],
        out_specs=pl.BlockSpec(memory_space=pltpu.VMEM),
        cost_estimate=pl.CostEstimate(flops=flops, bytes_accessed=moved, transcendentals=0),
    )(*operands)


def _shift(field, axis, step):
    size = lax.axis_size(axis)
    pairs = [(i + step, i) for i in range(size) if 0 <= i + step < size]
    return lax.ppermute(field, axis, pairs)


def halo(field):
    lead, bricks = field.shape[:-3], field.shape[-3]
    column = jnp.stack([_shift(field, "wide", -1), field, _shift(field, "wide", 1)], axis=-4)
    block = jnp.stack([_shift(column, "narrow", -1), column, _shift(column, "narrow", 1)], axis=-4)
    block = block.reshape(lead + (9 * bricks,) + field.shape[-2:])
    zero = jnp.zeros(lead + (1,) + field.shape[-2:], field.dtype)
    return jnp.concatenate([block, zero], axis=-3)


def shards(point_owner, point_cell, normals, strip_count, neighbours):
    owners = lax.axis_size("wide")
    devices = owners * lax.axis_size("narrow")
    point_total = point_cell.shape[0]
    bricks = neighbours.shape[2]
    table = neighbours.reshape(bricks * 27)

    owner = point_owner[:, 0]
    slots = jnp.arange(point_total, dtype=jnp.int32)
    is_live = slots < strip_count[0]
    code = jnp.where(is_live, point_cell + 1, 0).astype(jnp.float32)
    owner_hot = (owner[:, None] == jnp.arange(owners, dtype=jnp.int32)[None, :]).astype(jnp.bfloat16)
    earlier = (slots[None, :] < slots[:, None]).astype(jnp.bfloat16)
    before = jnp.dot(earlier, owner_hot, preferred_element_type=jnp.float32)
    rank = jnp.sum(before * owner_hot.astype(jnp.float32), axis=1).astype(jnp.int32)
    dest = owner * CAP + rank
    payload = jnp.concatenate([code[:, None], normals.T], axis=1)
    place_hot = (jnp.arange(owners * CAP, dtype=jnp.int32)[:, None] == dest[None, :]).astype(jnp.bfloat16)
    send = _exact_rows(place_hot, payload)
    got = lax.all_to_all(send.reshape(owners, CAP, 4), "wide", 0, 0, tiled=True).reshape(owners * CAP, 4)

    cell = got[:, 0].astype(jnp.int32) - 1
    brick_x = cell >> 8
    cell_yz = cell & (LANES - 1)
    bx_hot = (brick_x[:, None] == jnp.arange(bricks * ROWS, dtype=jnp.int32)[None, :]).astype(jnp.float32)
    yz_hot = (cell_yz[:, None] == jnp.arange(LANES, dtype=jnp.int32)[None, :]).astype(jnp.float32)
    weighted = jnp.concatenate([bx_hot * got[:, 1:2], bx_hot * got[:, 2:3], bx_hot * got[:, 3:4], bx_hot], axis=1)
    splatted = jnp.einsum("pa,pb->ab", weighted, yz_hot, precision=HIGHEST, preferred_element_type=jnp.float32)
    splatted = splatted.reshape(4, bricks, ROWS, LANES)
    vector_field = splatted[:3]
    diagonal = 14.5 + 2.0 * splatted[3]

    shape = (bricks, ROWS, LANES)
    right_side = _local_call(_divergence_kernel, shape, [table, halo(vector_field)], 20 * bricks * 4096)

    basis = [right_side]
    kernel = functools.partial(_stencil_kernel, shift=SHIFT, scale=1.0 / SPAN)
    for k in range(ITERS):
        operands = [table, halo(basis[-1]), diagonal] + ([basis[-2]] if k > 0 else [])
        basis.append(_local_call(kernel, shape, operands, 60 * bricks * 4096))
    lift = [[0.0] * ITERS for _ in range(ITERS + 1)]
    for k in range(ITERS):
        lift[k][k] = SHIFT
        if k == 0:
            lift[1][0] = SPAN
        else:
            lift[k - 1][k] = lift[k + 1][k] = 0.5 * SPAN
    vmem = pl.BlockSpec(memory_space=pltpu.VMEM)
    payload = pl.pallas_call(
        _gram_kernel, out_shape=jax.ShapeDtypeStruct((1, 32), jnp.float32), in_specs=[vmem] * len(basis), out_specs=vmem
    )(*basis)
    gathered = lax.all_to_all(jnp.broadcast_to(payload, (devices, 32)), ("wide", "narrow"), 0, 0, tiled=True)
    flat = jax.ShapeDtypeStruct((bricks, ROWS * LANES), jnp.float32)
    solution, residual = pl.pallas_call(
        functools.partial(_galerkin_kernel, lift=lift),
        out_shape=(flat, flat),
        in_specs=[vmem] * (1 + len(basis)),
        out_specs=(vmem, vmem),
    )(jnp.pad(gathered.T, ((0, 0), (0, max(0, 128 - devices)))), *basis)
    out = (1, 1, bricks, ROWS * LANES)
    return solution.reshape(out), residual.reshape(out)


def solution(mesh):
    return jax.shard_map(
        shards,
        mesh=mesh,
        in_specs=(
            P(("wide", "narrow"), None),
            P(("wide", "narrow")),
            P(None, ("wide", "narrow")),
            P(("wide", "narrow")),
            P("wide", "narrow", None, None),
        ),
        out_specs=(P("wide", "narrow", None, None), P("wide", "narrow", None, None)),
        check_vma=False,
    )
```
